32 devices in a mesh: groups: 2 (over x), seq: 8 (over z, y), tgrp: 2 (over core).
Axes of the slice: x: 2, y: 2, z: 4, core: 2. Of those that a mesh axis runs over, the one named last changes fastest.
Arguments:
- student_hidden: bfloat16 [8192, 4096], P(('groups', 'seq'), 'tgrp'), parts along dimension 0, may hold values from -6 to 6
- teacher_hidden: bfloat16 [8192, 8192], P(('groups', 'seq'), 'tgrp'), parts along dimension 0, may hold values from -6 to 6
- student_proj: bfloat16 [4096, 128], P('tgrp'), may hold values from -0.09375 to 0.09375
- teacher_proj: bfloat16 [8192, 128], P('tgrp'), may hold values from -0.0625 to 0.0625
- student_chars: int32 [8192], P(('groups', 'seq')), parts along dimension 0, may hold values from 0 to 18427, as said below
- teacher_chars: int32 [8192], P(('groups', 'seq')), parts along dimension 0, may hold values from 0 to 18427, as said below
- band: int32 [16, 2], P(('groups', 'seq')), parts along dimension 0, may hold values from 0 to 1, as said below
Outputs:
- aligned: bfloat16 [8192, 8192], P(('groups', 'seq'), 'tgrp'), parts along dimension 0
The draws below stay inside these ranges and needn't reach their ends.
There are 2 independent parts, one for each index of `groups`. The reference program is written for one: setup_inputs(seed, part) draws one part's arguments, and reference() takes and returns one part's arrays. A program takes and returns all parts, laid end to end along the dimension named above; an argument that names none is the same for every part. Nothing has to cross between parts.
Inputs may be any that keep to these rules, and one draw needn't show every extreme that they name: `student_chars`: offsets of consecutive tokens rise by 1 to 8; the first token's offset is 0 and the last one's is 18427. `teacher_chars`: offsets of consecutive tokens rise by 1 to 8; the first token's offset is 0 and the last one's is 18427. `band`: every row has at least one 1; the first row's column 0 and the last row's column 1 are 0.
All inputs are finite; a program needn't handle non-finite values.
Results may differ from the reference program's by a relative error of at most 0.008.
Values may be sent and summed in bfloat16 or wider, within the bound.
No kernel may reach another device: no remote copies, remote signals or barrier semaphores. Data moves between devices by JAX's collectives and lax.ppermute only.
A program may use at most 64 MiB of HBM per device.

```python
import math
import jax
import jax.numpy as jnp
from jax import lax

DS = 4096
DT = 8192
PROJ = 128
BLOCK = 512
ITERS = 4
BLOCKS = 8
STU_TOK = 4096
TEA_TOK = 4096


def char_offsets(key, count):
    first_rise = jax.random.randint(key, (count // 2,), 1, 9).astype(jnp.int32)
    paired = jnp.stack([first_rise, 9 - first_rise], 1).reshape(count)
    rises = jnp.concatenate([jnp.full((1,), 4, jnp.int32), paired[:count - 2]], 0)
    return jnp.concatenate([jnp.zeros((1,), jnp.int32), jnp.cumsum(rises).astype(jnp.int32)], 0).astype(jnp.int32)


def draw_student_chars(key, part):
    return char_offsets(jax.random.fold_in(key, 11), STU_TOK)


def draw_teacher_chars(key, part):
    return char_offsets(jax.random.fold_in(key, 12), TEA_TOK)


def draw_band(key, part):
    coins = jax.random.randint(jax.random.fold_in(key, 21), (BLOCKS, 2), 0, 2).astype(jnp.int32)
    position = jnp.arange(BLOCKS, dtype=jnp.int32)
    left_flag = jnp.where(position == 0, 0, coins[:, 0])
    right_flag = jnp.where(position == BLOCKS - 1, 0, coins[:, 1])
    right_flag = jnp.where((left_flag + right_flag == 0) & (position < BLOCKS - 1), 1, right_flag)
    left_flag = jnp.where(left_flag + right_flag == 0, 1, left_flag)
    return jnp.stack([left_flag, right_flag], 1).astype(jnp.int32)


def levels(stream_key, shape, pieces, least, top_value):
    factor_of, own = 1.0, jax.random.fold_in(stream_key, 6)
    for dim, shards_of in pieces:
        heights = jnp.exp(jax.random.uniform(jax.random.fold_in(own, dim), (shards_of,), jnp.float32, least / len(pieces), top_value / len(pieces)))
        factor_of = factor_of * jnp.repeat(heights, shape[dim] // shards_of).reshape([-1 if axis == dim else 1 for axis in range(len(shape))])
    return factor_of


def scatter_about(stream_key, shape, deviation, bound, cuts=(), kind=jnp.bfloat16):
    gain = levels(stream_key, shape, cuts, -0.22, 0.18) if cuts else 1.0
    array = jax.random.normal(stream_key, shape, jnp.float32) * deviation * gain
    return jnp.minimum(jnp.maximum(array, -bound), bound).astype(kind)


def setup_inputs(seed: int = 0, part: int = 0) -> dict:
    seeds = jax.random.split(jax.random.key(seed), 8)
    part_keys = jax.random.split(jax.random.fold_in(seeds[7], part), 8)
    return {
        "student_hidden": scatter_about(part_keys[0], (STU_TOK, DS), 1.0, 6.0, ((0, 8), (1, 2))),
        "teacher_hidden": scatter_about(part_keys[1], (TEA_TOK, DT), 1.0, 6.0, ((0, 8), (1, 2))),
        "student_proj": scatter_about(seeds[2], (DS, PROJ), DS ** -0.5, 0.09375, ((0, 2),)),
        "teacher_proj": scatter_about(seeds[3], (DT, PROJ), DT ** -0.5, 0.0625, ((0, 2),)),
        "student_chars": draw_student_chars(jax.random.fold_in(jax.random.fold_in(seeds[7], part), 71), part),
        "teacher_chars": draw_teacher_chars(jax.random.fold_in(jax.random.fold_in(seeds[7], part), 71), part),
        "band": draw_band(jax.random.fold_in(jax.random.fold_in(seeds[7], part), 71), part),
    }


norm_eps = 1e-05

def unit_rows(features):
    factor = lax.rsqrt(lax.optimization_barrier(jnp.mean(features * features, axis=-1, keepdims=True)) + norm_eps)
    return (features * factor).astype(jnp.bfloat16)

def beside(values):
    zero_row = jnp.zeros_like(values[:1])
    from_left = jnp.concatenate([zero_row, values[:-1]], 0)
    from_right = jnp.concatenate([values[1:], zero_row], 0)
    return jnp.stack([from_left, values, from_right], 1)

def reference(student_hidden, teacher_hidden, student_proj, teacher_proj, student_chars, teacher_chars, band):
    s_unit = unit_rows(jnp.dot(student_hidden, student_proj, preferred_element_type=jnp.float32)).reshape(BLOCKS, BLOCK, PROJ)
    t_unit = unit_rows(jnp.dot(teacher_hidden, teacher_proj, preferred_element_type=jnp.float32)).reshape(BLOCKS, BLOCK, PROJ)
    s_pos = student_chars.reshape(BLOCKS, BLOCK).astype(jnp.float32)
    t_pos = beside(teacher_chars.reshape(BLOCKS, BLOCK).astype(jnp.float32))
    ones_col = jnp.ones((BLOCKS,), jnp.int32)
    slot_mask = jnp.stack([band[:, 0], ones_col, band[:, 1]], 1).astype(jnp.float32)
    scores = jnp.einsum('bip,bkjp->bkij', s_unit.astype(jnp.float32), beside(t_unit).astype(jnp.float32)) / math.sqrt(PROJ)
    distance = jnp.abs(s_pos[:, None, :, None] - t_pos[:, :, None, :]) / (4.0 * BLOCK)
    kernel = jnp.exp(scores - distance) * slot_mask[:, :, None, None]
    row_scale = jnp.ones((BLOCKS, BLOCK), jnp.float32)
    col_scale = jnp.zeros((BLOCKS, 3, BLOCK), jnp.float32)
    for iteration in range(ITERS):
        partial_cols = lax.optimization_barrier(jnp.sum(row_scale[:, None, :, None] * kernel, axis=2))
        zero_row = jnp.zeros_like(partial_cols[:1, 0])
        column_total = partial_cols[:, 1] + jnp.concatenate([zero_row, partial_cols[:-1, 2]], 0) + jnp.concatenate([partial_cols[1:, 0], zero_row], 0)
        col_scale = beside(1.0 / column_total)
        row_scale = 1.0 / lax.optimization_barrier(jnp.sum(kernel * col_scale[:, :, None, :], axis=(1, 3)))
    plan = (row_scale[:, None, :, None] * kernel * col_scale[:, :, None, :]).astype(jnp.bfloat16)
    plan = jnp.transpose(plan, (0, 2, 1, 3)).reshape(BLOCKS, BLOCK, 3 * BLOCK)
    padded = jnp.pad(teacher_hidden, ((BLOCK, BLOCK), (0, 0)))

    def apply_block(index):
        start = (index * BLOCK).astype(jnp.int32)
        teacher_rows = lax.dynamic_slice_in_dim(padded, start, 3 * BLOCK, 0)
        plan_rows = lax.dynamic_index_in_dim(plan, index, 0, keepdims=False)
        return jnp.dot(plan_rows, teacher_rows, preferred_element_type=jnp.float32).astype(jnp.bfloat16)
    aligned = lax.map(apply_block, jnp.arange(BLOCKS, dtype=jnp.int32))
    return aligned.reshape(BLOCKS * BLOCK, DT)
```

```python
import math

import jax
import jax.numpy as jnp
from jax import lax
from jax.sharding import PartitionSpec as P

ITERS = 4

LOCAL_KERNEL_BYTES = 24 * 2**20

norm_eps = 1e-05


def shifted(block, axis, distance):
    devices = range(lax.axis_size(axis))
    route = [(i - distance, i) for i in devices if i - distance in devices]
    return lax.ppermute(block, axis, route)


def unit_rows(features):
    factor = lax.rsqrt(jnp.mean(features * features, axis=-1, keepdims=True) + norm_eps)
    return (features * factor).astype(jnp.bfloat16)


def beside(values):
    zero_row = jnp.zeros_like(values[:1])
    from_left = jnp.concatenate([zero_row, values[:-1]], 0)
    from_right = jnp.concatenate([values[1:], zero_row], 0)
    return jnp.stack([from_left, values, from_right], 1)


def tgrp_sum(value):
    if lax.axis_size("tgrp") == 2:
        return value + lax.ppermute(value, "tgrp", [(0, 1), (1, 0)])
    return lax.psum(value, "tgrp")


def body_local(
    student_hidden, teacher_hidden, student_proj, teacher_proj, student_chars, teacher_chars, band
):
    rows = student_hidden.shape[0]
    proj_width = student_proj.shape[1]
    blocks = lax.axis_size("seq")
    me = lax.axis_index("seq")

    s_part = jnp.dot(student_hidden, student_proj, preferred_element_type=jnp.float32)
    t_part = jnp.dot(teacher_hidden, teacher_proj, preferred_element_type=jnp.float32)
    feats = tgrp_sum(jnp.concatenate([s_part, t_part], 1))
    units = jnp.concatenate(
        [unit_rows(feats[:, :proj_width]), unit_rows(feats[:, proj_width:])], 1
    )
    ints = jnp.concatenate([student_chars, teacher_chars, band[0]])
    all_units = lax.all_gather(units, "seq")
    all_ints = lax.all_gather(ints, "seq")

    teacher_rows, all_units, all_ints = lax.optimization_barrier((teacher_hidden, all_units, all_ints))
    left_rows = shifted(teacher_rows, "seq", 1)
    right_rows = shifted(teacher_rows, "seq", -1)

    s_unit = all_units[:, :, :proj_width]
    t_unit = all_units[:, :, proj_width:]
    s_pos = all_ints[:, :rows].astype(jnp.float32)
    t_pos = beside(all_ints[:, rows : 2 * rows].astype(jnp.float32))
    flags = all_ints[:, 2 * rows :]
    ones_col = jnp.ones((blocks,), jnp.int32)
    slot_mask = jnp.stack([flags[:, 0], ones_col, flags[:, 1]], 1).astype(jnp.float32)
    scores = jnp.einsum(
        "bkjp,bip->bkji", beside(t_unit), s_unit, preferred_element_type=jnp.float32
    ) / math.sqrt(proj_width)
    distance = jnp.abs(s_pos[:, None, None, :] - t_pos[:, :, :, None]) / (4.0 * rows)
    kernel = jnp.exp(scores - distance) * slot_mask[:, :, None, None]

    def iterate(iteration, scales):
        row_scale, col_scale = scales
        partial_cols = jnp.sum(row_scale[:, None, None, :] * kernel, axis=3)
        zero_row = jnp.zeros_like(partial_cols[:1, 0])
        column_total = (
            partial_cols[:, 1]
            + jnp.concatenate([zero_row, partial_cols[:-1, 2]], 0)
            + jnp.concatenate([partial_cols[1:, 0], zero_row], 0)
        )
        col_scale = beside(1.0 / column_total)
        row_scale = 1.0 / jnp.sum(kernel * col_scale[:, :, :, None], axis=(1, 2))
        return row_scale, col_scale

    row_scale, col_scale = lax.fori_loop(
        0,
        ITERS,
        iterate,
        (jnp.ones((blocks, rows), jnp.float32), jnp.zeros((blocks, 3, rows), jnp.float32)),
    )
    own_kernel = lax.dynamic_index_in_dim(kernel, me, 0, keepdims=False)
    own_row = lax.dynamic_index_in_dim(row_scale, me, 0, keepdims=False)
    own_col = lax.dynamic_index_in_dim(col_scale, me, 0, keepdims=False)
    plan = (own_row[None, None, :] * own_kernel * own_col[:, :, None]).astype(jnp.bfloat16)
    along_j = (((0,), (0,)), ((), ()))
    aligned = lax.dot_general(plan[1], teacher_hidden, along_j, preferred_element_type=jnp.float32)
    aligned = aligned + lax.dot_general(plan[0], left_rows, along_j, preferred_element_type=jnp.float32)
    aligned = aligned + lax.dot_general(plan[2], right_rows, along_j, preferred_element_type=jnp.float32)
    return aligned.astype(jnp.bfloat16)


def body_banded(
    student_hidden, teacher_hidden, student_proj, teacher_proj, student_chars, teacher_chars, band
):
    block_rows = student_hidden.shape[0]
    proj_width = student_proj.shape[1]
    s_part = jnp.dot(student_hidden, student_proj, preferred_element_type=jnp.float32)
    t_part = jnp.dot(teacher_hidden, teacher_proj, preferred_element_type=jnp.float32)
    s_feat, t_feat = lax.psum((s_part, t_part), "tgrp")
    s_unit = unit_rows(s_feat)
    t_unit = unit_rows(t_feat)
    left_rows, left_unit, left_chars = shifted((teacher_hidden, t_unit, teacher_chars), "seq", 1)
    right_rows, right_unit, right_chars = shifted(
        (teacher_hidden, t_unit, teacher_chars), "seq", -1
    )
    near_unit = jnp.stack([left_unit, t_unit, right_unit])
    near_pos = jnp.stack([left_chars, teacher_chars, right_chars]).astype(jnp.float32)
    s_pos = student_chars.astype(jnp.float32)
    flags = band[0]
    slot_mask = jnp.stack([flags[0], jnp.ones((), jnp.int32), flags[1]]).astype(jnp.float32)
    scores = jnp.einsum(
        "ip,kjp->kij", s_unit, near_unit, preferred_element_type=jnp.float32
    ) / math.sqrt(proj_width)
    distance = jnp.abs(s_pos[None, :, None] - near_pos[:, None, :]) / (4.0 * block_rows)
    kernel = jnp.exp(scores - distance) * slot_mask[:, None, None]
    row_scale = jnp.ones((block_rows,), jnp.float32)
    col_scale = jnp.zeros((3, block_rows), jnp.float32)
    for iteration in range(ITERS):
        partial_cols = jnp.sum(row_scale[None, :, None] * kernel, axis=1)
        left_one = shifted(partial_cols[1:], "seq", 1)
        left_two = shifted(partial_cols[2:], "seq", 2)
        right_one = shifted(partial_cols[:2], "seq", -1)
        right_two = shifted(partial_cols[:1], "seq", -2)
        column_total = jnp.stack(
            [
                left_two[0] + left_one[0] + partial_cols[0],
                left_one[1] + partial_cols[1] + right_one[0],
                partial_cols[2] + right_one[1] + right_two[0],
            ]
        )
        col_scale = slot_mask[:, None] / jnp.where(slot_mask[:, None] > 0.0, column_total, 1.0)
        row_scale = 1.0 / jnp.sum(kernel * col_scale[:, None, :], axis=(0, 2))
    plan = (row_scale[None, :, None] * kernel * col_scale[:, None, :]).astype(jnp.bfloat16)
    aligned = jnp.dot(plan[0], left_rows, preferred_element_type=jnp.float32)
    aligned = aligned + jnp.dot(plan[1], teacher_hidden, preferred_element_type=jnp.float32)
    aligned = aligned + jnp.dot(plan[2], right_rows, preferred_element_type=jnp.float32)
    return aligned.astype(jnp.bfloat16)


def solution(mesh):
    blocks = mesh.shape["seq"]

    def body(*args):
        rows = args[0].shape[0]
        if blocks * 3 * rows * rows * 4 <= LOCAL_KERNEL_BYTES:
            return body_local(*args)
        return body_banded(*args)

    return jax.shard_map(
        body,
        mesh=mesh,
        in_specs=(
            P(("groups", "seq"), "tgrp"),
            P(("groups", "seq"), "tgrp"),
            P("tgrp", None),
            P("tgrp", None),
            P(("groups", "seq")),
            P(("groups", "seq")),
            P(("groups", "seq"), None),
        ),
        out_specs=P(("groups", "seq"), "tgrp"),
        check_vma=False,
    )
```

```python
import math

import jax
import jax.numpy as jnp
from jax import lax
from jax.sharding import PartitionSpec as P

ITERS = 4

LOCAL_KERNEL_BYTES = 24 * 2**20

norm_eps = 1e-05


def shifted(block, axis, distance):
    devices = range(lax.axis_size(axis))
    route = [(i - distance, i) for i in devices if i - distance in devices]
    return lax.ppermute(block, axis, route)


def unit_rows(features):
    factor = lax.rsqrt(jnp.mean(features * features, axis=-1, keepdims=True) + norm_eps)
    return (features * factor).astype(jnp.bfloat16)


def beside(values):
    zero_row = jnp.zeros_like(values[:1])
    from_left = jnp.concatenate([zero_row, values[:-1]], 0)
    from_right = jnp.concatenate([values[1:], zero_row], 0)
    return jnp.stack([from_left, values, from_right], 1)


def tgrp_sum(value):
    if lax.axis_size("tgrp") == 2:
        return value + lax.ppermute(value, "tgrp", [(0, 1), (1, 0)])
    return lax.psum(value, "tgrp")


def body_local(
    student_hidden, teacher_hidden, student_proj, teacher_proj, student_chars, teacher_chars, band
):
    rows = student_hidden.shape[0]
    proj_width = student_proj.shape[1]
    blocks = lax.axis_size("seq")
    me = lax.axis_index("seq")

    s_part = jnp.dot(student_hidden, student_proj, preferred_element_type=jnp.float32)
    t_part = jnp.dot(teacher_hidden, teacher_proj, preferred_element_type=jnp.float32)
    feats = tgrp_sum(jnp.concatenate([s_part, t_part], 1))
    units = jnp.concatenate(
        [unit_rows(feats[:, :proj_width]), unit_rows(feats[:, proj_width:])], 1
    )
    digits = jnp.stack([student_chars, teacher_chars])
    digits = jnp.stack([digits // 4096, digits // 64 % 64, digits % 64], 1)
    digit_rows = digits.reshape(-1, units.shape[1]).astype(jnp.bfloat16)
    flag_row = jnp.zeros((1, units.shape[1]), jnp.bfloat16).at[0, :2].set(band[0].astype(jnp.bfloat16))
    extra = jnp.concatenate([digit_rows, flag_row], 0)
    pad = -(rows + extra.shape[0]) % 16
    packed = jnp.concatenate([units, extra, jnp.zeros((pad, units.shape[1]), jnp.bfloat16)], 0)
    gathered = lax.all_gather(packed, "seq")

    teacher_rows, gathered = lax.optimization_barrier((teacher_hidden, gathered))
    left_rows = shifted(teacher_rows, "seq", 1)
    right_rows = shifted(teacher_rows, "seq", -1)

    s_unit = gathered[:, :rows, :proj_width]
    t_unit = gathered[:, :rows, proj_width:]
    got = gathered[:, rows : rows + digit_rows.shape[0]].astype(jnp.float32).reshape(blocks, 2, 3, rows)
    chars = got[:, :, 0] * 4096.0 + got[:, :, 1] * 64.0 + got[:, :, 2]
    s_pos = chars[:, 0]
    t_pos = beside(chars[:, 1])
    flags = gathered[:, rows + digit_rows.shape[0], :2].astype(jnp.int32)
    ones_col = jnp.ones((blocks,), jnp.int32)
    slot_mask = jnp.stack([flags[:, 0], ones_col, flags[:, 1]], 1).astype(jnp.float32)
    scores = jnp.einsum(
        "bkjp,bip->bkji", beside(t_unit), s_unit, preferred_element_type=jnp.float32
    ) / math.sqrt(proj_width)
    distance = jnp.abs(s_pos[:, None, None, :] - t_pos[:, :, :, None]) / (4.0 * rows)
    kernel = jnp.exp(scores - distance) * slot_mask[:, :, None, None]

    def iterate(iteration, scales):
        row_scale, col_scale = scales
        partial_cols = jnp.sum(row_scale[:, None, None, :] * kernel, axis=3)
        zero_row = jnp.zeros_like(partial_cols[:1, 0])
        column_total = (
            partial_cols[:, 1]
            + jnp.concatenate([zero_row, partial_cols[:-1, 2]], 0)
            + jnp.concatenate([partial_cols[1:, 0], zero_row], 0)
        )
        col_scale = beside(1.0 / column_total)
        row_scale = 1.0 / jnp.sum(kernel * col_scale[:, :, :, None], axis=(1, 2))
        return row_scale, col_scale

    row_scale, col_scale = lax.fori_loop(
        0,
        ITERS,
        iterate,
        (jnp.ones((blocks, rows), jnp.float32), jnp.zeros((blocks, 3, rows), jnp.float32)),
    )
    own_kernel = lax.dynamic_index_in_dim(kernel, me, 0, keepdims=False)
    own_row = lax.dynamic_index_in_dim(row_scale, me, 0, keepdims=False)
    own_col = lax.dynamic_index_in_dim(col_scale, me, 0, keepdims=False)
    plan = (own_row[None, None, :] * own_kernel * own_col[:, :, None]).astype(jnp.bfloat16)
    along_j = (((0,), (0,)), ((), ()))
    aligned = lax.dot_general(plan[1], teacher_hidden, along_j, preferred_element_type=jnp.float32)
    aligned = aligned + lax.dot_general(plan[0], left_rows, along_j, preferred_element_type=jnp.float32)
    aligned = aligned + lax.dot_general(plan[2], right_rows, along_j, preferred_element_type=jnp.float32)
    return aligned.astype(jnp.bfloat16)


def body_banded(
    student_hidden, teacher_hidden, student_proj, teacher_proj, student_chars, teacher_chars, band
):
    block_rows = student_hidden.shape[0]
    proj_width = student_proj.shape[1]
    s_part = jnp.dot(student_hidden, student_proj, preferred_element_type=jnp.float32)
    t_part = jnp.dot(teacher_hidden, teacher_proj, preferred_element_type=jnp.float32)
    s_feat, t_feat = lax.psum((s_part, t_part), "tgrp")
    s_unit = unit_rows(s_feat)
    t_unit = unit_rows(t_feat)
    left_rows, left_unit, left_chars = shifted((teacher_hidden, t_unit, teacher_chars), "seq", 1)
    right_rows, right_unit, right_chars = shifted(
        (teacher_hidden, t_unit, teacher_chars), "seq", -1
    )
    near_unit = jnp.stack([left_unit, t_unit, right_unit])
    near_pos = jnp.stack([left_chars, teacher_chars, right_chars]).astype(jnp.float32)
    s_pos = student_chars.astype(jnp.float32)
    flags = band[0]
    slot_mask = jnp.stack([flags[0], jnp.ones((), jnp.int32), flags[1]]).astype(jnp.float32)
    scores = jnp.einsum(
        "ip,kjp->kij", s_unit, near_unit, preferred_element_type=jnp.float32
    ) / math.sqrt(proj_width)
    distance = jnp.abs(s_pos[None, :, None] - near_pos[:, None, :]) / (4.0 * block_rows)
    kernel = jnp.exp(scores - distance) * slot_mask[:, None, None]
    row_scale = jnp.ones((block_rows,), jnp.float32)
    col_scale = jnp.zeros((3, block_rows), jnp.float32)
    for iteration in range(ITERS):
        partial_cols = jnp.sum(row_scale[None, :, None] * kernel, axis=1)
        left_one = shifted(partial_cols[1:], "seq", 1)
        left_two = shifted(partial_cols[2:], "seq", 2)
        right_one = shifted(partial_cols[:2], "seq", -1)
        right_two = shifted(partial_cols[:1], "seq", -2)
        column_total = jnp.stack(
            [
                left_two[0] + left_one[0] + partial_cols[0],
                left_one[1] + partial_cols[1] + right_one[0],
                partial_cols[2] + right_one[1] + right_two[0],
            ]
        )
        col_scale = slot_mask[:, None] / jnp.where(slot_mask[:, None] > 0.0, column_total, 1.0)
        row_scale = 1.0 / jnp.sum(kernel * col_scale[:, None, :], axis=(0, 2))
    plan = (row_scale[None, :, None] * kernel * col_scale[:, None, :]).astype(jnp.bfloat16)
    aligned = jnp.dot(plan[0], left_rows, preferred_element_type=jnp.float32)
    aligned = aligned + jnp.dot(plan[1], teacher_hidden, preferred_element_type=jnp.float32)
    aligned = aligned + jnp.dot(plan[2], right_rows, preferred_element_type=jnp.float32)
    return aligned.astype(jnp.bfloat16)


def solution(mesh):
    blocks = mesh.shape["seq"]

    def body(*args):
        rows = args[0].shape[0]
        if blocks * 3 * rows * rows * 4 <= LOCAL_KERNEL_BYTES:
            return body_local(*args)
        return body_banded(*args)

    return jax.shard_map(
        body,
        mesh=mesh,
        in_specs=(
            P(("groups", "seq"), "tgrp"),
            P(("groups", "seq"), "tgrp"),
            P("tgrp", None),
            P("tgrp", None),
            P(("groups", "seq")),
            P(("groups", "seq")),
            P(("groups", "seq"), None),
        ),
        out_specs=P(("groups", "seq"), "tgrp"),
        check_vma=False,
    )
```

```python
import math

import jax
import jax.numpy as jnp
from jax import lax
from jax.sharding import PartitionSpec as P

ITERS = 4

LOCAL_KERNEL_BYTES = 24 * 2**20

norm_eps = 1e-05


def shifted(block, axis, distance):
    devices = range(lax.axis_size(axis))
    route = [(i - distance, i) for i in devices if i - distance in devices]
    return lax.ppermute(block, axis, route)


def unit_rows(features):
    factor = lax.rsqrt(jnp.mean(features * features, axis=-1, keepdims=True) + norm_eps)
    return (features * factor).astype(jnp.bfloat16)


def beside(values):
    zero_row = jnp.zeros_like(values[:1])
    from_left = jnp.concatenate([zero_row, values[:-1]], 0)
    from_right = jnp.concatenate([values[1:], zero_row], 0)
    return jnp.stack([from_left, values, from_right], 1)


def tgrp_sum(value):
    if lax.axis_size("tgrp") == 2:
        return value + lax.ppermute(value, "tgrp", [(0, 1), (1, 0)])
    return lax.psum(value, "tgrp")


def body_local(
    student_hidden, teacher_hidden, student_proj, teacher_proj, student_chars, teacher_chars, band
):
    rows = student_hidden.shape[0]
    proj_width = student_proj.shape[1]
    blocks = lax.axis_size("seq")
    me = lax.axis_index("seq")

    s_part = jnp.dot(student_hidden, student_proj, preferred_element_type=jnp.float32)
    t_part = jnp.dot(teacher_hidden, teacher_proj, preferred_element_type=jnp.float32)
    feats = tgrp_sum(jnp.concatenate([s_part, t_part], 1))
    units = jnp.concatenate(
        [unit_rows(feats[:, :proj_width]), unit_rows(feats[:, proj_width:])], 1
    )
    digits = jnp.stack([student_chars, teacher_chars])
    digits = jnp.stack([digits // 4096, digits // 64 % 64, digits % 64], 1)
    digit_rows = digits.reshape(-1, units.shape[1]).astype(jnp.bfloat16)
    flag_row = jnp.zeros((1, units.shape[1]), jnp.bfloat16).at[0, :2].set(band[0].astype(jnp.bfloat16))
    extra = jnp.concatenate([digit_rows, flag_row], 0)
    pad = -(rows + extra.shape[0]) % 16
    packed = jnp.concatenate([units, extra, jnp.zeros((pad, units.shape[1]), jnp.bfloat16)], 0)
    gathered = lax.all_gather(packed, "seq")

    left_rows = shifted(teacher_hidden, "seq", 1)
    right_rows = shifted(teacher_hidden, "seq", -1)

    s_unit = gathered[:, :rows, :proj_width]
    t_unit = gathered[:, :rows, proj_width:]
    got = gathered[:, rows : rows + digit_rows.shape[0]].astype(jnp.float32).reshape(blocks, 2, 3, rows)
    chars = got[:, :, 0] * 4096.0 + got[:, :, 1] * 64.0 + got[:, :, 2]
    s_pos = chars[:, 0]
    t_pos = beside(chars[:, 1])
    flags = gathered[:, rows + digit_rows.shape[0]].astype(jnp.float32)
    ones_col = jnp.ones((blocks,), jnp.float32)
    slot_mask = jnp.stack([flags[:, 0], ones_col, flags[:, 1]], 1)
    scores = jnp.einsum(
        "bkjp,bip->bkji", beside(t_unit), s_unit, preferred_element_type=jnp.float32
    ) / math.sqrt(proj_width)
    distance = jnp.abs(s_pos[:, None, None, :] - t_pos[:, :, :, None]) / (4.0 * rows)
    kernel = jnp.exp(scores - distance) * slot_mask[:, :, None, None]

    def iterate(iteration, scales):
        row_scale, col_scale = scales
        partial_cols = jnp.sum(row_scale[:, None, None, :] * kernel, axis=3)
        zero_row = jnp.zeros_like(partial_cols[:1, 0])
        column_total = (
            partial_cols[:, 1]
            + jnp.concatenate([zero_row, partial_cols[:-1, 2]], 0)
            + jnp.concatenate([partial_cols[1:, 0], zero_row], 0)
        )
        col_scale = beside(1.0 / column_total)
        row_scale = 1.0 / jnp.sum(kernel * col_scale[:, :, :, None], axis=(1, 2))
        return row_scale, col_scale

    row_scale, col_scale = lax.fori_loop(
        0,
        ITERS,
        iterate,
        (jnp.ones((blocks, rows), jnp.float32), jnp.zeros((blocks, 3, rows), jnp.float32)),
    )
    own_kernel = lax.dynamic_index_in_dim(kernel, me, 0, keepdims=False)
    own_row = lax.dynamic_index_in_dim(row_scale, me, 0, keepdims=False)
    own_col = lax.dynamic_index_in_dim(col_scale, me, 0, keepdims=False)
    plan = (own_row[None, None, :] * own_kernel * own_col[:, :, None]).astype(jnp.bfloat16)
    along_j = (((0,), (0,)), ((), ()))
    aligned = lax.dot_general(plan[1], teacher_hidden, along_j, preferred_element_type=jnp.float32)
    aligned = aligned + lax.dot_general(plan[0], left_rows, along_j, preferred_element_type=jnp.float32)
    aligned = aligned + lax.dot_general(plan[2], right_rows, along_j, preferred_element_type=jnp.float32)
    return aligned.astype(jnp.bfloat16)


def body_banded(
    student_hidden, teacher_hidden, student_proj, teacher_proj, student_chars, teacher_chars, band
):
    block_rows = student_hidden.shape[0]
    proj_width = student_proj.shape[1]
    s_part = jnp.dot(student_hidden, student_proj, preferred_element_type=jnp.float32)
    t_part = jnp.dot(teacher_hidden, teacher_proj, preferred_element_type=jnp.float32)
    s_feat, t_feat = lax.psum((s_part, t_part), "tgrp")
    s_unit = unit_rows(s_feat)
    t_unit = unit_rows(t_feat)
    left_rows, left_unit, left_chars = shifted((teacher_hidden, t_unit, teacher_chars), "seq", 1)
    right_rows, right_unit, right_chars = shifted(
        (teacher_hidden, t_unit, teacher_chars), "seq", -1
    )
    near_unit = jnp.stack([left_unit, t_unit, right_unit])
    near_pos = jnp.stack([left_chars, teacher_chars, right_chars]).astype(jnp.float32)
    s_pos = student_chars.astype(jnp.float32)
    flags = band[0]
    slot_mask = jnp.stack([flags[0], jnp.ones((), jnp.int32), flags[1]]).astype(jnp.float32)
    scores = jnp.einsum(
        "ip,kjp->kij", s_unit, near_unit, preferred_element_type=jnp.float32
    ) / math.sqrt(proj_width)
    distance = jnp.abs(s_pos[None, :, None] - near_pos[:, None, :]) / (4.0 * block_rows)
    kernel = jnp.exp(scores - distance) * slot_mask[:, None, None]
    row_scale = jnp.ones((block_rows,), jnp.float32)
    col_scale = jnp.zeros((3, block_rows), jnp.float32)
    for iteration in range(ITERS):
        partial_cols = jnp.sum(row_scale[None, :, None] * kernel, axis=1)
        left_one = shifted(partial_cols[1:], "seq", 1)
        left_two = shifted(partial_cols[2:], "seq", 2)
        right_one = shifted(partial_cols[:2], "seq", -1)
        right_two = shifted(partial_cols[:1], "seq", -2)
        column_total = jnp.stack(
            [
                left_two[0] + left_one[0] + partial_cols[0],
                left_one[1] + partial_cols[1] + right_one[0],
                partial_cols[2] + right_one[1] + right_two[0],
            ]
        )
        col_scale = slot_mask[:, None] / jnp.where(slot_mask[:, None] > 0.0, column_total, 1.0)
        row_scale = 1.0 / jnp.sum(kernel * col_scale[:, None, :], axis=(0, 2))
    plan = (row_scale[None, :, None] * kernel * col_scale[:, None, :]).astype(jnp.bfloat16)
    aligned = jnp.dot(plan[0], left_rows, preferred_element_type=jnp.float32)
    aligned = aligned + jnp.dot(plan[1], teacher_hidden, preferred_element_type=jnp.float32)
    aligned = aligned + jnp.dot(plan[2], right_rows, preferred_element_type=jnp.float32)
    return aligned.astype(jnp.bfloat16)


def solution(mesh):
    blocks = mesh.shape["seq"]

    def body(*args):
        rows = args[0].shape[0]
        if blocks * 3 * rows * rows * 4 <= LOCAL_KERNEL_BYTES:
            return body_local(*args)
        return body_banded(*args)

    return jax.shard_map(
        body,
        mesh=mesh,
        in_specs=(
            P(("groups", "seq"), "tgrp"),
            P(("groups", "seq"), "tgrp"),
            P("tgrp", None),
            P("tgrp", None),
            P(("groups", "seq")),
            P(("groups", "seq")),
            P(("groups", "seq"), None),
        ),
        out_specs=P(("groups", "seq"), "tgrp"),
        check_vma=False,
    )
```

```python
import math

import jax
import jax.numpy as jnp
from jax import lax
from jax.sharding import PartitionSpec as P

ITERS = 4

LOCAL_KERNEL_BYTES = 24 * 2**20

norm_eps = 1e-05


def shifted(block, axis, distance):
    devices = range(lax.axis_size(axis))
    route = [(i - distance, i) for i in devices if i - distance in devices]
    return lax.ppermute(block, axis, route)


def unit_rows(features):
    factor = lax.rsqrt(jnp.mean(features * features, axis=-1, keepdims=True) + norm_eps)
    return (features * factor).astype(jnp.bfloat16)


def beside(values):
    zero_row = jnp.zeros_like(values[:1])
    from_left = jnp.concatenate([zero_row, values[:-1]], 0)
    from_right = jnp.concatenate([values[1:], zero_row], 0)
    return jnp.stack([from_left, values, from_right], 1)


def tgrp_sum(value):
    if lax.axis_size("tgrp") == 2:
        return value + lax.ppermute(value, "tgrp", [(0, 1), (1, 0)])
    return lax.psum(value, "tgrp")


def gather_halves(packed):
    if lax.axis_size("tgrp") != 2:
        return lax.all_gather(packed, "seq")
    half = packed.shape[1] // 2
    core = lax.axis_index("tgrp")
    mine = lax.dynamic_slice_in_dim(packed, core * half, half, 1)
    got = lax.all_gather(mine, "seq")
    theirs = lax.ppermute(got, "tgrp", [(0, 1), (1, 0)])
    first = jnp.where(core == 0, got, theirs)
    second = jnp.where(core == 0, theirs, got)
    return jnp.concatenate([first, second], 2)


def body_local(
    student_hidden, teacher_hidden, student_proj, teacher_proj, student_chars, teacher_chars, band
):
    rows = student_hidden.shape[0]
    proj_width = student_proj.shape[1]
    blocks = lax.axis_size("seq")
    me = lax.axis_index("seq")

    s_part = jnp.dot(student_hidden, student_proj, preferred_element_type=jnp.float32)
    t_part = jnp.dot(teacher_hidden, teacher_proj, preferred_element_type=jnp.float32)
    feats = tgrp_sum(jnp.concatenate([s_part, t_part], 1))
    units = jnp.concatenate(
        [unit_rows(feats[:, :proj_width]), unit_rows(feats[:, proj_width:])], 1
    )
    digits = jnp.stack([student_chars, teacher_chars])
    digits = jnp.stack([digits // 4096, digits // 64 % 64, digits % 64], 1)
    digit_rows = digits.reshape(-1, units.shape[1]).astype(jnp.bfloat16)
    flag_row = jnp.zeros((1, units.shape[1]), jnp.bfloat16).at[0, :2].set(band[0].astype(jnp.bfloat16))
    extra = jnp.concatenate([digit_rows, flag_row], 0)
    pad = -(rows + extra.shape[0]) % 16
    packed = jnp.concatenate([units, extra, jnp.zeros((pad, units.shape[1]), jnp.bfloat16)], 0)
    gathered = gather_halves(packed)

    teacher_rows, gathered = lax.optimization_barrier((teacher_hidden, gathered))
    left_rows = shifted(teacher_rows, "seq", 1)
    right_rows = shifted(teacher_rows, "seq", -1)

    s_unit = gathered[:, :rows, :proj_width]
    t_unit = gathered[:, :rows, proj_width:]
    got = gathered[:, rows : rows + digit_rows.shape[0]].astype(jnp.float32).reshape(blocks, 2, 3, rows)
    chars = got[:, :, 0] * 4096.0 + got[:, :, 1] * 64.0 + got[:, :, 2]
    s_pos = chars[:, 0]
    t_pos = beside(chars[:, 1])
    flags = gathered[:, rows + digit_rows.shape[0]].astype(jnp.float32)
    ones_col = jnp.ones((blocks,), jnp.float32)
    slot_mask = jnp.stack([flags[:, 0], ones_col, flags[:, 1]], 1)
    scores = jnp.einsum(
        "bkjp,bip->bkji", beside(t_unit), s_unit, preferred_element_type=jnp.float32
    ) / math.sqrt(proj_width)
    distance = jnp.abs(s_pos[:, None, None, :] - t_pos[:, :, :, None]) / (4.0 * rows)
    kernel = jnp.exp(scores - distance) * slot_mask[:, :, None, None]

    def iterate(iteration, scales):
        row_scale, col_scale = scales
        partial_cols = jnp.sum(row_scale[:, None, None, :] * kernel, axis=3)
        zero_row = jnp.zeros_like(partial_cols[:1, 0])
        column_total = (
            partial_cols[:, 1]
            + jnp.concatenate([zero_row, partial_cols[:-1, 2]], 0)
            + jnp.concatenate([partial_cols[1:, 0], zero_row], 0)
        )
        col_scale = beside(1.0 / column_total)
        row_scale = 1.0 / jnp.sum(kernel * col_scale[:, :, :, None], axis=(1, 2))
        return row_scale, col_scale

    row_scale, col_scale = lax.fori_loop(
        0,
        ITERS,
        iterate,
        (jnp.ones((blocks, rows), jnp.float32), jnp.zeros((blocks, 3, rows), jnp.float32)),
    )
    own_kernel = lax.dynamic_index_in_dim(kernel, me, 0, keepdims=False)
    own_row = lax.dynamic_index_in_dim(row_scale, me, 0, keepdims=False)
    own_col = lax.dynamic_index_in_dim(col_scale, me, 0, keepdims=False)
    plan = (own_row[None, None, :] * own_kernel * own_col[:, :, None]).astype(jnp.bfloat16)
    along_j = (((0,), (0,)), ((), ()))
    aligned = lax.dot_general(plan[1], teacher_hidden, along_j, preferred_element_type=jnp.float32)
    aligned = aligned + lax.dot_general(plan[0], left_rows, along_j, preferred_element_type=jnp.float32)
    aligned = aligned + lax.dot_general(plan[2], right_rows, along_j, preferred_element_type=jnp.float32)
    return aligned.astype(jnp.bfloat16)


def body_banded(
    student_hidden, teacher_hidden, student_proj, teacher_proj, student_chars, teacher_chars, band
):
    block_rows = student_hidden.shape[0]
    proj_width = student_proj.shape[1]
    s_part = jnp.dot(student_hidden, student_proj, preferred_element_type=jnp.float32)
    t_part = jnp.dot(teacher_hidden, teacher_proj, preferred_element_type=jnp.float32)
    s_feat, t_feat = lax.psum((s_part, t_part), "tgrp")
    s_unit = unit_rows(s_feat)
    t_unit = unit_rows(t_feat)
    left_rows, left_unit, left_chars = shifted((teacher_hidden, t_unit, teacher_chars), "seq", 1)
    right_rows, right_unit, right_chars = shifted(
        (teacher_hidden, t_unit, teacher_chars), "seq", -1
    )
    near_unit = jnp.stack([left_unit, t_unit, right_unit])
    near_pos = jnp.stack([left_chars, teacher_chars, right_chars]).astype(jnp.float32)
    s_pos = student_chars.astype(jnp.float32)
    flags = band[0]
    slot_mask = jnp.stack([flags[0], jnp.ones((), jnp.int32), flags[1]]).astype(jnp.float32)
    scores = jnp.einsum(
        "ip,kjp->kij", s_unit, near_unit, preferred_element_type=jnp.float32
    ) / math.sqrt(proj_width)
    distance = jnp.abs(s_pos[None, :, None] - near_pos[:, None, :]) / (4.0 * block_rows)
    kernel = jnp.exp(scores - distance) * slot_mask[:, None, None]
    row_scale = jnp.ones((block_rows,), jnp.float32)
    col_scale = jnp.zeros((3, block_rows), jnp.float32)
    for iteration in range(ITERS):
        partial_cols = jnp.sum(row_scale[None, :, None] * kernel, axis=1)
        left_one = shifted(partial_cols[1:], "seq", 1)
        left_two = shifted(partial_cols[2:], "seq", 2)
        right_one = shifted(partial_cols[:2], "seq", -1)
        right_two = shifted(partial_cols[:1], "seq", -2)
        column_total = jnp.stack(
            [
                left_two[0] + left_one[0] + partial_cols[0],
                left_one[1] + partial_cols[1] + right_one[0],
                partial_cols[2] + right_one[1] + right_two[0],
            ]
        )
        col_scale = slot_mask[:, None] / jnp.where(slot_mask[:, None] > 0.0, column_total, 1.0)
        row_scale = 1.0 / jnp.sum(kernel * col_scale[:, None, :], axis=(0, 2))
    plan = (row_scale[None, :, None] * kernel * col_scale[:, None, :]).astype(jnp.bfloat16)
    aligned = jnp.dot(plan[0], left_rows, preferred_element_type=jnp.float32)
    aligned = aligned + jnp.dot(plan[1], teacher_hidden, preferred_element_type=jnp.float32)
    aligned = aligned + jnp.dot(plan[2], right_rows, preferred_element_type=jnp.float32)
    return aligned.astype(jnp.bfloat16)


def solution(mesh):
    blocks = mesh.shape["seq"]

    def body(*args):
        rows = args[0].shape[0]
        if blocks * 3 * rows * rows * 4 <= LOCAL_KERNEL_BYTES:
            return body_local(*args)
        return body_banded(*args)

    return jax.shard_map(
        body,
        mesh=mesh,
        in_specs=(
            P(("groups", "seq"), "tgrp"),
            P(("groups", "seq"), "tgrp"),
            P("tgrp", None),
            P("tgrp", None),
            P(("groups", "seq")),
            P(("groups", "seq")),
            P(("groups", "seq"), None),
        ),
        out_specs=P(("groups", "seq"), "tgrp"),
        check_vma=False,
    )
```

```python
import math

import jax
import jax.numpy as jnp
from jax import lax
from jax.sharding import PartitionSpec as P

ITERS = 4

LOCAL_KERNEL_BYTES = 24 * 2**20

norm_eps = 1e-05


def shifted(block, axis, distance):
    devices = range(lax.axis_size(axis))
    route = [(i - distance, i) for i in devices if i - distance in devices]
    return lax.ppermute(block, axis, route)


def unit_rows(features):
    factor = lax.rsqrt(jnp.mean(features * features, axis=-1, keepdims=True) + norm_eps)
    return (features * factor).astype(jnp.bfloat16)


def beside(values):
    zero_row = jnp.zeros_like(values[:1])
    from_left = jnp.concatenate([zero_row, values[:-1]], 0)
    from_right = jnp.concatenate([values[1:], zero_row], 0)
    return jnp.stack([from_left, values, from_right], 1)


def tgrp_sum(value):
    if lax.axis_size("tgrp") == 2:
        return value + lax.ppermute(value, "tgrp", [(0, 1), (1, 0)])
    return lax.psum(value, "tgrp")


def gather_halves(packed):
    if lax.axis_size("tgrp") != 2:
        return lax.all_gather(packed, "seq")
    half = packed.shape[1] // 2
    core = lax.axis_index("tgrp")
    mine = lax.dynamic_slice_in_dim(packed, core * half, half, 1)
    got = lax.all_gather(mine, "seq")
    theirs = lax.ppermute(got, "tgrp", [(0, 1), (1, 0)])
    first = jnp.where(core == 0, got, theirs)
    second = jnp.where(core == 0, theirs, got)
    return jnp.concatenate([first, second], 2)


def body_local(
    student_hidden, teacher_hidden, student_proj, teacher_proj, student_chars, teacher_chars, band
):
    rows = student_hidden.shape[0]
    proj_width = student_proj.shape[1]
    blocks = lax.axis_size("seq")
    me = lax.axis_index("seq")

    s_part = jnp.dot(student_hidden, student_proj, preferred_element_type=jnp.float32)
    t_part = jnp.dot(teacher_hidden, teacher_proj, preferred_element_type=jnp.float32)
    feats = tgrp_sum(jnp.concatenate([s_part, t_part], 1))
    units = jnp.concatenate(
        [unit_rows(feats[:, :proj_width]), unit_rows(feats[:, proj_width:])], 1
    )
    digits = jnp.stack([student_chars, teacher_chars])
    digits = jnp.stack([digits // 4096, digits // 64 % 64, digits % 64], 1)
    digit_rows = digits.reshape(-1, units.shape[1]).astype(jnp.bfloat16)
    flag_row = jnp.zeros((1, units.shape[1]), jnp.bfloat16).at[0, :2].set(band[0].astype(jnp.bfloat16))
    extra = jnp.concatenate([digit_rows, flag_row], 0)
    pad = -(rows + extra.shape[0]) % 16
    packed = jnp.concatenate([units, extra, jnp.zeros((pad, units.shape[1]), jnp.bfloat16)], 0)
    gathered = gather_halves(packed)

    teacher_rows, gathered = lax.optimization_barrier((teacher_hidden, gathered))
    width = teacher_rows.shape[1]
    pieces = 2 if width % 256 == 0 else 1
    cut = width // pieces
    column_pieces = [teacher_rows[:, p * cut : (p + 1) * cut] for p in range(pieces)]
    near_pieces = [
        (shifted(piece, "seq", 1), piece, shifted(piece, "seq", -1)) for piece in column_pieces
    ]

    s_unit = gathered[:, :rows, :proj_width]
    t_unit = gathered[:, :rows, proj_width:]
    got = gathered[:, rows : rows + digit_rows.shape[0]].astype(jnp.float32).reshape(blocks, 2, 3, rows)
    chars = got[:, :, 0] * 4096.0 + got[:, :, 1] * 64.0 + got[:, :, 2]
    s_pos = chars[:, 0]
    t_pos = beside(chars[:, 1])
    flags = gathered[:, rows + digit_rows.shape[0]].astype(jnp.float32)
    ones_col = jnp.ones((blocks,), jnp.float32)
    slot_mask = jnp.stack([flags[:, 0], ones_col, flags[:, 1]], 1)
    scores = jnp.einsum(
        "bkjp,bip->bkji", beside(t_unit), s_unit, preferred_element_type=jnp.float32
    ) / math.sqrt(proj_width)
    distance = jnp.abs(s_pos[:, None, None, :] - t_pos[:, :, :, None]) / (4.0 * rows)
    kernel = jnp.exp(scores - distance) * slot_mask[:, :, None, None]

    def iterate(iteration, scales):
        row_scale, col_scale = scales
        partial_cols = jnp.sum(row_scale[:, None, None, :] * kernel, axis=3)
        zero_row = jnp.zeros_like(partial_cols[:1, 0])
        column_total = (
            partial_cols[:, 1]
            + jnp.concatenate([zero_row, partial_cols[:-1, 2]], 0)
            + jnp.concatenate([partial_cols[1:, 0], zero_row], 0)
        )
        col_scale = beside(1.0 / column_total)
        row_scale = 1.0 / jnp.sum(kernel * col_scale[:, :, :, None], axis=(1, 2))
        return row_scale, col_scale

    row_scale, col_scale = lax.fori_loop(
        0,
        ITERS,
        iterate,
        (jnp.ones((blocks, rows), jnp.float32), jnp.zeros((blocks, 3, rows), jnp.float32)),
    )
    own_kernel = lax.dynamic_index_in_dim(kernel, me, 0, keepdims=False)
    own_row = lax.dynamic_index_in_dim(row_scale, me, 0, keepdims=False)
    own_col = lax.dynamic_index_in_dim(col_scale, me, 0, keepdims=False)
    plan = (own_row[None, None, :] * own_kernel * own_col[:, :, None]).astype(jnp.bfloat16)
    along_j = (((0,), (0,)), ((), ()))
    outs = []
    for left_rows, own_rows, right_rows in near_pieces:
        if outs:
            left_rows, right_rows, outs = lax.optimization_barrier((left_rows, right_rows, outs))
        aligned = lax.dot_general(plan[1], own_rows, along_j, preferred_element_type=jnp.float32)
        aligned = aligned + lax.dot_general(plan[0], left_rows, along_j, preferred_element_type=jnp.float32)
        aligned = aligned + lax.dot_general(plan[2], right_rows, along_j, preferred_element_type=jnp.float32)
        outs.append(aligned.astype(jnp.bfloat16))
    return jnp.concatenate(outs, 1)


def body_banded(
    student_hidden, teacher_hidden, student_proj, teacher_proj, student_chars, teacher_chars, band
):
    block_rows = student_hidden.shape[0]
    proj_width = student_proj.shape[1]
    s_part = jnp.dot(student_hidden, student_proj, preferred_element_type=jnp.float32)
    t_part = jnp.dot(teacher_hidden, teacher_proj, preferred_element_type=jnp.float32)
    s_feat, t_feat = lax.psum((s_part, t_part), "tgrp")
    s_unit = unit_rows(s_feat)
    t_unit = unit_rows(t_feat)
    left_rows, left_unit, left_chars = shifted((teacher_hidden, t_unit, teacher_chars), "seq", 1)
    right_rows, right_unit, right_chars = shifted(
        (teacher_hidden, t_unit, teacher_chars), "seq", -1
    )
    near_unit = jnp.stack([left_unit, t_unit, right_unit])
    near_pos = jnp.stack([left_chars, teacher_chars, right_chars]).astype(jnp.float32)
    s_pos = student_chars.astype(jnp.float32)
    flags = band[0]
    slot_mask = jnp.stack([flags[0], jnp.ones((), jnp.int32), flags[1]]).astype(jnp.float32)
    scores = jnp.einsum(
        "ip,kjp->kij", s_unit, near_unit, preferred_element_type=jnp.float32
    ) / math.sqrt(proj_width)
    distance = jnp.abs(s_pos[None, :, None] - near_pos[:, None, :]) / (4.0 * block_rows)
    kernel = jnp.exp(scores - distance) * slot_mask[:, None, None]
    row_scale = jnp.ones((block_rows,), jnp.float32)
    col_scale = jnp.zeros((3, block_rows), jnp.float32)
    for iteration in range(ITERS):
        partial_cols = jnp.sum(row_scale[None, :, None] * kernel, axis=1)
        left_one = shifted(partial_cols[1:], "seq", 1)
        left_two = shifted(partial_cols[2:], "seq", 2)
        right_one = shifted(partial_cols[:2], "seq", -1)
        right_two = shifted(partial_cols[:1], "seq", -2)
        column_total = jnp.stack(
            [
                left_two[0] + left_one[0] + partial_cols[0],
                left_one[1] + partial_cols[1] + right_one[0],
                partial_cols[2] + right_one[1] + right_two[0],
            ]
        )
        col_scale = slot_mask[:, None] / jnp.where(slot_mask[:, None] > 0.0, column_total, 1.0)
        row_scale = 1.0 / jnp.sum(kernel * col_scale[:, None, :], axis=(0, 2))
    plan = (row_scale[None, :, None] * kernel * col_scale[:, None, :]).astype(jnp.bfloat16)
    aligned = jnp.dot(plan[0], left_rows, preferred_element_type=jnp.float32)
    aligned = aligned + jnp.dot(plan[1], teacher_hidden, preferred_element_type=jnp.float32)
    aligned = aligned + jnp.dot(plan[2], right_rows, preferred_element_type=jnp.float32)
    return aligned.astype(jnp.bfloat16)


def solution(mesh):
    blocks = mesh.shape["seq"]

    def body(*args):
        rows = args[0].shape[0]
        if blocks * 3 * rows * rows * 4 <= LOCAL_KERNEL_BYTES:
            return body_local(*args)
        return body_banded(*args)

    return jax.shard_map(
        body,
        mesh=mesh,
        in_specs=(
            P(("groups", "seq"), "tgrp"),
            P(("groups", "seq"), "tgrp"),
            P("tgrp", None),
            P("tgrp", None),
            P(("groups", "seq")),
            P(("groups", "seq")),
            P(("groups", "seq"), None),
        ),
        out_specs=P(("groups", "seq"), "tgrp"),
        check_vma=False,
    )
```

```python
import math

import jax
import jax.numpy as jnp
from jax import lax
from jax.sharding import PartitionSpec as P

ITERS = 4

LOCAL_KERNEL_BYTES = 24 * 2**20

norm_eps = 1e-05


def shifted(block, axis, distance):
    devices = range(lax.axis_size(axis))
    route = [(i - distance, i) for i in devices if i - distance in devices]
    return lax.ppermute(block, axis, route)


def unit_rows(features):
    factor = lax.rsqrt(jnp.mean(features * features, axis=-1, keepdims=True) + norm_eps)
    return (features * factor).astype(jnp.bfloat16)


def beside(values):
    zero_row = jnp.zeros_like(values[:1])
    from_left = jnp.concatenate([zero_row, values[:-1]], 0)
    from_right = jnp.concatenate([values[1:], zero_row], 0)
    return jnp.stack([from_left, values, from_right], 1)


def tgrp_sum(value):
    if lax.axis_size("tgrp") == 2:
        return value + lax.ppermute(value, "tgrp", [(0, 1), (1, 0)])
    return lax.psum(value, "tgrp")


def gather_seq(block):
    n = lax.axis_size("seq")
    if n % 2:
        return lax.all_gather(block, "seq")
    me = lax.axis_index("seq")
    pairs = n // 2
    partner = lax.ppermute(block, "seq", [(i, i ^ 1) for i in range(n)])
    odd = me % 2 == 1
    pair = jnp.stack([jnp.where(odd, partner, block), jnp.where(odd, block, partner)])
    by_offset = [pair]
    for d in range(1, pairs):
        by_offset = [shifted(pair, "seq", 2 * d)] + by_offset + [shifted(pair, "seq", -2 * d)]
    window = lax.dynamic_slice_in_dim(jnp.stack(by_offset), pairs - 1 - me // 2, pairs, 0)
    return window.reshape((n,) + block.shape)


def gather_halves(packed):
    if lax.axis_size("tgrp") != 2:
        return lax.all_gather(packed, "seq")
    half = packed.shape[1] // 2
    core = lax.axis_index("tgrp")
    mine = lax.dynamic_slice_in_dim(packed, core * half, half, 1)
    got = gather_seq(mine)
    theirs = lax.ppermute(got, "tgrp", [(0, 1), (1, 0)])
    first = jnp.where(core == 0, got, theirs)
    second = jnp.where(core == 0, theirs, got)
    return jnp.concatenate([first, second], 2)


def body_local(
    student_hidden, teacher_hidden, student_proj, teacher_proj, student_chars, teacher_chars, band
):
    rows = student_hidden.shape[0]
    proj_width = student_proj.shape[1]
    blocks = lax.axis_size("seq")
    me = lax.axis_index("seq")

    s_part = jnp.dot(student_hidden, student_proj, preferred_element_type=jnp.float32)
    t_part = jnp.dot(teacher_hidden, teacher_proj, preferred_element_type=jnp.float32)
    feats = tgrp_sum(jnp.concatenate([s_part, t_part], 1))
    units = jnp.concatenate(
        [unit_rows(feats[:, :proj_width]), unit_rows(feats[:, proj_width:])], 1
    )
    digits = jnp.stack([student_chars, teacher_chars])
    digits = jnp.stack([digits // 4096, digits // 64 % 64, digits % 64], 1)
    digit_rows = digits.reshape(-1, units.shape[1]).astype(jnp.bfloat16)
    flag_row = jnp.zeros((1, units.shape[1]), jnp.bfloat16).at[0, :2].set(band[0].astype(jnp.bfloat16))
    extra = jnp.concatenate([digit_rows, flag_row], 0)
    pad = -(rows + extra.shape[0]) % 16
    packed = jnp.concatenate([units, extra, jnp.zeros((pad, units.shape[1]), jnp.bfloat16)], 0)
    gathered = gather_halves(packed)

    teacher_rows, gathered = lax.optimization_barrier((teacher_hidden, gathered))
    left_rows = shifted(teacher_rows, "seq", 1)
    right_rows = shifted(teacher_rows, "seq", -1)

    s_unit = gathered[:, :rows, :proj_width]
    t_unit = gathered[:, :rows, proj_width:]
    got = gathered[:, rows : rows + digit_rows.shape[0]].astype(jnp.float32).reshape(blocks, 2, 3, rows)
    chars = got[:, :, 0] * 4096.0 + got[:, :, 1] * 64.0 + got[:, :, 2]
    s_pos = chars[:, 0]
    t_pos = beside(chars[:, 1])
    flags = gathered[:, rows + digit_rows.shape[0]].astype(jnp.float32)
    ones_col = jnp.ones((blocks,), jnp.float32)
    slot_mask = jnp.stack([flags[:, 0], ones_col, flags[:, 1]], 1)
    scores = jnp.einsum(
        "bkjp,bip->bkji", beside(t_unit), s_unit, preferred_element_type=jnp.float32
    ) / math.sqrt(proj_width)
    distance = jnp.abs(s_pos[:, None, None, :] - t_pos[:, :, :, None]) / (4.0 * rows)
    kernel = jnp.exp(scores - distance) * slot_mask[:, :, None, None]

    def iterate(iteration, scales):
        row_scale, col_scale = scales
        partial_cols = jnp.sum(row_scale[:, None, None, :] * kernel, axis=3)
        zero_row = jnp.zeros_like(partial_cols[:1, 0])
        column_total = (
            partial_cols[:, 1]
            + jnp.concatenate([zero_row, partial_cols[:-1, 2]], 0)
            + jnp.concatenate([partial_cols[1:, 0], zero_row], 0)
        )
        col_scale = beside(1.0 / column_total)
        row_scale = 1.0 / jnp.sum(kernel * col_scale[:, :, :, None], axis=(1, 2))
        return row_scale, col_scale

    row_scale, col_scale = lax.fori_loop(
        0,
        ITERS,
        iterate,
        (jnp.ones((blocks, rows), jnp.float32), jnp.zeros((blocks, 3, rows), jnp.float32)),
    )
    own_kernel = lax.dynamic_index_in_dim(kernel, me, 0, keepdims=False)
    own_row = lax.dynamic_index_in_dim(row_scale, me, 0, keepdims=False)
    own_col = lax.dynamic_index_in_dim(col_scale, me, 0, keepdims=False)
    plan = (own_row[None, None, :] * own_kernel * own_col[:, :, None]).astype(jnp.bfloat16)
    along_j = (((0,), (0,)), ((), ()))
    aligned = lax.dot_general(plan[1], teacher_hidden, along_j, preferred_element_type=jnp.float32)
    aligned = aligned + lax.dot_general(plan[0], left_rows, along_j, preferred_element_type=jnp.float32)
    aligned = aligned + lax.dot_general(plan[2], right_rows, along_j, preferred_element_type=jnp.float32)
    return aligned.astype(jnp.bfloat16)


def body_banded(
    student_hidden, teacher_hidden, student_proj, teacher_proj, student_chars, teacher_chars, band
):
    block_rows = student_hidden.shape[0]
    proj_width = student_proj.shape[1]
    s_part = jnp.dot(student_hidden, student_proj, preferred_element_type=jnp.float32)
    t_part = jnp.dot(teacher_hidden, teacher_proj, preferred_element_type=jnp.float32)
    s_feat, t_feat = lax.psum((s_part, t_part), "tgrp")
    s_unit = unit_rows(s_feat)
    t_unit = unit_rows(t_feat)
    left_rows, left_unit, left_chars = shifted((teacher_hidden, t_unit, teacher_chars), "seq", 1)
    right_rows, right_unit, right_chars = shifted(
        (teacher_hidden, t_unit, teacher_chars), "seq", -1
    )
    near_unit = jnp.stack([left_unit, t_unit, right_unit])
    near_pos = jnp.stack([left_chars, teacher_chars, right_chars]).astype(jnp.float32)
    s_pos = student_chars.astype(jnp.float32)
    flags = band[0]
    slot_mask = jnp.stack([flags[0], jnp.ones((), jnp.int32), flags[1]]).astype(jnp.float32)
    scores = jnp.einsum(
        "ip,kjp->kij", s_unit, near_unit, preferred_element_type=jnp.float32
    ) / math.sqrt(proj_width)
    distance = jnp.abs(s_pos[None, :, None] - near_pos[:, None, :]) / (4.0 * block_rows)
    kernel = jnp.exp(scores - distance) * slot_mask[:, None, None]
    row_scale = jnp.ones((block_rows,), jnp.float32)
    col_scale = jnp.zeros((3, block_rows), jnp.float32)
    for iteration in range(ITERS):
        partial_cols = jnp.sum(row_scale[None, :, None] * kernel, axis=1)
        left_one = shifted(partial_cols[1:], "seq", 1)
        left_two = shifted(partial_cols[2:], "seq", 2)
        right_one = shifted(partial_cols[:2], "seq", -1)
        right_two = shifted(partial_cols[:1], "seq", -2)
        column_total = jnp.stack(
            [
                left_two[0] + left_one[0] + partial_cols[0],
                left_one[1] + partial_cols[1] + right_one[0],
                partial_cols[2] + right_one[1] + right_two[0],
            ]
        )
        col_scale = slot_mask[:, None] / jnp.where(slot_mask[:, None] > 0.0, column_total, 1.0)
        row_scale = 1.0 / jnp.sum(kernel * col_scale[:, None, :], axis=(0, 2))
    plan = (row_scale[None, :, None] * kernel * col_scale[:, None, :]).astype(jnp.bfloat16)
    aligned = jnp.dot(plan[0], left_rows, preferred_element_type=jnp.float32)
    aligned = aligned + jnp.dot(plan[1], teacher_hidden, preferred_element_type=jnp.float32)
    aligned = aligned + jnp.dot(plan[2], right_rows, preferred_element_type=jnp.float32)
    return aligned.astype(jnp.bfloat16)


def solution(mesh):
    blocks = mesh.shape["seq"]

    def body(*args):
        rows = args[0].shape[0]
        if blocks * 3 * rows * rows * 4 <= LOCAL_KERNEL_BYTES:
            return body_local(*args)
        return body_banded(*args)

    return jax.shard_map(
        body,
        mesh=mesh,
        in_specs=(
            P(("groups", "seq"), "tgrp"),
            P(("groups", "seq"), "tgrp"),
            P("tgrp", None),
            P("tgrp", None),
            P(("groups", "seq")),
            P(("groups", "seq")),
            P(("groups", "seq"), None),
        ),
        out_specs=P(("groups", "seq"), "tgrp"),
        check_vma=False,
    )
```

```python
import math

import jax
import jax.numpy as jnp
from jax import lax
from jax.experimental import pallas as pl
from jax.sharding import PartitionSpec as P

ITERS = 4

LOCAL_KERNEL_BYTES = 24 * 2**20

norm_eps = 1e-05


def shifted(block, axis, distance):
    devices = range(lax.axis_size(axis))
    route = [(i - distance, i) for i in devices if i - distance in devices]
    return lax.ppermute(block, axis, route)


def unit_rows(features):
    factor = lax.rsqrt(jnp.mean(features * features, axis=-1, keepdims=True) + norm_eps)
    return (features * factor).astype(jnp.bfloat16)


def beside(values):
    zero_row = jnp.zeros_like(values[:1])
    from_left = jnp.concatenate([zero_row, values[:-1]], 0)
    from_right = jnp.concatenate([values[1:], zero_row], 0)
    return jnp.stack([from_left, values, from_right], 1)


def tgrp_sum(value):
    if lax.axis_size("tgrp") == 2:
        return value + lax.ppermute(value, "tgrp", [(0, 1), (1, 0)])
    return lax.psum(value, "tgrp")


def gather_seq(block):
    n = lax.axis_size("seq")
    if n % 2:
        return lax.all_gather(block, "seq")
    me = lax.axis_index("seq")
    pairs = n // 2
    partner = lax.ppermute(block, "seq", [(i, i ^ 1) for i in range(n)])
    odd = me % 2 == 1
    pair = jnp.stack([jnp.where(odd, partner, block), jnp.where(odd, block, partner)])
    by_offset = [pair]
    for d in range(1, pairs):
        by_offset = [shifted(pair, "seq", 2 * d)] + by_offset + [shifted(pair, "seq", -2 * d)]
    window = lax.dynamic_slice_in_dim(jnp.stack(by_offset), pairs - 1 - me // 2, pairs, 0)
    return window.reshape((n,) + block.shape)


def gather_halves(packed):
    if lax.axis_size("tgrp") != 2:
        return lax.all_gather(packed, "seq")
    half = packed.shape[1] // 2
    core = lax.axis_index("tgrp")
    mine = lax.dynamic_slice_in_dim(packed, core * half, half, 1)
    got = gather_seq(mine)
    theirs = lax.ppermute(got, "tgrp", [(0, 1), (1, 0)])
    first = jnp.where(core == 0, got, theirs)
    second = jnp.where(core == 0, theirs, got)
    return jnp.concatenate([first, second], 2)


def body_local(
    student_hidden, teacher_hidden, student_proj, teacher_proj, student_chars, teacher_chars, band
):
    rows = student_hidden.shape[0]
    proj_width = student_proj.shape[1]
    blocks = lax.axis_size("seq")
    me = lax.axis_index("seq")

    s_part = jnp.dot(student_hidden, student_proj, preferred_element_type=jnp.float32)
    t_part = jnp.dot(teacher_hidden, teacher_proj, preferred_element_type=jnp.float32)
    feats = tgrp_sum(jnp.concatenate([s_part, t_part], 1))
    units = jnp.concatenate(
        [unit_rows(feats[:, :proj_width]), unit_rows(feats[:, proj_width:])], 1
    )
    digits = jnp.stack([student_chars, teacher_chars])
    digits = jnp.stack([digits // 4096, digits // 64 % 64, digits % 64], 1)
    digit_rows = digits.reshape(-1, units.shape[1]).astype(jnp.bfloat16)
    flag_row = jnp.zeros((1, units.shape[1]), jnp.bfloat16).at[0, :2].set(band[0].astype(jnp.bfloat16))
    extra = jnp.concatenate([digit_rows, flag_row], 0)
    pad = -(rows + extra.shape[0]) % 16
    packed = jnp.concatenate([units, extra, jnp.zeros((pad, units.shape[1]), jnp.bfloat16)], 0)
    gathered = gather_halves(packed)

    teacher_rows, gathered = lax.optimization_barrier((teacher_hidden, gathered))
    left_rows = shifted(teacher_rows, "seq", 1)
    right_rows = shifted(teacher_rows, "seq", -1)

    s_unit = gathered[:, :rows, :proj_width]
    t_unit = gathered[:, :rows, proj_width:]
    got = gathered[:, rows : rows + digit_rows.shape[0]].astype(jnp.float32).reshape(blocks, 2, 3, rows)
    chars = got[:, :, 0] * 4096.0 + got[:, :, 1] * 64.0 + got[:, :, 2]
    s_pos = chars[:, 0]
    t_pos = beside(chars[:, 1])
    flags = gathered[:, rows + digit_rows.shape[0]].astype(jnp.float32)
    ones_col = jnp.ones((blocks,), jnp.float32)
    slot_mask = jnp.stack([flags[:, 0], ones_col, flags[:, 1]], 1)
    scores = jnp.einsum(
        "bkjp,bip->bkji", beside(t_unit), s_unit, preferred_element_type=jnp.float32
    ) / math.sqrt(proj_width)
    distance = jnp.abs(s_pos[:, None, None, :] - t_pos[:, :, :, None]) / (4.0 * rows)
    kernel = jnp.exp(scores - distance) * slot_mask[:, :, None, None]

    def iterate(iteration, scales):
        row_scale, col_scale = scales
        partial_cols = jnp.sum(row_scale[:, None, None, :] * kernel, axis=3)
        zero_row = jnp.zeros_like(partial_cols[:1, 0])
        column_total = (
            partial_cols[:, 1]
            + jnp.concatenate([zero_row, partial_cols[:-1, 2]], 0)
            + jnp.concatenate([partial_cols[1:, 0], zero_row], 0)
        )
        col_scale = beside(1.0 / column_total)
        row_scale = 1.0 / jnp.sum(kernel * col_scale[:, :, :, None], axis=(1, 2))
        return row_scale, col_scale

    row_scale, col_scale = lax.fori_loop(
        0,
        ITERS,
        iterate,
        (jnp.ones((blocks, rows), jnp.float32), jnp.zeros((blocks, 3, rows), jnp.float32)),
    )
    own_kernel = lax.dynamic_index_in_dim(kernel, me, 0, keepdims=False)
    own_row = lax.dynamic_index_in_dim(row_scale, me, 0, keepdims=False)
    own_col = lax.dynamic_index_in_dim(col_scale, me, 0, keepdims=False)
    plan = (own_row[None, None, :] * own_kernel * own_col[:, :, None]).astype(jnp.bfloat16)
    along_j = (((0,), (0,)), ((), ()))
    center = lax.dot_general(plan[1], teacher_hidden, along_j, preferred_element_type=jnp.float32)
    sides = jnp.swapaxes(plan[::2], 1, 2)
    return neighbour_products(sides, left_rows, right_rows, center)


def neighbour_kernel(sides_ref, left_ref, right_ref, center_ref, out_ref):
    total = center_ref[...]
    total = total + jnp.dot(sides_ref[0], left_ref[...], preferred_element_type=jnp.float32)
    total = total + jnp.dot(sides_ref[1], right_ref[...], preferred_element_type=jnp.float32)
    out_ref[...] = total.astype(out_ref.dtype)


def neighbour_products(sides, left_rows, right_rows, center):
    rows, width = center.shape
    depth = left_rows.shape[0]
    tile = 512 if width % 512 == 0 else width
    column = pl.BlockSpec((depth, tile), lambda c: (0, c))
    return pl.pallas_call(
        neighbour_kernel,
        grid=(width // tile,),
        in_specs=[
            pl.BlockSpec((2, rows, depth), lambda c: (0, 0, 0)),
            column,
            column,
            pl.BlockSpec((rows, tile), lambda c: (0, c)),
        ],
        out_specs=pl.BlockSpec((rows, tile), lambda c: (0, c)),
        out_shape=jax.ShapeDtypeStruct((rows, width), jnp.bfloat16),
        cost_estimate=pl.CostEstimate(
            flops=4 * rows * depth * width,
            bytes_accessed=2 * rows * depth * 2 + 2 * depth * width * 2 + rows * width * 6,
            transcendentals=0,
        ),
    )(sides, left_rows, right_rows, center)


def body_banded(
    student_hidden, teacher_hidden, student_proj, teacher_proj, student_chars, teacher_chars, band
):
    block_rows = student_hidden.shape[0]
    proj_width = student_proj.shape[1]
    s_part = jnp.dot(student_hidden, student_proj, preferred_element_type=jnp.float32)
    t_part = jnp.dot(teacher_hidden, teacher_proj, preferred_element_type=jnp.float32)
    s_feat, t_feat = lax.psum((s_part, t_part), "tgrp")
    s_unit = unit_rows(s_feat)
    t_unit = unit_rows(t_feat)
    left_rows, left_unit, left_chars = shifted((teacher_hidden, t_unit, teacher_chars), "seq", 1)
    right_rows, right_unit, right_chars = shifted(
        (teacher_hidden, t_unit, teacher_chars), "seq", -1
    )
    near_unit = jnp.stack([left_unit, t_unit, right_unit])
    near_pos = jnp.stack([left_chars, teacher_chars, right_chars]).astype(jnp.float32)
    s_pos = student_chars.astype(jnp.float32)
    flags = band[0]
    slot_mask = jnp.stack([flags[0], jnp.ones((), jnp.int32), flags[1]]).astype(jnp.float32)
    scores = jnp.einsum(
        "ip,kjp->kij", s_unit, near_unit, preferred_element_type=jnp.float32
    ) / math.sqrt(proj_width)
    distance = jnp.abs(s_pos[None, :, None] - near_pos[:, None, :]) / (4.0 * block_rows)
    kernel = jnp.exp(scores - distance) * slot_mask[:, None, None]
    row_scale = jnp.ones((block_rows,), jnp.float32)
    col_scale = jnp.zeros((3, block_rows), jnp.float32)
    for iteration in range(ITERS):
        partial_cols = jnp.sum(row_scale[None, :, None] * kernel, axis=1)
        left_one = shifted(partial_cols[1:], "seq", 1)
        left_two = shifted(partial_cols[2:], "seq", 2)
        right_one = shifted(partial_cols[:2], "seq", -1)
        right_two = shifted(partial_cols[:1], "seq", -2)
        column_total = jnp.stack(
            [
                left_two[0] + left_one[0] + partial_cols[0],
                left_one[1] + partial_cols[1] + right_one[0],
                partial_cols[2] + right_one[1] + right_two[0],
            ]
        )
        col_scale = slot_mask[:, None] / jnp.where(slot_mask[:, None] > 0.0, column_total, 1.0)
        row_scale = 1.0 / jnp.sum(kernel * col_scale[:, None, :], axis=(0, 2))
    plan = (row_scale[None, :, None] * kernel * col_scale[:, None, :]).astype(jnp.bfloat16)
    aligned = jnp.dot(plan[0], left_rows, preferred_element_type=jnp.float32)
    aligned = aligned + jnp.dot(plan[1], teacher_hidden, preferred_element_type=jnp.float32)
    aligned = aligned + jnp.dot(plan[2], right_rows, preferred_element_type=jnp.float32)
    return aligned.astype(jnp.bfloat16)


def solution(mesh):
    blocks = mesh.shape["seq"]

    def body(*args):
        rows = args[0].shape[0]
        if blocks * 3 * rows * rows * 4 <= LOCAL_KERNEL_BYTES:
            return body_local(*args)
        return body_banded(*args)

    return jax.shard_map(
        body,
        mesh=mesh,
        in_specs=(
            P(("groups", "seq"), "tgrp"),
            P(("groups", "seq"), "tgrp"),
            P("tgrp", None),
            P("tgrp", None),
            P(("groups", "seq")),
            P(("groups", "seq")),
            P(("groups", "seq"), None),
        ),
        out_specs=P(("groups", "seq"), "tgrp"),
        check_vma=False,
    )
```

```python
import math

import jax
import jax.numpy as jnp
from jax import lax
from jax.sharding import PartitionSpec as P

ITERS = 4

LOCAL_KERNEL_BYTES = 24 * 2**20

norm_eps = 1e-05


def shifted(block, axis, distance):
    devices = range(lax.axis_size(axis))
    route = [(i - distance, i) for i in devices if i - distance in devices]
    return lax.ppermute(block, axis, route)


def unit_rows(features):
    factor = lax.rsqrt(jnp.mean(features * features, axis=-1, keepdims=True) + norm_eps)
    return (features * factor).astype(jnp.bfloat16)


def beside(values):
    zero_row = jnp.zeros_like(values[:1])
    from_left = jnp.concatenate([zero_row, values[:-1]], 0)
    from_right = jnp.concatenate([values[1:], zero_row], 0)
    return jnp.stack([from_left, values, from_right], 1)


def tgrp_sum(value):
    if lax.axis_size("tgrp") == 2:
        return value + lax.ppermute(value, "tgrp", [(0, 1), (1, 0)])
    return lax.psum(value, "tgrp")


def gather_seq(block):
    n = lax.axis_size("seq")
    if n % 2:
        return lax.all_gather(block, "seq")
    me = lax.axis_index("seq")
    pairs = n // 2
    partner = lax.ppermute(block, "seq", [(i, i ^ 1) for i in range(n)])
    odd = me % 2 == 1
    pair = jnp.stack([jnp.where(odd, partner, block), jnp.where(odd, block, partner)])
    by_offset = [pair]
    for d in range(1, pairs):
        by_offset = [shifted(pair, "seq", 2 * d)] + by_offset + [shifted(pair, "seq", -2 * d)]
    window = lax.dynamic_slice_in_dim(jnp.stack(by_offset), pairs - 1 - me // 2, pairs, 0)
    return window.reshape((n,) + block.shape)


def gather_halves(packed):
    if lax.axis_size("tgrp") != 2:
        return lax.all_gather(packed, "seq")
    half = packed.shape[1] // 2
    core = lax.axis_index("tgrp")
    mine = lax.dynamic_slice_in_dim(packed, core * half, half, 1)
    n = lax.axis_size("seq")
    got = lax.all_to_all(jnp.broadcast_to(mine, (n,) + mine.shape), "seq", 0, 0, tiled=False)
    theirs = lax.ppermute(got, "tgrp", [(0, 1), (1, 0)])
    first = jnp.where(core == 0, got, theirs)
    second = jnp.where(core == 0, theirs, got)
    return jnp.concatenate([first, second], 2)


def body_local(
    student_hidden, teacher_hidden, student_proj, teacher_proj, student_chars, teacher_chars, band
):
    rows = student_hidden.shape[0]
    proj_width = student_proj.shape[1]
    blocks = lax.axis_size("seq")
    me = lax.axis_index("seq")

    s_part = jnp.dot(student_hidden, student_proj, preferred_element_type=jnp.float32)
    t_part = jnp.dot(teacher_hidden, teacher_proj, preferred_element_type=jnp.float32)
    feats = tgrp_sum(jnp.concatenate([s_part, t_part], 1))
    units = jnp.concatenate(
        [unit_rows(feats[:, :proj_width]), unit_rows(feats[:, proj_width:])], 1
    )
    digits = jnp.stack([student_chars, teacher_chars])
    digits = jnp.stack([digits // 4096, digits // 64 % 64, digits % 64], 1)
    digit_rows = digits.reshape(-1, units.shape[1]).astype(jnp.bfloat16)
    flag_row = jnp.zeros((1, units.shape[1]), jnp.bfloat16).at[0, :2].set(band[0].astype(jnp.bfloat16))
    extra = jnp.concatenate([digit_rows, flag_row], 0)
    pad = -(rows + extra.shape[0]) % 16
    packed = jnp.concatenate([units, extra, jnp.zeros((pad, units.shape[1]), jnp.bfloat16)], 0)
    gathered = gather_halves(packed)

    teacher_rows, gathered = lax.optimization_barrier((teacher_hidden, gathered))
    left_rows = shifted(teacher_rows, "seq", 1)
    right_rows = shifted(teacher_rows, "seq", -1)

    s_unit = gathered[:, :rows, :proj_width]
    t_unit = gathered[:, :rows, proj_width:]
    got = gathered[:, rows : rows + digit_rows.shape[0]].astype(jnp.float32).reshape(blocks, 2, 3, rows)
    chars = got[:, :, 0] * 4096.0 + got[:, :, 1] * 64.0 + got[:, :, 2]
    s_pos = chars[:, 0]
    t_pos = beside(chars[:, 1])
    flags = gathered[:, rows + digit_rows.shape[0]].astype(jnp.float32)
    ones_col = jnp.ones((blocks,), jnp.float32)
    slot_mask = jnp.stack([flags[:, 0], ones_col, flags[:, 1]], 1)
    scores = jnp.einsum(
        "bkjp,bip->bkji", beside(t_unit), s_unit, preferred_element_type=jnp.float32
    ) / math.sqrt(proj_width)
    distance = jnp.abs(s_pos[:, None, None, :] - t_pos[:, :, :, None]) / (4.0 * rows)
    kernel = jnp.exp(scores - distance) * slot_mask[:, :, None, None]

    def iterate(iteration, scales):
        row_scale, col_scale = scales
        partial_cols = jnp.sum(row_scale[:, None, None, :] * kernel, axis=3)
        zero_row = jnp.zeros_like(partial_cols[:1, 0])
        column_total = (
            partial_cols[:, 1]
            + jnp.concatenate([zero_row, partial_cols[:-1, 2]], 0)
            + jnp.concatenate([partial_cols[1:, 0], zero_row], 0)
        )
        col_scale = beside(1.0 / column_total)
        row_scale = 1.0 / jnp.sum(kernel * col_scale[:, :, :, None], axis=(1, 2))
        return row_scale, col_scale

    row_scale, col_scale = lax.fori_loop(
        0,
        ITERS,
        iterate,
        (jnp.ones((blocks, rows), jnp.float32), jnp.zeros((blocks, 3, rows), jnp.float32)),
    )
    own_kernel = lax.dynamic_index_in_dim(kernel, me, 0, keepdims=False)
    own_row = lax.dynamic_index_in_dim(row_scale, me, 0, keepdims=False)
    own_col = lax.dynamic_index_in_dim(col_scale, me, 0, keepdims=False)
    plan = (own_row[None, None, :] * own_kernel * own_col[:, :, None]).astype(jnp.bfloat16)
    along_j = (((0,), (0,)), ((), ()))
    aligned = lax.dot_general(plan[1], teacher_hidden, along_j, preferred_element_type=jnp.float32)
    aligned = aligned + lax.dot_general(plan[0], left_rows, along_j, preferred_element_type=jnp.float32)
    aligned = aligned + lax.dot_general(plan[2], right_rows, along_j, preferred_element_type=jnp.float32)
    return aligned.astype(jnp.bfloat16)


def body_banded(
    student_hidden, teacher_hidden, student_proj, teacher_proj, student_chars, teacher_chars, band
):
    block_rows = student_hidden.shape[0]
    proj_width = student_proj.shape[1]
    s_part = jnp.dot(student_hidden, student_proj, preferred_element_type=jnp.float32)
    t_part = jnp.dot(teacher_hidden, teacher_proj, preferred_element_type=jnp.float32)
    s_feat, t_feat = lax.psum((s_part, t_part), "tgrp")
    s_unit = unit_rows(s_feat)
    t_unit = unit_rows(t_feat)
    left_rows, left_unit, left_chars = shifted((teacher_hidden, t_unit, teacher_chars), "seq", 1)
    right_rows, right_unit, right_chars = shifted(
        (teacher_hidden, t_unit, teacher_chars), "seq", -1
    )
    near_unit = jnp.stack([left_unit, t_unit, right_unit])
    near_pos = jnp.stack([left_chars, teacher_chars, right_chars]).astype(jnp.float32)
    s_pos = student_chars.astype(jnp.float32)
    flags = band[0]
    slot_mask = jnp.stack([flags[0], jnp.ones((), jnp.int32), flags[1]]).astype(jnp.float32)
    scores = jnp.einsum(
        "ip,kjp->kij", s_unit, near_unit, preferred_element_type=jnp.float32
    ) / math.sqrt(proj_width)
    distance = jnp.abs(s_pos[None, :, None] - near_pos[:, None, :]) / (4.0 * block_rows)
    kernel = jnp.exp(scores - distance) * slot_mask[:, None, None]
    row_scale = jnp.ones((block_rows,), jnp.float32)
    col_scale = jnp.zeros((3, block_rows), jnp.float32)
    for iteration in range(ITERS):
        partial_cols = jnp.sum(row_scale[None, :, None] * kernel, axis=1)
        left_one = shifted(partial_cols[1:], "seq", 1)
        left_two = shifted(partial_cols[2:], "seq", 2)
        right_one = shifted(partial_cols[:2], "seq", -1)
        right_two = shifted(partial_cols[:1], "seq", -2)
        column_total = jnp.stack(
            [
                left_two[0] + left_one[0] + partial_cols[0],
                left_one[1] + partial_cols[1] + right_one[0],
                partial_cols[2] + right_one[1] + right_two[0],
            ]
        )
        col_scale = slot_mask[:, None] / jnp.where(slot_mask[:, None] > 0.0, column_total, 1.0)
        row_scale = 1.0 / jnp.sum(kernel * col_scale[:, None, :], axis=(0, 2))
    plan = (row_scale[None, :, None] * kernel * col_scale[:, None, :]).astype(jnp.bfloat16)
    aligned = jnp.dot(plan[0], left_rows, preferred_element_type=jnp.float32)
    aligned = aligned + jnp.dot(plan[1], teacher_hidden, preferred_element_type=jnp.float32)
    aligned = aligned + jnp.dot(plan[2], right_rows, preferred_element_type=jnp.float32)
    return aligned.astype(jnp.bfloat16)


def solution(mesh):
    blocks = mesh.shape["seq"]

    def body(*args):
        rows = args[0].shape[0]
        if blocks * 3 * rows * rows * 4 <= LOCAL_KERNEL_BYTES:
            return body_local(*args)
        return body_banded(*args)

    return jax.shard_map(
        body,
        mesh=mesh,
        in_specs=(
            P(("groups", "seq"), "tgrp"),
            P(("groups", "seq"), "tgrp"),
            P("tgrp", None),
            P("tgrp", None),
            P(("groups", "seq")),
            P(("groups", "seq")),
            P(("groups", "seq"), None),
        ),
        out_specs=P(("groups", "seq"), "tgrp"),
        check_vma=False,
    )
```

```python
import math

import jax
import jax.numpy as jnp
from jax import lax
from jax.sharding import PartitionSpec as P

ITERS = 4

LOCAL_KERNEL_BYTES = 24 * 2**20

norm_eps = 1e-05


def shifted(block, axis, distance):
    devices = range(lax.axis_size(axis))
    route = [(i - distance, i) for i in devices if i - distance in devices]
    return lax.ppermute(block, axis, route)


def unit_rows(features):
    factor = lax.rsqrt(jnp.mean(features * features, axis=-1, keepdims=True) + norm_eps)
    return (features * factor).astype(jnp.bfloat16)


def beside(values):
    zero_row = jnp.zeros_like(values[:1])
    from_left = jnp.concatenate([zero_row, values[:-1]], 0)
    from_right = jnp.concatenate([values[1:], zero_row], 0)
    return jnp.stack([from_left, values, from_right], 1)


def tgrp_sum(value):
    if lax.axis_size("tgrp") == 2:
        return value + lax.ppermute(value, "tgrp", [(0, 1), (1, 0)])
    return lax.psum(value, "tgrp")


def gather_seq(block):
    n = lax.axis_size("seq")
    if n % 2:
        return lax.all_gather(block, "seq")
    me = lax.axis_index("seq")
    pairs = n // 2
    partner = lax.ppermute(block, "seq", [(i, i ^ 1) for i in range(n)])
    odd = me % 2 == 1
    pair = jnp.stack([jnp.where(odd, partner, block), jnp.where(odd, block, partner)])
    by_offset = [pair]
    for d in range(1, pairs):
        by_offset = [shifted(pair, "seq", 2 * d)] + by_offset + [shifted(pair, "seq", -2 * d)]
    window = lax.dynamic_slice_in_dim(jnp.stack(by_offset), pairs - 1 - me // 2, pairs, 0)
    return window.reshape((n,) + block.shape)


def gather_halves(packed):
    if lax.axis_size("tgrp") != 2:
        return lax.all_gather(packed, "seq")
    half = packed.shape[1] // 2
    core = lax.axis_index("tgrp")
    mine = lax.dynamic_slice_in_dim(packed, core * half, half, 1)
    n = lax.axis_size("seq")
    got = lax.all_to_all(jnp.broadcast_to(mine, (n,) + mine.shape), "seq", 0, 0, tiled=False)
    theirs = lax.ppermute(got, "tgrp", [(0, 1), (1, 0)])
    first = jnp.where(core == 0, got, theirs)
    second = jnp.where(core == 0, theirs, got)
    return jnp.concatenate([first, second], 2)


def body_local(
    student_hidden, teacher_hidden, student_proj, teacher_proj, student_chars, teacher_chars, band
):
    rows = student_hidden.shape[0]
    proj_width = student_proj.shape[1]
    blocks = lax.axis_size("seq")
    me = lax.axis_index("seq")

    s_part = jnp.dot(student_hidden, student_proj, preferred_element_type=jnp.float32)
    t_part = jnp.dot(teacher_hidden, teacher_proj, preferred_element_type=jnp.float32)
    feats = tgrp_sum(jnp.concatenate([s_part, t_part], 1))
    units = jnp.concatenate(
        [unit_rows(feats[:, :proj_width]), unit_rows(feats[:, proj_width:])], 1
    )
    digits = jnp.stack([student_chars, teacher_chars])
    digits = jnp.stack([digits // 4096, digits // 64 % 64, digits % 64], 1)
    digit_rows = digits.reshape(-1, units.shape[1]).astype(jnp.bfloat16)
    flag_row = jnp.zeros((1, units.shape[1]), jnp.bfloat16).at[0, :2].set(band[0].astype(jnp.bfloat16))
    extra = jnp.concatenate([digit_rows, flag_row], 0)
    pad = -(rows + extra.shape[0]) % 16
    packed = jnp.concatenate([units, extra, jnp.zeros((pad, units.shape[1]), jnp.bfloat16)], 0)
    gathered = gather_halves(packed)

    left_rows = shifted(teacher_hidden, "seq", 1)
    right_rows = shifted(teacher_hidden, "seq", -1)

    s_unit = gathered[:, :rows, :proj_width]
    t_unit = gathered[:, :rows, proj_width:]
    got = gathered[:, rows : rows + digit_rows.shape[0]].astype(jnp.float32).reshape(blocks, 2, 3, rows)
    chars = got[:, :, 0] * 4096.0 + got[:, :, 1] * 64.0 + got[:, :, 2]
    s_pos = chars[:, 0]
    t_pos = beside(chars[:, 1])
    flags = gathered[:, rows + digit_rows.shape[0]].astype(jnp.float32)
    ones_col = jnp.ones((blocks,), jnp.float32)
    slot_mask = jnp.stack([flags[:, 0], ones_col, flags[:, 1]], 1)
    scores = jnp.einsum(
        "bkjp,bip->bkji", beside(t_unit), s_unit, preferred_element_type=jnp.float32
    ) / math.sqrt(proj_width)
    distance = jnp.abs(s_pos[:, None, None, :] - t_pos[:, :, :, None]) / (4.0 * rows)
    kernel = jnp.exp(scores - distance) * slot_mask[:, :, None, None]

    def iterate(iteration, scales):
        row_scale, col_scale = scales
        partial_cols = jnp.sum(row_scale[:, None, None, :] * kernel, axis=3)
        zero_row = jnp.zeros_like(partial_cols[:1, 0])
        column_total = (
            partial_cols[:, 1]
            + jnp.concatenate([zero_row, partial_cols[:-1, 2]], 0)
            + jnp.concatenate([partial_cols[1:, 0], zero_row], 0)
        )
        col_scale = beside(1.0 / column_total)
        row_scale = 1.0 / jnp.sum(kernel * col_scale[:, :, :, None], axis=(1, 2))
        return row_scale, col_scale

    row_scale, col_scale = lax.fori_loop(
        0,
        ITERS,
        iterate,
        (jnp.ones((blocks, rows), jnp.float32), jnp.zeros((blocks, 3, rows), jnp.float32)),
    )
    own_kernel = lax.dynamic_index_in_dim(kernel, me, 0, keepdims=False)
    own_row = lax.dynamic_index_in_dim(row_scale, me, 0, keepdims=False)
    own_col = lax.dynamic_index_in_dim(col_scale, me, 0, keepdims=False)
    plan = (own_row[None, None, :] * own_kernel * own_col[:, :, None]).astype(jnp.bfloat16)
    along_j = (((0,), (0,)), ((), ()))
    aligned = lax.dot_general(plan[1], teacher_hidden, along_j, preferred_element_type=jnp.float32)
    aligned = aligned + lax.dot_general(plan[0], left_rows, along_j, preferred_element_type=jnp.float32)
    aligned = aligned + lax.dot_general(plan[2], right_rows, along_j, preferred_element_type=jnp.float32)
    return aligned.astype(jnp.bfloat16)


def body_banded(
    student_hidden, teacher_hidden, student_proj, teacher_proj, student_chars, teacher_chars, band
):
    block_rows = student_hidden.shape[0]
    proj_width = student_proj.shape[1]
    s_part = jnp.dot(student_hidden, student_proj, preferred_element_type=jnp.float32)
    t_part = jnp.dot(teacher_hidden, teacher_proj, preferred_element_type=jnp.float32)
    s_feat, t_feat = lax.psum((s_part, t_part), "tgrp")
    s_unit = unit_rows(s_feat)
    t_unit = unit_rows(t_feat)
    left_rows, left_unit, left_chars = shifted((teacher_hidden, t_unit, teacher_chars), "seq", 1)
    right_rows, right_unit, right_chars = shifted(
        (teacher_hidden, t_unit, teacher_chars), "seq", -1
    )
    near_unit = jnp.stack([left_unit, t_unit, right_unit])
    near_pos = jnp.stack([left_chars, teacher_chars, right_chars]).astype(jnp.float32)
    s_pos = student_chars.astype(jnp.float32)
    flags = band[0]
    slot_mask = jnp.stack([flags[0], jnp.ones((), jnp.int32), flags[1]]).astype(jnp.float32)
    scores = jnp.einsum(
        "ip,kjp->kij", s_unit, near_unit, preferred_element_type=jnp.float32
    ) / math.sqrt(proj_width)
    distance = jnp.abs(s_pos[None, :, None] - near_pos[:, None, :]) / (4.0 * block_rows)
    kernel = jnp.exp(scores - distance) * slot_mask[:, None, None]
    row_scale = jnp.ones((block_rows,), jnp.float32)
    col_scale = jnp.zeros((3, block_rows), jnp.float32)
    for iteration in range(ITERS):
        partial_cols = jnp.sum(row_scale[None, :, None] * kernel, axis=1)
        left_one = shifted(partial_cols[1:], "seq", 1)
        left_two = shifted(partial_cols[2:], "seq", 2)
        right_one = shifted(partial_cols[:2], "seq", -1)
        right_two = shifted(partial_cols[:1], "seq", -2)
        column_total = jnp.stack(
            [
                left_two[0] + left_one[0] + partial_cols[0],
                left_one[1] + partial_cols[1] + right_one[0],
                partial_cols[2] + right_one[1] + right_two[0],
            ]
        )
        col_scale = slot_mask[:, None] / jnp.where(slot_mask[:, None] > 0.0, column_total, 1.0)
        row_scale = 1.0 / jnp.sum(kernel * col_scale[:, None, :], axis=(0, 2))
    plan = (row_scale[None, :, None] * kernel * col_scale[:, None, :]).astype(jnp.bfloat16)
    aligned = jnp.dot(plan[0], left_rows, preferred_element_type=jnp.float32)
    aligned = aligned + jnp.dot(plan[1], teacher_hidden, preferred_element_type=jnp.float32)
    aligned = aligned + jnp.dot(plan[2], right_rows, preferred_element_type=jnp.float32)
    return aligned.astype(jnp.bfloat16)


def solution(mesh):
    blocks = mesh.shape["seq"]

    def body(*args):
        rows = args[0].shape[0]
        if blocks * 3 * rows * rows * 4 <= LOCAL_KERNEL_BYTES:
            return body_local(*args)
        return body_banded(*args)

    return jax.shard_map(
        body,
        mesh=mesh,
        in_specs=(
            P(("groups", "seq"), "tgrp"),
            P(("groups", "seq"), "tgrp"),
            P("tgrp", None),
            P("tgrp", None),
            P(("groups", "seq")),
            P(("groups", "seq")),
            P(("groups", "seq"), None),
        ),
        out_specs=P(("groups", "seq"), "tgrp"),
        check_vma=False,
    )
```

```python
import math

import jax
import jax.numpy as jnp
from jax import lax
from jax.sharding import PartitionSpec as P

ITERS = 4

LOCAL_KERNEL_BYTES = 24 * 2**20

norm_eps = 1e-05


def shifted(block, axis, distance):
    devices = range(lax.axis_size(axis))
    route = [(i - distance, i) for i in devices if i - distance in devices]
    return lax.ppermute(block, axis, route)


def unit_rows(features):
    factor = lax.rsqrt(jnp.mean(features * features, axis=-1, keepdims=True) + norm_eps)
    return (features * factor).astype(jnp.bfloat16)


def beside(values):
    zero_row = jnp.zeros_like(values[:1])
    from_left = jnp.concatenate([zero_row, values[:-1]], 0)
    from_right = jnp.concatenate([values[1:], zero_row], 0)
    return jnp.stack([from_left, values, from_right], 1)


def tgrp_sum(value):
    if lax.axis_size("tgrp") == 2:
        return value + lax.ppermute(value, "tgrp", [(0, 1), (1, 0)])
    return lax.psum(value, "tgrp")


def gather_seq(block):
    n = lax.axis_size("seq")
    if n % 2:
        return lax.all_gather(block, "seq")
    me = lax.axis_index("seq")
    pairs = n // 2
    partner = lax.ppermute(block, "seq", [(i, i ^ 1) for i in range(n)])
    odd = me % 2 == 1
    pair = jnp.stack([jnp.where(odd, partner, block), jnp.where(odd, block, partner)])
    by_offset = [pair]
    for d in range(1, pairs):
        by_offset = [shifted(pair, "seq", 2 * d)] + by_offset + [shifted(pair, "seq", -2 * d)]
    window = lax.dynamic_slice_in_dim(jnp.stack(by_offset), pairs - 1 - me // 2, pairs, 0)
    return window.reshape((n,) + block.shape)


def gather_halves(packed):
    if lax.axis_size("tgrp") != 2:
        return lax.all_gather(packed, "seq")
    half = packed.shape[1] // 2
    core = lax.axis_index("tgrp")
    mine = lax.dynamic_slice_in_dim(packed, core * half, half, 1)
    n = lax.axis_size("seq")
    got = lax.all_to_all(jnp.broadcast_to(mine, (n,) + mine.shape), "seq", 0, 0, tiled=False)
    theirs = lax.ppermute(got, "tgrp", [(0, 1), (1, 0)])
    first = jnp.where(core == 0, got, theirs)
    second = jnp.where(core == 0, theirs, got)
    return jnp.concatenate([first, second], 2)


def body_local(
    student_hidden, teacher_hidden, student_proj, teacher_proj, student_chars, teacher_chars, band
):
    rows = student_hidden.shape[0]
    proj_width = student_proj.shape[1]
    blocks = lax.axis_size("seq")
    me = lax.axis_index("seq")

    s_part = jnp.dot(student_hidden, student_proj, preferred_element_type=jnp.float32)
    t_part = jnp.dot(teacher_hidden, teacher_proj, preferred_element_type=jnp.float32)
    feats = tgrp_sum(jnp.concatenate([s_part, t_part], 1))
    units = jnp.concatenate(
        [unit_rows(feats[:, :proj_width]), unit_rows(feats[:, proj_width:])], 1
    )
    digits = jnp.stack([student_chars, teacher_chars])
    digits = jnp.stack([digits // 4096, digits // 64 % 64, digits % 64], 1)
    digit_rows = digits.reshape(-1, units.shape[1]).astype(jnp.bfloat16)
    flag_row = jnp.zeros((1, units.shape[1]), jnp.bfloat16).at[0, :2].set(band[0].astype(jnp.bfloat16))
    extra = jnp.concatenate([digit_rows, flag_row], 0)
    pad = -(rows + extra.shape[0]) % 16
    packed = jnp.concatenate([units, extra, jnp.zeros((pad, units.shape[1]), jnp.bfloat16)], 0)
    gathered = gather_halves(packed)

    left_rows = shifted(teacher_hidden, "seq", 1)
    right_rows = shifted(teacher_hidden, "seq", -1)

    s_unit = gathered[:, :rows, :proj_width]
    t_unit = gathered[:, :rows, proj_width:]
    got = gathered[:, rows : rows + digit_rows.shape[0]].astype(jnp.float32).reshape(blocks, 2, 3, rows)
    chars = got[:, :, 0] * 4096.0 + got[:, :, 1] * 64.0 + got[:, :, 2]
    s_pos = chars[:, 0]
    t_pos = beside(chars[:, 1])
    flags = gathered[:, rows + digit_rows.shape[0]].astype(jnp.float32)
    ones_col = jnp.ones((blocks,), jnp.float32)
    slot_mask = jnp.stack([flags[:, 0], ones_col, flags[:, 1]], 1)
    scores = jnp.einsum(
        "bkjp,bip->bkji", beside(t_unit), s_unit, preferred_element_type=jnp.float32
    ) / math.sqrt(proj_width)
    distance = jnp.abs(s_pos[:, None, None, :] - t_pos[:, :, :, None]) / (4.0 * rows)
    kernel = jnp.exp(scores - distance) * slot_mask[:, :, None, None]

    def iterate(iteration, scales):
        row_scale, col_scale = scales
        partial_cols = jnp.sum(row_scale[:, None, None, :] * kernel, axis=3)
        zero_row = jnp.zeros_like(partial_cols[:1, 0])
        column_total = (
            partial_cols[:, 1]
            + jnp.concatenate([zero_row, partial_cols[:-1, 2]], 0)
            + jnp.concatenate([partial_cols[1:, 0], zero_row], 0)
        )
        col_scale = beside(1.0 / column_total)
        row_scale = 1.0 / jnp.sum(kernel * col_scale[:, :, :, None], axis=(1, 2))
        return row_scale, col_scale

    row_scale, col_scale = lax.fori_loop(
        0,
        ITERS,
        iterate,
        (jnp.ones((blocks, rows), jnp.float32), jnp.zeros((blocks, 3, rows), jnp.float32)),
    )
    own_kernel = lax.dynamic_index_in_dim(kernel, me, 0, keepdims=False)
    own_row = lax.dynamic_index_in_dim(row_scale, me, 0, keepdims=False)
    own_col = lax.dynamic_index_in_dim(col_scale, me, 0, keepdims=False)
    plan = (own_row[None, None, :] * own_kernel * own_col[:, :, None]).astype(jnp.bfloat16)
    along_j = (((0,), (0,)), ((), ()))
    aligned = lax.dot_general(plan[1], teacher_hidden, along_j, preferred_element_type=jnp.float32)
    sides = jnp.concatenate([plan[0], plan[2]], 0)
    near_rows = jnp.concatenate([left_rows, right_rows], 0)
    aligned = aligned + lax.dot_general(sides, near_rows, along_j, preferred_element_type=jnp.float32)
    return aligned.astype(jnp.bfloat16)


def body_banded(
    student_hidden, teacher_hidden, student_proj, teacher_proj, student_chars, teacher_chars, band
):
    block_rows = student_hidden.shape[0]
    proj_width = student_proj.shape[1]
    s_part = jnp.dot(student_hidden, student_proj, preferred_element_type=jnp.float32)
    t_part = jnp.dot(teacher_hidden, teacher_proj, preferred_element_type=jnp.float32)
    s_feat, t_feat = lax.psum((s_part, t_part), "tgrp")
    s_unit = unit_rows(s_feat)
    t_unit = unit_rows(t_feat)
    left_rows, left_unit, left_chars = shifted((teacher_hidden, t_unit, teacher_chars), "seq", 1)
    right_rows, right_unit, right_chars = shifted(
        (teacher_hidden, t_unit, teacher_chars), "seq", -1
    )
    near_unit = jnp.stack([left_unit, t_unit, right_unit])
    near_pos = jnp.stack([left_chars, teacher_chars, right_chars]).astype(jnp.float32)
    s_pos = student_chars.astype(jnp.float32)
    flags = band[0]
    slot_mask = jnp.stack([flags[0], jnp.ones((), jnp.int32), flags[1]]).astype(jnp.float32)
    scores = jnp.einsum(
        "ip,kjp->kij", s_unit, near_unit, preferred_element_type=jnp.float32
    ) / math.sqrt(proj_width)
    distance = jnp.abs(s_pos[None, :, None] - near_pos[:, None, :]) / (4.0 * block_rows)
    kernel = jnp.exp(scores - distance) * slot_mask[:, None, None]
    row_scale = jnp.ones((block_rows,), jnp.float32)
    col_scale = jnp.zeros((3, block_rows), jnp.float32)
    for iteration in range(ITERS):
        partial_cols = jnp.sum(row_scale[None, :, None] * kernel, axis=1)
        left_one = shifted(partial_cols[1:], "seq", 1)
        left_two = shifted(partial_cols[2:], "seq", 2)
        right_one = shifted(partial_cols[:2], "seq", -1)
        right_two = shifted(partial_cols[:1], "seq", -2)
        column_total = jnp.stack(
            [
                left_two[0] + left_one[0] + partial_cols[0],
                left_one[1] + partial_cols[1] + right_one[0],
                partial_cols[2] + right_one[1] + right_two[0],
            ]
        )
        col_scale = slot_mask[:, None] / jnp.where(slot_mask[:, None] > 0.0, column_total, 1.0)
        row_scale = 1.0 / jnp.sum(kernel * col_scale[:, None, :], axis=(0, 2))
    plan = (row_scale[None, :, None] * kernel * col_scale[:, None, :]).astype(jnp.bfloat16)
    aligned = jnp.dot(plan[0], left_rows, preferred_element_type=jnp.float32)
    aligned = aligned + jnp.dot(plan[1], teacher_hidden, preferred_element_type=jnp.float32)
    aligned = aligned + jnp.dot(plan[2], right_rows, preferred_element_type=jnp.float32)
    return aligned.astype(jnp.bfloat16)


def solution(mesh):
    blocks = mesh.shape["seq"]

    def body(*args):
        rows = args[0].shape[0]
        if blocks * 3 * rows * rows * 4 <= LOCAL_KERNEL_BYTES:
            return body_local(*args)
        return body_banded(*args)

    return jax.shard_map(
        body,
        mesh=mesh,
        in_specs=(
            P(("groups", "seq"), "tgrp"),
            P(("groups", "seq"), "tgrp"),
            P("tgrp", None),
            P("tgrp", None),
            P(("groups", "seq")),
            P(("groups", "seq")),
            P(("groups", "seq"), None),
        ),
        out_specs=P(("groups", "seq"), "tgrp"),
        check_vma=False,
    )
```

```python
import math

import jax
import jax.numpy as jnp
from jax import lax
from jax.sharding import PartitionSpec as P

ITERS = 4

LOCAL_KERNEL_BYTES = 24 * 2**20

norm_eps = 1e-05


def shifted(block, axis, distance):
    devices = range(lax.axis_size(axis))
    route = [(i - distance, i) for i in devices if i - distance in devices]
    return lax.ppermute(block, axis, route)


def unit_rows(features):
    factor = lax.rsqrt(jnp.mean(features * features, axis=-1, keepdims=True) + norm_eps)
    return (features * factor).astype(jnp.bfloat16)


def beside(values):
    zero_row = jnp.zeros_like(values[:1])
    from_left = jnp.concatenate([zero_row, values[:-1]], 0)
    from_right = jnp.concatenate([values[1:], zero_row], 0)
    return jnp.stack([from_left, values, from_right], 1)


def tgrp_sum(value):
    if lax.axis_size("tgrp") == 2:
        return value + lax.ppermute(value, "tgrp", [(0, 1), (1, 0)])
    return lax.psum(value, "tgrp")


def gather_seq(block):
    n = lax.axis_size("seq")
    if n % 2:
        return lax.all_gather(block, "seq")
    me = lax.axis_index("seq")
    pairs = n // 2
    partner = lax.ppermute(block, "seq", [(i, i ^ 1) for i in range(n)])
    odd = me % 2 == 1
    pair = jnp.stack([jnp.where(odd, partner, block), jnp.where(odd, block, partner)])
    by_offset = [pair]
    for d in range(1, pairs):
        by_offset = [shifted(pair, "seq", 2 * d)] + by_offset + [shifted(pair, "seq", -2 * d)]
    window = lax.dynamic_slice_in_dim(jnp.stack(by_offset), pairs - 1 - me // 2, pairs, 0)
    return window.reshape((n,) + block.shape)


def gather_halves(packed):
    if lax.axis_size("tgrp") != 2:
        return lax.all_gather(packed, "seq")
    half = packed.shape[1] // 2
    core = lax.axis_index("tgrp")
    mine = lax.dynamic_slice_in_dim(packed, core * half, half, 1)
    n = lax.axis_size("seq")
    got = lax.all_to_all(jnp.broadcast_to(mine, (n,) + mine.shape), "seq", 0, 0, tiled=False)
    theirs = lax.ppermute(got, "tgrp", [(0, 1), (1, 0)])
    first = jnp.where(core == 0, got, theirs)
    second = jnp.where(core == 0, theirs, got)
    return jnp.concatenate([first, second], 2)


def body_local(
    student_hidden, teacher_hidden, student_proj, teacher_proj, student_chars, teacher_chars, band
):
    rows = student_hidden.shape[0]
    proj_width = student_proj.shape[1]
    blocks = lax.axis_size("seq")
    me = lax.axis_index("seq")

    s_part = jnp.dot(student_hidden, student_proj, preferred_element_type=jnp.float32)
    t_part = jnp.dot(teacher_hidden, teacher_proj, preferred_element_type=jnp.float32)
    feats = tgrp_sum(jnp.concatenate([s_part, t_part], 1))
    units = jnp.concatenate(
        [unit_rows(feats[:, :proj_width]), unit_rows(feats[:, proj_width:])], 1
    )
    digits = jnp.stack([student_chars, teacher_chars])
    digits = jnp.stack([digits // 4096, digits // 64 % 64, digits % 64], 1)
    digit_rows = digits.reshape(-1, units.shape[1]).astype(jnp.bfloat16)
    flag_row = jnp.zeros((1, units.shape[1]), jnp.bfloat16).at[0, :2].set(band[0].astype(jnp.bfloat16))
    extra = jnp.concatenate([digit_rows, flag_row], 0)
    pad = -(rows + extra.shape[0]) % 16
    packed = jnp.concatenate([units, extra, jnp.zeros((pad, units.shape[1]), jnp.bfloat16)], 0)
    gathered = gather_halves(packed)

    pieces = 2 if rows % 16 == 0 else 1
    cut = rows // pieces
    near_pieces = [
        (shifted(teacher_hidden[p * cut : (p + 1) * cut], "seq", 1),
         shifted(teacher_hidden[p * cut : (p + 1) * cut], "seq", -1))
        for p in range(pieces)
    ]

    s_unit = gathered[:, :rows, :proj_width]
    t_unit = gathered[:, :rows, proj_width:]
    got = gathered[:, rows : rows + digit_rows.shape[0]].astype(jnp.float32).reshape(blocks, 2, 3, rows)
    chars = got[:, :, 0] * 4096.0 + got[:, :, 1] * 64.0 + got[:, :, 2]
    s_pos = chars[:, 0]
    t_pos = beside(chars[:, 1])
    flags = gathered[:, rows + digit_rows.shape[0]].astype(jnp.float32)
    ones_col = jnp.ones((blocks,), jnp.float32)
    slot_mask = jnp.stack([flags[:, 0], ones_col, flags[:, 1]], 1)
    scores = jnp.einsum(
        "bkjp,bip->bkji", beside(t_unit), s_unit, preferred_element_type=jnp.float32
    ) / math.sqrt(proj_width)
    distance = jnp.abs(s_pos[:, None, None, :] - t_pos[:, :, :, None]) / (4.0 * rows)
    kernel = jnp.exp(scores - distance) * slot_mask[:, :, None, None]

    def iterate(iteration, scales):
        row_scale, col_scale = scales
        partial_cols = jnp.sum(row_scale[:, None, None, :] * kernel, axis=3)
        zero_row = jnp.zeros_like(partial_cols[:1, 0])
        column_total = (
            partial_cols[:, 1]
            + jnp.concatenate([zero_row, partial_cols[:-1, 2]], 0)
            + jnp.concatenate([partial_cols[1:, 0], zero_row], 0)
        )
        col_scale = beside(1.0 / column_total)
        row_scale = 1.0 / jnp.sum(kernel * col_scale[:, :, :, None], axis=(1, 2))
        return row_scale, col_scale

    row_scale, col_scale = lax.fori_loop(
        0,
        ITERS,
        iterate,
        (jnp.ones((blocks, rows), jnp.float32), jnp.zeros((blocks, 3, rows), jnp.float32)),
    )
    own_kernel = lax.dynamic_index_in_dim(kernel, me, 0, keepdims=False)
    own_row = lax.dynamic_index_in_dim(row_scale, me, 0, keepdims=False)
    own_col = lax.dynamic_index_in_dim(col_scale, me, 0, keepdims=False)
    plan = (own_row[None, None, :] * own_kernel * own_col[:, :, None]).astype(jnp.bfloat16)
    along_j = (((0,), (0,)), ((), ()))
    aligned = lax.dot_general(plan[1], teacher_hidden, along_j, preferred_element_type=jnp.float32)
    for p, (left_rows, right_rows) in enumerate(near_pieces):
        if p:
            left_rows, right_rows, aligned = lax.optimization_barrier((left_rows, right_rows, aligned))
        sides = jnp.concatenate([plan[0, p * cut : (p + 1) * cut], plan[2, p * cut : (p + 1) * cut]], 0)
        near_rows = jnp.concatenate([left_rows, right_rows], 0)
        aligned = aligned + lax.dot_general(sides, near_rows, along_j, preferred_element_type=jnp.float32)
    return aligned.astype(jnp.bfloat16)


def body_banded(
    student_hidden, teacher_hidden, student_proj, teacher_proj, student_chars, teacher_chars, band
):
    block_rows = student_hidden.shape[0]
    proj_width = student_proj.shape[1]
    s_part = jnp.dot(student_hidden, student_proj, preferred_element_type=jnp.float32)
    t_part = jnp.dot(teacher_hidden, teacher_proj, preferred_element_type=jnp.float32)
    s_feat, t_feat = lax.psum((s_part, t_part), "tgrp")
    s_unit = unit_rows(s_feat)
    t_unit = unit_rows(t_feat)
    left_rows, left_unit, left_chars = shifted((teacher_hidden, t_unit, teacher_chars), "seq", 1)
    right_rows, right_unit, right_chars = shifted(
        (teacher_hidden, t_unit, teacher_chars), "seq", -1
    )
    near_unit = jnp.stack([left_unit, t_unit, right_unit])
    near_pos = jnp.stack([left_chars, teacher_chars, right_chars]).astype(jnp.float32)
    s_pos = student_chars.astype(jnp.float32)
    flags = band[0]
    slot_mask = jnp.stack([flags[0], jnp.ones((), jnp.int32), flags[1]]).astype(jnp.float32)
    scores = jnp.einsum(
        "ip,kjp->kij", s_unit, near_unit, preferred_element_type=jnp.float32
    ) / math.sqrt(proj_width)
    distance = jnp.abs(s_pos[None, :, None] - near_pos[:, None, :]) / (4.0 * block_rows)
    kernel = jnp.exp(scores - distance) * slot_mask[:, None, None]
    row_scale = jnp.ones((block_rows,), jnp.float32)
    col_scale = jnp.zeros((3, block_rows), jnp.float32)
    for iteration in range(ITERS):
        partial_cols = jnp.sum(row_scale[None, :, None] * kernel, axis=1)
        left_one = shifted(partial_cols[1:], "seq", 1)
        left_two = shifted(partial_cols[2:], "seq", 2)
        right_one = shifted(partial_cols[:2], "seq", -1)
        right_two = shifted(partial_cols[:1], "seq", -2)
        column_total = jnp.stack(
            [
                left_two[0] + left_one[0] + partial_cols[0],
                left_one[1] + partial_cols[1] + right_one[0],
                partial_cols[2] + right_one[1] + right_two[0],
            ]
        )
        col_scale = slot_mask[:, None] / jnp.where(slot_mask[:, None] > 0.0, column_total, 1.0)
        row_scale = 1.0 / jnp.sum(kernel * col_scale[:, None, :], axis=(0, 2))
    plan = (row_scale[None, :, None] * kernel * col_scale[:, None, :]).astype(jnp.bfloat16)
    aligned = jnp.dot(plan[0], left_rows, preferred_element_type=jnp.float32)
    aligned = aligned + jnp.dot(plan[1], teacher_hidden, preferred_element_type=jnp.float32)
    aligned = aligned + jnp.dot(plan[2], right_rows, preferred_element_type=jnp.float32)
    return aligned.astype(jnp.bfloat16)


def solution(mesh):
    blocks = mesh.shape["seq"]

    def body(*args):
        rows = args[0].shape[0]
        if blocks * 3 * rows * rows * 4 <= LOCAL_KERNEL_BYTES:
            return body_local(*args)
        return body_banded(*args)

    return jax.shard_map(
        body,
        mesh=mesh,
        in_specs=(
            P(("groups", "seq"), "tgrp"),
            P(("groups", "seq"), "tgrp"),
            P("tgrp", None),
            P("tgrp", None),
            P(("groups", "seq")),
            P(("groups", "seq")),
            P(("groups", "seq"), None),
        ),
        out_specs=P(("groups", "seq"), "tgrp"),
        check_vma=False,
    )
```

```python
import math

import jax
import jax.numpy as jnp
from jax import lax
from jax.sharding import PartitionSpec as P

ITERS = 4

LOCAL_KERNEL_BYTES = 24 * 2**20

norm_eps = 1e-05


def shifted(block, axis, distance):
    devices = range(lax.axis_size(axis))
    route = [(i - distance, i) for i in devices if i - distance in devices]
    return lax.ppermute(block, axis, route)


def unit_rows(features):
    factor = lax.rsqrt(jnp.mean(features * features, axis=-1, keepdims=True) + norm_eps)
    return (features * factor).astype(jnp.bfloat16)


def beside(values):
    zero_row = jnp.zeros_like(values[:1])
    from_left = jnp.concatenate([zero_row, values[:-1]], 0)
    from_right = jnp.concatenate([values[1:], zero_row], 0)
    return jnp.stack([from_left, values, from_right], 1)


def tgrp_sum(value):
    if lax.axis_size("tgrp") == 2:
        return value + lax.ppermute(value, "tgrp", [(0, 1), (1, 0)])
    return lax.psum(value, "tgrp")


def gather_seq(block):
    n = lax.axis_size("seq")
    if n % 2:
        return lax.all_gather(block, "seq")
    me = lax.axis_index("seq")
    pairs = n // 2
    partner = lax.ppermute(block, "seq", [(i, i ^ 1) for i in range(n)])
    odd = me % 2 == 1
    pair = jnp.stack([jnp.where(odd, partner, block), jnp.where(odd, block, partner)])
    by_offset = [pair]
    for d in range(1, pairs):
        by_offset = [shifted(pair, "seq", 2 * d)] + by_offset + [shifted(pair, "seq", -2 * d)]
    window = lax.dynamic_slice_in_dim(jnp.stack(by_offset), pairs - 1 - me // 2, pairs, 0)
    return window.reshape((n,) + block.shape)


def gather_halves(packed):
    if lax.axis_size("tgrp") != 2:
        return lax.all_gather(packed, "seq")
    half = packed.shape[1] // 2
    core = lax.axis_index("tgrp")
    mine = lax.dynamic_slice_in_dim(packed, core * half, half, 1)
    n = lax.axis_size("seq")
    got = lax.all_to_all(jnp.broadcast_to(mine, (n,) + mine.shape), "seq", 0, 0, tiled=False)
    theirs = lax.ppermute(got, "tgrp", [(0, 1), (1, 0)])
    first = jnp.where(core == 0, got, theirs)
    second = jnp.where(core == 0, theirs, got)
    return jnp.concatenate([first, second], 2)


def body_local(
    student_hidden, teacher_hidden, student_proj, teacher_proj, student_chars, teacher_chars, band
):
    rows = student_hidden.shape[0]
    proj_width = student_proj.shape[1]
    blocks = lax.axis_size("seq")
    me = lax.axis_index("seq")

    s_part = jnp.dot(student_hidden, student_proj, preferred_element_type=jnp.float32)
    t_part = jnp.dot(teacher_hidden, teacher_proj, preferred_element_type=jnp.float32)
    feats = tgrp_sum(jnp.concatenate([s_part, t_part], 1))
    units = jnp.concatenate(
        [unit_rows(feats[:, :proj_width]), unit_rows(feats[:, proj_width:])], 1
    )
    digits = jnp.stack([student_chars, teacher_chars])
    digits = jnp.stack([digits // 4096, digits // 64 % 64, digits % 64], 1)
    digit_rows = digits.reshape(-1, units.shape[1]).astype(jnp.bfloat16)
    flag_row = jnp.zeros((1, units.shape[1]), jnp.bfloat16).at[0, :2].set(band[0].astype(jnp.bfloat16))
    extra = jnp.concatenate([digit_rows, flag_row], 0)
    pad = -(rows + extra.shape[0]) % 16
    packed = jnp.concatenate([units, extra, jnp.zeros((pad, units.shape[1]), jnp.bfloat16)], 0)
    gathered = gather_halves(packed)

    left_rows = shifted(teacher_hidden, "seq", 1)
    second_rows, left_rows = lax.optimization_barrier((teacher_hidden, left_rows))
    right_rows = shifted(second_rows, "seq", -1)

    s_unit = gathered[:, :rows, :proj_width]
    t_unit = gathered[:, :rows, proj_width:]
    got = gathered[:, rows : rows + digit_rows.shape[0]].astype(jnp.float32).reshape(blocks, 2, 3, rows)
    chars = got[:, :, 0] * 4096.0 + got[:, :, 1] * 64.0 + got[:, :, 2]
    s_pos = chars[:, 0]
    t_pos = beside(chars[:, 1])
    flags = gathered[:, rows + digit_rows.shape[0]].astype(jnp.float32)
    ones_col = jnp.ones((blocks,), jnp.float32)
    slot_mask = jnp.stack([flags[:, 0], ones_col, flags[:, 1]], 1)
    scores = jnp.einsum(
        "bkjp,bip->bkji", beside(t_unit), s_unit, preferred_element_type=jnp.float32
    ) / math.sqrt(proj_width)
    distance = jnp.abs(s_pos[:, None, None, :] - t_pos[:, :, :, None]) / (4.0 * rows)
    kernel = jnp.exp(scores - distance) * slot_mask[:, :, None, None]

    def iterate(iteration, scales):
        row_scale, col_scale = scales
        partial_cols = jnp.sum(row_scale[:, None, None, :] * kernel, axis=3)
        zero_row = jnp.zeros_like(partial_cols[:1, 0])
        column_total = (
            partial_cols[:, 1]
            + jnp.concatenate([zero_row, partial_cols[:-1, 2]], 0)
            + jnp.concatenate([partial_cols[1:, 0], zero_row], 0)
        )
        col_scale = beside(1.0 / column_total)
        row_scale = 1.0 / jnp.sum(kernel * col_scale[:, :, :, None], axis=(1, 2))
        return row_scale, col_scale

    row_scale, col_scale = lax.fori_loop(
        0,
        ITERS,
        iterate,
        (jnp.ones((blocks, rows), jnp.float32), jnp.zeros((blocks, 3, rows), jnp.float32)),
    )
    own_kernel = lax.dynamic_index_in_dim(kernel, me, 0, keepdims=False)
    own_row = lax.dynamic_index_in_dim(row_scale, me, 0, keepdims=False)
    own_col = lax.dynamic_index_in_dim(col_scale, me, 0, keepdims=False)
    plan = (own_row[None, None, :] * own_kernel * own_col[:, :, None]).astype(jnp.bfloat16)
    along_j = (((0,), (0,)), ((), ()))
    aligned = lax.dot_general(plan[1], teacher_hidden, along_j, preferred_element_type=jnp.float32)
    aligned = aligned + lax.dot_general(plan[0], left_rows, along_j, preferred_element_type=jnp.float32)
    aligned = aligned + lax.dot_general(plan[2], right_rows, along_j, preferred_element_type=jnp.float32)
    return aligned.astype(jnp.bfloat16)


def body_banded(
    student_hidden, teacher_hidden, student_proj, teacher_proj, student_chars, teacher_chars, band
):
    block_rows = student_hidden.shape[0]
    proj_width = student_proj.shape[1]
    s_part = jnp.dot(student_hidden, student_proj, preferred_element_type=jnp.float32)
    t_part = jnp.dot(teacher_hidden, teacher_proj, preferred_element_type=jnp.float32)
    s_feat, t_feat = lax.psum((s_part, t_part), "tgrp")
    s_unit = unit_rows(s_feat)
    t_unit = unit_rows(t_feat)
    left_rows, left_unit, left_chars = shifted((teacher_hidden, t_unit, teacher_chars), "seq", 1)
    right_rows, right_unit, right_chars = shifted(
        (teacher_hidden, t_unit, teacher_chars), "seq", -1
    )
    near_unit = jnp.stack([left_unit, t_unit, right_unit])
    near_pos = jnp.stack([left_chars, teacher_chars, right_chars]).astype(jnp.float32)
    s_pos = student_chars.astype(jnp.float32)
    flags = band[0]
    slot_mask = jnp.stack([flags[0], jnp.ones((), jnp.int32), flags[1]]).astype(jnp.float32)
    scores = jnp.einsum(
        "ip,kjp->kij", s_unit, near_unit, preferred_element_type=jnp.float32
    ) / math.sqrt(proj_width)
    distance = jnp.abs(s_pos[None, :, None] - near_pos[:, None, :]) / (4.0 * block_rows)
    kernel = jnp.exp(scores - distance) * slot_mask[:, None, None]
    row_scale = jnp.ones((block_rows,), jnp.float32)
    col_scale = jnp.zeros((3, block_rows), jnp.float32)
    for iteration in range(ITERS):
        partial_cols = jnp.sum(row_scale[None, :, None] * kernel, axis=1)
        left_one = shifted(partial_cols[1:], "seq", 1)
        left_two = shifted(partial_cols[2:], "seq", 2)
        right_one = shifted(partial_cols[:2], "seq", -1)
        right_two = shifted(partial_cols[:1], "seq", -2)
        column_total = jnp.stack(
            [
                left_two[0] + left_one[0] + partial_cols[0],
                left_one[1] + partial_cols[1] + right_one[0],
                partial_cols[2] + right_one[1] + right_two[0],
            ]
        )
        col_scale = slot_mask[:, None] / jnp.where(slot_mask[:, None] > 0.0, column_total, 1.0)
        row_scale = 1.0 / jnp.sum(kernel * col_scale[:, None, :], axis=(0, 2))
    plan = (row_scale[None, :, None] * kernel * col_scale[:, None, :]).astype(jnp.bfloat16)
    aligned = jnp.dot(plan[0], left_rows, preferred_element_type=jnp.float32)
    aligned = aligned + jnp.dot(plan[1], teacher_hidden, preferred_element_type=jnp.float32)
    aligned = aligned + jnp.dot(plan[2], right_rows, preferred_element_type=jnp.float32)
    return aligned.astype(jnp.bfloat16)


def solution(mesh):
    blocks = mesh.shape["seq"]

    def body(*args):
        rows = args[0].shape[0]
        if blocks * 3 * rows * rows * 4 <= LOCAL_KERNEL_BYTES:
            return body_local(*args)
        return body_banded(*args)

    return jax.shard_map(
        body,
        mesh=mesh,
        in_specs=(
            P(("groups", "seq"), "tgrp"),
            P(("groups", "seq"), "tgrp"),
            P("tgrp", None),
            P("tgrp", None),
            P(("groups", "seq")),
            P(("groups", "seq")),
            P(("groups", "seq"), None),
        ),
        out_specs=P(("groups", "seq"), "tgrp"),
        check_vma=False,
    )
```

```python
import math

import jax
import jax.numpy as jnp
from jax import lax
from jax.sharding import PartitionSpec as P

ITERS = 4

LOCAL_KERNEL_BYTES = 24 * 2**20

norm_eps = 1e-05


def shifted(block, axis, distance):
    devices = range(lax.axis_size(axis))
    route = [(i - distance, i) for i in devices if i - distance in devices]
    return lax.ppermute(block, axis, route)


def unit_rows(features):
    factor = lax.rsqrt(jnp.mean(features * features, axis=-1, keepdims=True) + norm_eps)
    return (features * factor).astype(jnp.bfloat16)


def beside(values):
    zero_row = jnp.zeros_like(values[:1])
    from_left = jnp.concatenate([zero_row, values[:-1]], 0)
    from_right = jnp.concatenate([values[1:], zero_row], 0)
    return jnp.stack([from_left, values, from_right], 1)


def tgrp_sum(value):
    if lax.axis_size("tgrp") == 2:
        return value + lax.ppermute(value, "tgrp", [(0, 1), (1, 0)])
    return lax.psum(value, "tgrp")


SEQ = ("z", "y")


def seq_shifted(block, distance):
    devices = range(lax.axis_size("z") * lax.axis_size("y"))
    route = [(i - distance, i) for i in devices if i - distance in devices]
    return lax.ppermute(block, SEQ, route)


def gather_pairs(mine):
    partner = lax.ppermute(mine, "y", [(0, 1), (1, 0)])
    second = lax.axis_index("y") == 1
    pair = jnp.stack([jnp.where(second, partner, mine), jnp.where(second, mine, partner)])
    z_size = lax.axis_size("z")
    got = lax.all_to_all(jnp.broadcast_to(pair, (z_size,) + pair.shape), "z", 0, 0, tiled=False)
    return got.reshape((z_size * 2,) + mine.shape)


def gather_halves(packed):
    half = packed.shape[1] // 2
    core = lax.axis_index("tgrp")
    mine = lax.dynamic_slice_in_dim(packed, core * half, half, 1)
    got = gather_pairs(mine)
    theirs = lax.ppermute(got, "tgrp", [(0, 1), (1, 0)])
    first = jnp.where(core == 0, got, theirs)
    second = jnp.where(core == 0, theirs, got)
    return jnp.concatenate([first, second], 2)


def body_local(
    student_hidden, teacher_hidden, student_proj, teacher_proj, student_chars, teacher_chars, band
):
    rows = student_hidden.shape[0]
    proj_width = student_proj.shape[1]
    blocks = lax.axis_size("z") * lax.axis_size("y")
    me = lax.axis_index("z") * lax.axis_size("y") + lax.axis_index("y")

    s_part = jnp.dot(student_hidden, student_proj, preferred_element_type=jnp.float32)
    t_part = jnp.dot(teacher_hidden, teacher_proj, preferred_element_type=jnp.float32)
    feats = tgrp_sum(jnp.concatenate([s_part, t_part], 1))
    units = jnp.concatenate(
        [unit_rows(feats[:, :proj_width]), unit_rows(feats[:, proj_width:])], 1
    )
    digits = jnp.stack([student_chars, teacher_chars])
    digits = jnp.stack([digits // 4096, digits // 64 % 64, digits % 64], 1)
    digit_rows = digits.reshape(-1, units.shape[1]).astype(jnp.bfloat16)
    flag_row = jnp.zeros((1, units.shape[1]), jnp.bfloat16).at[0, :2].set(band[0].astype(jnp.bfloat16))
    extra = jnp.concatenate([digit_rows, flag_row], 0)
    pad = -(rows + extra.shape[0]) % 16
    packed = jnp.concatenate([units, extra, jnp.zeros((pad, units.shape[1]), jnp.bfloat16)], 0)
    gathered = gather_halves(packed)

    left_rows = seq_shifted(teacher_hidden, 1)
    right_rows = seq_shifted(teacher_hidden, -1)

    s_unit = gathered[:, :rows, :proj_width]
    t_unit = gathered[:, :rows, proj_width:]
    got = gathered[:, rows : rows + digit_rows.shape[0]].astype(jnp.float32).reshape(blocks, 2, 3, rows)
    chars = got[:, :, 0] * 4096.0 + got[:, :, 1] * 64.0 + got[:, :, 2]
    s_pos = chars[:, 0]
    t_pos = beside(chars[:, 1])
    flags = gathered[:, rows + digit_rows.shape[0]].astype(jnp.float32)
    ones_col = jnp.ones((blocks,), jnp.float32)
    slot_mask = jnp.stack([flags[:, 0], ones_col, flags[:, 1]], 1)
    scores = jnp.einsum(
        "bkjp,bip->bkji", beside(t_unit), s_unit, preferred_element_type=jnp.float32
    ) / math.sqrt(proj_width)
    distance = jnp.abs(s_pos[:, None, None, :] - t_pos[:, :, :, None]) / (4.0 * rows)
    kernel = jnp.exp(scores - distance) * slot_mask[:, :, None, None]

    def iterate(iteration, scales):
        row_scale, col_scale = scales
        partial_cols = jnp.sum(row_scale[:, None, None, :] * kernel, axis=3)
        zero_row = jnp.zeros_like(partial_cols[:1, 0])
        column_total = (
            partial_cols[:, 1]
            + jnp.concatenate([zero_row, partial_cols[:-1, 2]], 0)
            + jnp.concatenate([partial_cols[1:, 0], zero_row], 0)
        )
        col_scale = beside(1.0 / column_total)
        row_scale = 1.0 / jnp.sum(kernel * col_scale[:, :, :, None], axis=(1, 2))
        return row_scale, col_scale

    row_scale, col_scale = lax.fori_loop(
        0,
        ITERS,
        iterate,
        (jnp.ones((blocks, rows), jnp.float32), jnp.zeros((blocks, 3, rows), jnp.float32)),
    )
    own_kernel = lax.dynamic_index_in_dim(kernel, me, 0, keepdims=False)
    own_row = lax.dynamic_index_in_dim(row_scale, me, 0, keepdims=False)
    own_col = lax.dynamic_index_in_dim(col_scale, me, 0, keepdims=False)
    plan = (own_row[None, None, :] * own_kernel * own_col[:, :, None]).astype(jnp.bfloat16)
    along_j = (((0,), (0,)), ((), ()))
    aligned = lax.dot_general(plan[1], teacher_hidden, along_j, preferred_element_type=jnp.float32)
    sides = jnp.concatenate([plan[0], plan[2]], 0)
    near_rows = jnp.concatenate([left_rows, right_rows], 0)
    aligned = aligned + lax.dot_general(sides, near_rows, along_j, preferred_element_type=jnp.float32)
    return aligned.astype(jnp.bfloat16)


def body_banded(
    student_hidden, teacher_hidden, student_proj, teacher_proj, student_chars, teacher_chars, band
):
    block_rows = student_hidden.shape[0]
    proj_width = student_proj.shape[1]
    s_part = jnp.dot(student_hidden, student_proj, preferred_element_type=jnp.float32)
    t_part = jnp.dot(teacher_hidden, teacher_proj, preferred_element_type=jnp.float32)
    s_feat, t_feat = lax.psum((s_part, t_part), "tgrp")
    s_unit = unit_rows(s_feat)
    t_unit = unit_rows(t_feat)
    left_rows, left_unit, left_chars = shifted((teacher_hidden, t_unit, teacher_chars), "seq", 1)
    right_rows, right_unit, right_chars = shifted(
        (teacher_hidden, t_unit, teacher_chars), "seq", -1
    )
    near_unit = jnp.stack([left_unit, t_unit, right_unit])
    near_pos = jnp.stack([left_chars, teacher_chars, right_chars]).astype(jnp.float32)
    s_pos = student_chars.astype(jnp.float32)
    flags = band[0]
    slot_mask = jnp.stack([flags[0], jnp.ones((), jnp.int32), flags[1]]).astype(jnp.float32)
    scores = jnp.einsum(
        "ip,kjp->kij", s_unit, near_unit, preferred_element_type=jnp.float32
    ) / math.sqrt(proj_width)
    distance = jnp.abs(s_pos[None, :, None] - near_pos[:, None, :]) / (4.0 * block_rows)
    kernel = jnp.exp(scores - distance) * slot_mask[:, None, None]
    row_scale = jnp.ones((block_rows,), jnp.float32)
    col_scale = jnp.zeros((3, block_rows), jnp.float32)
    for iteration in range(ITERS):
        partial_cols = jnp.sum(row_scale[None, :, None] * kernel, axis=1)
        left_one = shifted(partial_cols[1:], "seq", 1)
        left_two = shifted(partial_cols[2:], "seq", 2)
        right_one = shifted(partial_cols[:2], "seq", -1)
        right_two = shifted(partial_cols[:1], "seq", -2)
        column_total = jnp.stack(
            [
                left_two[0] + left_one[0] + partial_cols[0],
                left_one[1] + partial_cols[1] + right_one[0],
                partial_cols[2] + right_one[1] + right_two[0],
            ]
        )
        col_scale = slot_mask[:, None] / jnp.where(slot_mask[:, None] > 0.0, column_total, 1.0)
        row_scale = 1.0 / jnp.sum(kernel * col_scale[:, None, :], axis=(0, 2))
    plan = (row_scale[None, :, None] * kernel * col_scale[:, None, :]).astype(jnp.bfloat16)
    aligned = jnp.dot(plan[0], left_rows, preferred_element_type=jnp.float32)
    aligned = aligned + jnp.dot(plan[1], teacher_hidden, preferred_element_type=jnp.float32)
    aligned = aligned + jnp.dot(plan[2], right_rows, preferred_element_type=jnp.float32)
    return aligned.astype(jnp.bfloat16)


def specs(seq):
    return dict(
        in_specs=(
            P(("groups",) + seq, "tgrp"),
            P(("groups",) + seq, "tgrp"),
            P("tgrp", None),
            P("tgrp", None),
            P(("groups",) + seq),
            P(("groups",) + seq),
            P(("groups",) + seq, None),
        ),
        out_specs=P(("groups",) + seq, "tgrp"),
    )


def solution(mesh):
    blocks = mesh.shape["seq"]
    sizes = dict(mesh.shape)

    def fits(rows):
        return blocks * 3 * rows * rows * 4 <= LOCAL_KERNEL_BYTES

    local = blocks % 2 == 0 and sizes["tgrp"] == 2
    if local:
        view = jax.sharding.Mesh(
            mesh.devices.reshape(sizes["groups"], blocks // 2, 2, sizes["tgrp"]),
            ("groups", "z", "y", "tgrp"),
        )
        local_fn = jax.shard_map(body_local, mesh=view, check_vma=False, **specs(SEQ))
    banded_fn = jax.shard_map(body_banded, mesh=mesh, check_vma=False, **specs(("seq",)))

    def run(*args):
        rows = args[0].shape[0] // (sizes["groups"] * blocks)
        if local and fits(rows):
            return local_fn(*args)
        return banded_fn(*args)

    return run
```

```python
import math

import jax
import jax.numpy as jnp
from jax import lax
from jax.sharding import PartitionSpec as P

ITERS = 4

LOCAL_KERNEL_BYTES = 24 * 2**20

norm_eps = 1e-05


def shifted(block, axis, distance):
    devices = range(lax.axis_size(axis))
    route = [(i - distance, i) for i in devices if i - distance in devices]
    return lax.ppermute(block, axis, route)


def unit_rows(features):
    factor = lax.rsqrt(jnp.mean(features * features, axis=-1, keepdims=True) + norm_eps)
    return (features * factor).astype(jnp.bfloat16)


def beside(values):
    zero_row = jnp.zeros_like(values[:1])
    from_left = jnp.concatenate([zero_row, values[:-1]], 0)
    from_right = jnp.concatenate([values[1:], zero_row], 0)
    return jnp.stack([from_left, values, from_right], 1)


def tgrp_sum(value):
    if lax.axis_size("tgrp") == 2:
        return value + lax.ppermute(value, "tgrp", [(0, 1), (1, 0)])
    return lax.psum(value, "tgrp")


SEQ = ("z", "y")


def seq_shifted(block, distance):
    devices = range(lax.axis_size("z") * lax.axis_size("y"))
    route = [(i - distance, i) for i in devices if i - distance in devices]
    return lax.ppermute(block, SEQ, route)


def gather_pairs(mine):
    z_size = lax.axis_size("z")
    row = lax.all_to_all(jnp.broadcast_to(mine, (z_size,) + mine.shape), "z", 0, 0, tiled=False)
    other = lax.ppermute(row, "y", [(0, 1), (1, 0)])
    second = lax.axis_index("y") == 1
    got = jnp.stack([jnp.where(second, other, row), jnp.where(second, row, other)], 1)
    return got.reshape((z_size * 2,) + mine.shape)


def gather_halves(packed):
    half = packed.shape[1] // 2
    core = lax.axis_index("tgrp")
    mine = lax.dynamic_slice_in_dim(packed, core * half, half, 1)
    got = gather_pairs(mine)
    theirs = lax.ppermute(got, "tgrp", [(0, 1), (1, 0)])
    first = jnp.where(core == 0, got, theirs)
    second = jnp.where(core == 0, theirs, got)
    return jnp.concatenate([first, second], 2)


def body_local(
    student_hidden, teacher_hidden, student_proj, teacher_proj, student_chars, teacher_chars, band
):
    rows = student_hidden.shape[0]
    proj_width = student_proj.shape[1]
    blocks = lax.axis_size("z") * lax.axis_size("y")
    me = lax.axis_index("z") * lax.axis_size("y") + lax.axis_index("y")

    s_part = jnp.dot(student_hidden, student_proj, preferred_element_type=jnp.float32)
    t_part = jnp.dot(teacher_hidden, teacher_proj, preferred_element_type=jnp.float32)
    feats = tgrp_sum(jnp.concatenate([s_part, t_part], 1))
    units = jnp.concatenate(
        [unit_rows(feats[:, :proj_width]), unit_rows(feats[:, proj_width:])], 1
    )
    digits = jnp.stack([student_chars, teacher_chars])
    digits = jnp.stack([digits // 4096, digits // 64 % 64, digits % 64], 1)
    digit_rows = digits.reshape(-1, units.shape[1]).astype(jnp.bfloat16)
    flag_row = jnp.zeros((1, units.shape[1]), jnp.bfloat16).at[0, :2].set(band[0].astype(jnp.bfloat16))
    extra = jnp.concatenate([digit_rows, flag_row], 0)
    pad = -(rows + extra.shape[0]) % 16
    packed = jnp.concatenate([units, extra, jnp.zeros((pad, units.shape[1]), jnp.bfloat16)], 0)
    gathered = gather_halves(packed)

    left_rows = seq_shifted(teacher_hidden, 1)
    right_rows = seq_shifted(teacher_hidden, -1)

    s_unit = gathered[:, :rows, :proj_width]
    t_unit = gathered[:, :rows, proj_width:]
    got = gathered[:, rows : rows + digit_rows.shape[0]].astype(jnp.float32).reshape(blocks, 2, 3, rows)
    chars = got[:, :, 0] * 4096.0 + got[:, :, 1] * 64.0 + got[:, :, 2]
    s_pos = chars[:, 0]
    t_pos = beside(chars[:, 1])
    flags = gathered[:, rows + digit_rows.shape[0]].astype(jnp.float32)
    ones_col = jnp.ones((blocks,), jnp.float32)
    slot_mask = jnp.stack([flags[:, 0], ones_col, flags[:, 1]], 1)
    scores = jnp.einsum(
        "bkjp,bip->bkji", beside(t_unit), s_unit, preferred_element_type=jnp.float32
    ) / math.sqrt(proj_width)
    distance = jnp.abs(s_pos[:, None, None, :] - t_pos[:, :, :, None]) / (4.0 * rows)
    kernel = jnp.exp(scores - distance) * slot_mask[:, :, None, None]

    def iterate(iteration, scales):
        row_scale, col_scale = scales
        partial_cols = jnp.sum(row_scale[:, None, None, :] * kernel, axis=3)
        zero_row = jnp.zeros_like(partial_cols[:1, 0])
        column_total = (
            partial_cols[:, 1]
            + jnp.concatenate([zero_row, partial_cols[:-1, 2]], 0)
            + jnp.concatenate([partial_cols[1:, 0], zero_row], 0)
        )
        col_scale = beside(1.0 / column_total)
        row_scale = 1.0 / jnp.sum(kernel * col_scale[:, :, :, None], axis=(1, 2))
        return row_scale, col_scale

    row_scale, col_scale = lax.fori_loop(
        0,
        ITERS,
        iterate,
        (jnp.ones((blocks, rows), jnp.float32), jnp.zeros((blocks, 3, rows), jnp.float32)),
    )
    own_kernel = lax.dynamic_index_in_dim(kernel, me, 0, keepdims=False)
    own_row = lax.dynamic_index_in_dim(row_scale, me, 0, keepdims=False)
    own_col = lax.dynamic_index_in_dim(col_scale, me, 0, keepdims=False)
    plan = (own_row[None, None, :] * own_kernel * own_col[:, :, None]).astype(jnp.bfloat16)
    along_j = (((0,), (0,)), ((), ()))
    aligned = lax.dot_general(plan[1], teacher_hidden, along_j, preferred_element_type=jnp.float32)
    sides = jnp.concatenate([plan[0], plan[2]], 0)
    near_rows = jnp.concatenate([left_rows, right_rows], 0)
    aligned = aligned + lax.dot_general(sides, near_rows, along_j, preferred_element_type=jnp.float32)
    return aligned.astype(jnp.bfloat16)


def body_banded(
    student_hidden, teacher_hidden, student_proj, teacher_proj, student_chars, teacher_chars, band
):
    block_rows = student_hidden.shape[0]
    proj_width = student_proj.shape[1]
    s_part = jnp.dot(student_hidden, student_proj, preferred_element_type=jnp.float32)
    t_part = jnp.dot(teacher_hidden, teacher_proj, preferred_element_type=jnp.float32)
    s_feat, t_feat = lax.psum((s_part, t_part), "tgrp")
    s_unit = unit_rows(s_feat)
    t_unit = unit_rows(t_feat)
    left_rows, left_unit, left_chars = shifted((teacher_hidden, t_unit, teacher_chars), "seq", 1)
    right_rows, right_unit, right_chars = shifted(
        (teacher_hidden, t_unit, teacher_chars), "seq", -1
    )
    near_unit = jnp.stack([left_unit, t_unit, right_unit])
    near_pos = jnp.stack([left_chars, teacher_chars, right_chars]).astype(jnp.float32)
    s_pos = student_chars.astype(jnp.float32)
    flags = band[0]
    slot_mask = jnp.stack([flags[0], jnp.ones((), jnp.int32), flags[1]]).astype(jnp.float32)
    scores = jnp.einsum(
        "ip,kjp->kij", s_unit, near_unit, preferred_element_type=jnp.float32
    ) / math.sqrt(proj_width)
    distance = jnp.abs(s_pos[None, :, None] - near_pos[:, None, :]) / (4.0 * block_rows)
    kernel = jnp.exp(scores - distance) * slot_mask[:, None, None]
    row_scale = jnp.ones((block_rows,), jnp.float32)
    col_scale = jnp.zeros((3, block_rows), jnp.float32)
    for iteration in range(ITERS):
        partial_cols = jnp.sum(row_scale[None, :, None] * kernel, axis=1)
        left_one = shifted(partial_cols[1:], "seq", 1)
        left_two = shifted(partial_cols[2:], "seq", 2)
        right_one = shifted(partial_cols[:2], "seq", -1)
        right_two = shifted(partial_cols[:1], "seq", -2)
        column_total = jnp.stack(
            [
                left_two[0] + left_one[0] + partial_cols[0],
                left_one[1] + partial_cols[1] + right_one[0],
                partial_cols[2] + right_one[1] + right_two[0],
            ]
        )
        col_scale = slot_mask[:, None] / jnp.where(slot_mask[:, None] > 0.0, column_total, 1.0)
        row_scale = 1.0 / jnp.sum(kernel * col_scale[:, None, :], axis=(0, 2))
    plan = (row_scale[None, :, None] * kernel * col_scale[:, None, :]).astype(jnp.bfloat16)
    aligned = jnp.dot(plan[0], left_rows, preferred_element_type=jnp.float32)
    aligned = aligned + jnp.dot(plan[1], teacher_hidden, preferred_element_type=jnp.float32)
    aligned = aligned + jnp.dot(plan[2], right_rows, preferred_element_type=jnp.float32)
    return aligned.astype(jnp.bfloat16)


def specs(seq):
    return dict(
        in_specs=(
            P(("groups",) + seq, "tgrp"),
            P(("groups",) + seq, "tgrp"),
            P("tgrp", None),
            P("tgrp", None),
            P(("groups",) + seq),
            P(("groups",) + seq),
            P(("groups",) + seq, None),
        ),
        out_specs=P(("groups",) + seq, "tgrp"),
    )


def solution(mesh):
    blocks = mesh.shape["seq"]
    sizes = dict(mesh.shape)

    def fits(rows):
        return blocks * 3 * rows * rows * 4 <= LOCAL_KERNEL_BYTES

    local = blocks % 2 == 0 and sizes["tgrp"] == 2
    if local:
        view = jax.sharding.Mesh(
            mesh.devices.reshape(sizes["groups"], blocks // 2, 2, sizes["tgrp"]),
            ("groups", "z", "y", "tgrp"),
        )
        local_fn = jax.shard_map(body_local, mesh=view, check_vma=False, **specs(SEQ))
    banded_fn = jax.shard_map(body_banded, mesh=mesh, check_vma=False, **specs(("seq",)))

    def run(*args):
        rows = args[0].shape[0] // (sizes["groups"] * blocks)
        if local and fits(rows):
            return local_fn(*args)
        return banded_fn(*args)

    return run
```

```python
import math

import jax
import jax.numpy as jnp
from jax import lax
from jax.sharding import PartitionSpec as P

ITERS = 4

LOCAL_KERNEL_BYTES = 24 * 2**20

norm_eps = 1e-05


def shifted(block, axis, distance):
    devices = range(lax.axis_size(axis))
    route = [(i - distance, i) for i in devices if i - distance in devices]
    return lax.ppermute(block, axis, route)


def unit_rows(features):
    factor = lax.rsqrt(jnp.mean(features * features, axis=-1, keepdims=True) + norm_eps)
    return (features * factor).astype(jnp.bfloat16)


def beside(values):
    zero_row = jnp.zeros_like(values[:1])
    from_left = jnp.concatenate([zero_row, values[:-1]], 0)
    from_right = jnp.concatenate([values[1:], zero_row], 0)
    return jnp.stack([from_left, values, from_right], 1)


def tgrp_sum(value):
    if lax.axis_size("tgrp") == 2:
        return value + lax.ppermute(value, "tgrp", [(0, 1), (1, 0)])
    return lax.psum(value, "tgrp")


def gather_seq(block):
    n = lax.axis_size("seq")
    if n % 2:
        return lax.all_gather(block, "seq")
    me = lax.axis_index("seq")
    pairs = n // 2
    partner = lax.ppermute(block, "seq", [(i, i ^ 1) for i in range(n)])
    odd = me % 2 == 1
    pair = jnp.stack([jnp.where(odd, partner, block), jnp.where(odd, block, partner)])
    by_offset = [pair]
    for d in range(1, pairs):
        by_offset = [shifted(pair, "seq", 2 * d)] + by_offset + [shifted(pair, "seq", -2 * d)]
    window = lax.dynamic_slice_in_dim(jnp.stack(by_offset), pairs - 1 - me // 2, pairs, 0)
    return window.reshape((n,) + block.shape)


def gather_halves(packed):
    if lax.axis_size("tgrp") != 2:
        return lax.all_gather(packed, "seq")
    half = packed.shape[1] // 2
    core = lax.axis_index("tgrp")
    mine = lax.dynamic_slice_in_dim(packed, core * half, half, 1)
    n = lax.axis_size("seq")
    got = lax.all_to_all(jnp.broadcast_to(mine, (n,) + mine.shape), "seq", 0, 0, tiled=False)
    theirs = lax.ppermute(got, "tgrp", [(0, 1), (1, 0)])
    first = jnp.where(core == 0, got, theirs)
    second = jnp.where(core == 0, theirs, got)
    return jnp.concatenate([first, second], 2)


def body_local(
    student_hidden, teacher_hidden, student_proj, teacher_proj, student_chars, teacher_chars, band
):
    rows = student_hidden.shape[0]
    proj_width = student_proj.shape[1]
    blocks = lax.axis_size("seq")
    me = lax.axis_index("seq")

    along_width = (((0,), (1,)), ((), ()))
    s_part = lax.dot_general(student_proj, student_hidden, along_width, preferred_element_type=jnp.float32)
    t_part = lax.dot_general(teacher_proj, teacher_hidden, along_width, preferred_element_type=jnp.float32)
    feats = tgrp_sum(jnp.concatenate([s_part, t_part], 0).T)
    units = jnp.concatenate(
        [unit_rows(feats[:, :proj_width]), unit_rows(feats[:, proj_width:])], 1
    )
    digits = jnp.stack([student_chars, teacher_chars])
    digits = jnp.stack([digits // 4096, digits // 64 % 64, digits % 64], 1)
    digit_rows = digits.reshape(-1, units.shape[1]).astype(jnp.bfloat16)
    flag_row = jnp.zeros((1, units.shape[1]), jnp.bfloat16).at[0, :2].set(band[0].astype(jnp.bfloat16))
    extra = jnp.concatenate([digit_rows, flag_row], 0)
    pad = -(rows + extra.shape[0]) % 16
    packed = jnp.concatenate([units, extra, jnp.zeros((pad, units.shape[1]), jnp.bfloat16)], 0)
    gathered = gather_halves(packed)

    left_rows = shifted(teacher_hidden, "seq", 1)
    right_rows = shifted(teacher_hidden, "seq", -1)

    s_unit = gathered[:, :rows, :proj_width]
    t_unit = gathered[:, :rows, proj_width:]
    got = gathered[:, rows : rows + digit_rows.shape[0]].astype(jnp.float32).reshape(blocks, 2, 3, rows)
    chars = got[:, :, 0] * 4096.0 + got[:, :, 1] * 64.0 + got[:, :, 2]
    s_pos = chars[:, 0]
    t_pos = beside(chars[:, 1])
    flags = gathered[:, rows + digit_rows.shape[0]].astype(jnp.float32)
    ones_col = jnp.ones((blocks,), jnp.float32)
    slot_mask = jnp.stack([flags[:, 0], ones_col, flags[:, 1]], 1)
    scores = jnp.einsum(
        "bkjp,bip->bkji", beside(t_unit), s_unit, preferred_element_type=jnp.float32
    ) / math.sqrt(proj_width)
    distance = jnp.abs(s_pos[:, None, None, :] - t_pos[:, :, :, None]) / (4.0 * rows)
    kernel = jnp.exp(scores - distance) * slot_mask[:, :, None, None]

    def iterate(iteration, scales):
        row_scale, col_scale = scales
        partial_cols = jnp.sum(row_scale[:, None, None, :] * kernel, axis=3)
        zero_row = jnp.zeros_like(partial_cols[:1, 0])
        column_total = (
            partial_cols[:, 1]
            + jnp.concatenate([zero_row, partial_cols[:-1, 2]], 0)
            + jnp.concatenate([partial_cols[1:, 0], zero_row], 0)
        )
        col_scale = beside(1.0 / column_total)
        row_scale = 1.0 / jnp.sum(kernel * col_scale[:, :, :, None], axis=(1, 2))
        return row_scale, col_scale

    row_scale, col_scale = lax.fori_loop(
        0,
        ITERS,
        iterate,
        (jnp.ones((blocks, rows), jnp.float32), jnp.zeros((blocks, 3, rows), jnp.float32)),
    )
    own_kernel = lax.dynamic_index_in_dim(kernel, me, 0, keepdims=False)
    own_row = lax.dynamic_index_in_dim(row_scale, me, 0, keepdims=False)
    own_col = lax.dynamic_index_in_dim(col_scale, me, 0, keepdims=False)
    plan = (own_row[None, None, :] * own_kernel * own_col[:, :, None]).astype(jnp.bfloat16)
    along_j = (((0,), (0,)), ((), ()))
    aligned = lax.dot_general(plan[1], teacher_hidden, along_j, preferred_element_type=jnp.float32)
    sides = jnp.concatenate([plan[0], plan[2]], 0)
    near_rows = jnp.concatenate([left_rows, right_rows], 0)
    aligned = aligned + lax.dot_general(sides, near_rows, along_j, preferred_element_type=jnp.float32)
    return aligned.astype(jnp.bfloat16)


def body_banded(
    student_hidden, teacher_hidden, student_proj, teacher_proj, student_chars, teacher_chars, band
):
    block_rows = student_hidden.shape[0]
    proj_width = student_proj.shape[1]
    s_part = jnp.dot(student_hidden, student_proj, preferred_element_type=jnp.float32)
    t_part = jnp.dot(teacher_hidden, teacher_proj, preferred_element_type=jnp.float32)
    s_feat, t_feat = lax.psum((s_part, t_part), "tgrp")
    s_unit = unit_rows(s_feat)
    t_unit = unit_rows(t_feat)
    left_rows, left_unit, left_chars = shifted((teacher_hidden, t_unit, teacher_chars), "seq", 1)
    right_rows, right_unit, right_chars = shifted(
        (teacher_hidden, t_unit, teacher_chars), "seq", -1
    )
    near_unit = jnp.stack([left_unit, t_unit, right_unit])
    near_pos = jnp.stack([left_chars, teacher_chars, right_chars]).astype(jnp.float32)
    s_pos = student_chars.astype(jnp.float32)
    flags = band[0]
    slot_mask = jnp.stack([flags[0], jnp.ones((), jnp.int32), flags[1]]).astype(jnp.float32)
    scores = jnp.einsum(
        "ip,kjp->kij", s_unit, near_unit, preferred_element_type=jnp.float32
    ) / math.sqrt(proj_width)
    distance = jnp.abs(s_pos[None, :, None] - near_pos[:, None, :]) / (4.0 * block_rows)
    kernel = jnp.exp(scores - distance) * slot_mask[:, None, None]
    row_scale = jnp.ones((block_rows,), jnp.float32)
    col_scale = jnp.zeros((3, block_rows), jnp.float32)
    for iteration in range(ITERS):
        partial_cols = jnp.sum(row_scale[None, :, None] * kernel, axis=1)
        left_one = shifted(partial_cols[1:], "seq", 1)
        left_two = shifted(partial_cols[2:], "seq", 2)
        right_one = shifted(partial_cols[:2], "seq", -1)
        right_two = shifted(partial_cols[:1], "seq", -2)
        column_total = jnp.stack(
            [
                left_two[0] + left_one[0] + partial_cols[0],
                left_one[1] + partial_cols[1] + right_one[0],
                partial_cols[2] + right_one[1] + right_two[0],
            ]
        )
        col_scale = slot_mask[:, None] / jnp.where(slot_mask[:, None] > 0.0, column_total, 1.0)
        row_scale = 1.0 / jnp.sum(kernel * col_scale[:, None, :], axis=(0, 2))
    plan = (row_scale[None, :, None] * kernel * col_scale[:, None, :]).astype(jnp.bfloat16)
    aligned = jnp.dot(plan[0], left_rows, preferred_element_type=jnp.float32)
    aligned = aligned + jnp.dot(plan[1], teacher_hidden, preferred_element_type=jnp.float32)
    aligned = aligned + jnp.dot(plan[2], right_rows, preferred_element_type=jnp.float32)
    return aligned.astype(jnp.bfloat16)


def solution(mesh):
    blocks = mesh.shape["seq"]

    def body(*args):
        rows = args[0].shape[0]
        if blocks * 3 * rows * rows * 4 <= LOCAL_KERNEL_BYTES:
            return body_local(*args)
        return body_banded(*args)

    return jax.shard_map(
        body,
        mesh=mesh,
        in_specs=(
            P(("groups", "seq"), "tgrp"),
            P(("groups", "seq"), "tgrp"),
            P("tgrp", None),
            P("tgrp", None),
            P(("groups", "seq")),
            P(("groups", "seq")),
            P(("groups", "seq"), None),
        ),
        out_specs=P(("groups", "seq"), "tgrp"),
        check_vma=False,
    )
```

```python
import math

import jax
import jax.numpy as jnp
from jax import lax
from jax.sharding import PartitionSpec as P

ITERS = 4

LOCAL_KERNEL_BYTES = 24 * 2**20

norm_eps = 1e-05


def shifted(block, axis, distance):
    devices = range(lax.axis_size(axis))
    route = [(i - distance, i) for i in devices if i - distance in devices]
    return lax.ppermute(block, axis, route)


def unit_rows(features):
    factor = lax.rsqrt(jnp.mean(features * features, axis=-1, keepdims=True) + norm_eps)
    return (features * factor).astype(jnp.bfloat16)


def beside(values):
    zero_row = jnp.zeros_like(values[:1])
    from_left = jnp.concatenate([zero_row, values[:-1]], 0)
    from_right = jnp.concatenate([values[1:], zero_row], 0)
    return jnp.stack([from_left, values, from_right], 1)


def tgrp_sum(value):
    if lax.axis_size("tgrp") == 2:
        return value + lax.ppermute(value, "tgrp", [(0, 1), (1, 0)])
    return lax.psum(value, "tgrp")


SEQ = ("z", "y")


def seq_shifted(block, distance):
    devices = range(lax.axis_size("z") * lax.axis_size("y"))
    route = [(i - distance, i) for i in devices if i - distance in devices]
    return lax.ppermute(block, SEQ, route)


def gather_halves(packed):
    half = packed.shape[1] // 2
    core = lax.axis_index("tgrp")
    mine = lax.dynamic_slice_in_dim(packed, core * half, half, 1)
    z_size = lax.axis_size("z")
    row = lax.all_to_all(jnp.broadcast_to(mine, (z_size,) + mine.shape), "z", 0, 0, tiled=False)
    row_other_core = lax.ppermute(row, "tgrp", [(0, 1), (1, 0)])
    other_y = lax.ppermute(row, "y", [(0, 1), (1, 0)])
    other_y_other_core = lax.ppermute(row, ("y", "tgrp"), [(i, 3 - i) for i in range(4)])
    first_core = core == 0
    same_y = jnp.concatenate(
        [jnp.where(first_core, row, row_other_core), jnp.where(first_core, row_other_core, row)], 2
    )
    across_y = jnp.concatenate(
        [jnp.where(first_core, other_y, other_y_other_core), jnp.where(first_core, other_y_other_core, other_y)],
        2,
    )
    second_y = lax.axis_index("y") == 1
    got = jnp.stack([jnp.where(second_y, across_y, same_y), jnp.where(second_y, same_y, across_y)], 1)
    return got.reshape((z_size * 2,) + packed.shape)


def body_local(
    student_hidden, teacher_hidden, student_proj, teacher_proj, student_chars, teacher_chars, band
):
    rows = student_hidden.shape[0]
    proj_width = student_proj.shape[1]
    blocks = lax.axis_size("z") * lax.axis_size("y")
    me = lax.axis_index("z") * lax.axis_size("y") + lax.axis_index("y")

    s_part = jnp.dot(student_hidden, student_proj, preferred_element_type=jnp.float32)
    t_part = jnp.dot(teacher_hidden, teacher_proj, preferred_element_type=jnp.float32)
    feats = tgrp_sum(jnp.concatenate([s_part, t_part], 1))
    units = jnp.concatenate(
        [unit_rows(feats[:, :proj_width]), unit_rows(feats[:, proj_width:])], 1
    )
    digits = jnp.stack([student_chars, teacher_chars])
    digits = jnp.stack([digits // 4096, digits // 64 % 64, digits % 64], 1)
    digit_rows = digits.reshape(-1, units.shape[1]).astype(jnp.bfloat16)
    flag_row = jnp.zeros((1, units.shape[1]), jnp.bfloat16).at[0, :2].set(band[0].astype(jnp.bfloat16))
    extra = jnp.concatenate([digit_rows, flag_row], 0)
    pad = -(rows + extra.shape[0]) % 16
    packed = jnp.concatenate([units, extra, jnp.zeros((pad, units.shape[1]), jnp.bfloat16)], 0)
    gathered = gather_halves(packed)

    left_rows = seq_shifted(teacher_hidden, 1)
    right_rows = seq_shifted(teacher_hidden, -1)

    s_unit = gathered[:, :rows, :proj_width]
    t_unit = gathered[:, :rows, proj_width:]
    got = gathered[:, rows : rows + digit_rows.shape[0]].astype(jnp.float32).reshape(blocks, 2, 3, rows)
    chars = got[:, :, 0] * 4096.0 + got[:, :, 1] * 64.0 + got[:, :, 2]
    s_pos = chars[:, 0]
    t_pos = beside(chars[:, 1])
    flags = gathered[:, rows + digit_rows.shape[0]].astype(jnp.float32)
    ones_col = jnp.ones((blocks,), jnp.float32)
    slot_mask = jnp.stack([flags[:, 0], ones_col, flags[:, 1]], 1)
    scores = jnp.einsum(
        "bkjp,bip->bkji", beside(t_unit), s_unit, preferred_element_type=jnp.float32
    ) / math.sqrt(proj_width)
    distance = jnp.abs(s_pos[:, None, None, :] - t_pos[:, :, :, None]) / (4.0 * rows)
    kernel = jnp.exp(scores - distance) * slot_mask[:, :, None, None]

    def iterate(iteration, scales):
        row_scale, col_scale = scales
        partial_cols = jnp.sum(row_scale[:, None, None, :] * kernel, axis=3)
        zero_row = jnp.zeros_like(partial_cols[:1, 0])
        column_total = (
            partial_cols[:, 1]
            + jnp.concatenate([zero_row, partial_cols[:-1, 2]], 0)
            + jnp.concatenate([partial_cols[1:, 0], zero_row], 0)
        )
        col_scale = beside(1.0 / column_total)
        row_scale = 1.0 / jnp.sum(kernel * col_scale[:, :, :, None], axis=(1, 2))
        return row_scale, col_scale

    row_scale, col_scale = lax.fori_loop(
        0,
        ITERS,
        iterate,
        (jnp.ones((blocks, rows), jnp.float32), jnp.zeros((blocks, 3, rows), jnp.float32)),
    )
    own_kernel = lax.dynamic_index_in_dim(kernel, me, 0, keepdims=False)
    own_row = lax.dynamic_index_in_dim(row_scale, me, 0, keepdims=False)
    own_col = lax.dynamic_index_in_dim(col_scale, me, 0, keepdims=False)
    plan = (own_row[None, None, :] * own_kernel * own_col[:, :, None]).astype(jnp.bfloat16)
    along_j = (((0,), (0,)), ((), ()))
    aligned = lax.dot_general(plan[1], teacher_hidden, along_j, preferred_element_type=jnp.float32)
    sides = jnp.concatenate([plan[0], plan[2]], 0)
    near_rows = jnp.concatenate([left_rows, right_rows], 0)
    aligned = aligned + lax.dot_general(sides, near_rows, along_j, preferred_element_type=jnp.float32)
    return aligned.astype(jnp.bfloat16)


def body_banded(
    student_hidden, teacher_hidden, student_proj, teacher_proj, student_chars, teacher_chars, band
):
    block_rows = student_hidden.shape[0]
    proj_width = student_proj.shape[1]
    s_part = jnp.dot(student_hidden, student_proj, preferred_element_type=jnp.float32)
    t_part = jnp.dot(teacher_hidden, teacher_proj, preferred_element_type=jnp.float32)
    s_feat, t_feat = lax.psum((s_part, t_part), "tgrp")
    s_unit = unit_rows(s_feat)
    t_unit = unit_rows(t_feat)
    left_rows, left_unit, left_chars = shifted((teacher_hidden, t_unit, teacher_chars), "seq", 1)
    right_rows, right_unit, right_chars = shifted(
        (teacher_hidden, t_unit, teacher_chars), "seq", -1
    )
    near_unit = jnp.stack([left_unit, t_unit, right_unit])
    near_pos = jnp.stack([left_chars, teacher_chars, right_chars]).astype(jnp.float32)
    s_pos = student_chars.astype(jnp.float32)
    flags = band[0]
    slot_mask = jnp.stack([flags[0], jnp.ones((), jnp.int32), flags[1]]).astype(jnp.float32)
    scores = jnp.einsum(
        "ip,kjp->kij", s_unit, near_unit, preferred_element_type=jnp.float32
    ) / math.sqrt(proj_width)
    distance = jnp.abs(s_pos[None, :, None] - near_pos[:, None, :]) / (4.0 * block_rows)
    kernel = jnp.exp(scores - distance) * slot_mask[:, None, None]
    row_scale = jnp.ones((block_rows,), jnp.float32)
    col_scale = jnp.zeros((3, block_rows), jnp.float32)
    for iteration in range(ITERS):
        partial_cols = jnp.sum(row_scale[None, :, None] * kernel, axis=1)
        left_one = shifted(partial_cols[1:], "seq", 1)
        left_two = shifted(partial_cols[2:], "seq", 2)
        right_one = shifted(partial_cols[:2], "seq", -1)
        right_two = shifted(partial_cols[:1], "seq", -2)
        column_total = jnp.stack(
            [
                left_two[0] + left_one[0] + partial_cols[0],
                left_one[1] + partial_cols[1] + right_one[0],
                partial_cols[2] + right_one[1] + right_two[0],
            ]
        )
        col_scale = slot_mask[:, None] / jnp.where(slot_mask[:, None] > 0.0, column_total, 1.0)
        row_scale = 1.0 / jnp.sum(kernel * col_scale[:, None, :], axis=(0, 2))
    plan = (row_scale[None, :, None] * kernel * col_scale[:, None, :]).astype(jnp.bfloat16)
    aligned = jnp.dot(plan[0], left_rows, preferred_element_type=jnp.float32)
    aligned = aligned + jnp.dot(plan[1], teacher_hidden, preferred_element_type=jnp.float32)
    aligned = aligned + jnp.dot(plan[2], right_rows, preferred_element_type=jnp.float32)
    return aligned.astype(jnp.bfloat16)


def specs(seq):
    return dict(
        in_specs=(
            P(("groups",) + seq, "tgrp"),
            P(("groups",) + seq, "tgrp"),
            P("tgrp", None),
            P("tgrp", None),
            P(("groups",) + seq),
            P(("groups",) + seq),
            P(("groups",) + seq, None),
        ),
        out_specs=P(("groups",) + seq, "tgrp"),
    )


def solution(mesh):
    blocks = mesh.shape["seq"]
    sizes = dict(mesh.shape)

    def fits(rows):
        return blocks * 3 * rows * rows * 4 <= LOCAL_KERNEL_BYTES

    local = blocks % 2 == 0 and sizes["tgrp"] == 2
    if local:
        view = jax.sharding.Mesh(
            mesh.devices.reshape(sizes["groups"], blocks // 2, 2, sizes["tgrp"]),
            ("groups", "z", "y", "tgrp"),
        )
        local_fn = jax.shard_map(body_local, mesh=view, check_vma=False, **specs(SEQ))
    banded_fn = jax.shard_map(body_banded, mesh=mesh, check_vma=False, **specs(("seq",)))

    def run(*args):
        rows = args[0].shape[0] // (sizes["groups"] * blocks)
        if local and fits(rows):
            return local_fn(*args)
        return banded_fn(*args)

    return run
```

```python
import math

import jax
import jax.numpy as jnp
from jax import lax
from jax.sharding import PartitionSpec as P

ITERS = 4

LOCAL_KERNEL_BYTES = 24 * 2**20

norm_eps = 1e-05


def shifted(block, axis, distance):
    devices = range(lax.axis_size(axis))
    route = [(i - distance, i) for i in devices if i - distance in devices]
    return lax.ppermute(block, axis, route)


def unit_rows(features):
    factor = lax.rsqrt(jnp.mean(features * features, axis=-1, keepdims=True) + norm_eps)
    return (features * factor).astype(jnp.bfloat16)


def beside(values):
    zero_row = jnp.zeros_like(values[:1])
    from_left = jnp.concatenate([zero_row, values[:-1]], 0)
    from_right = jnp.concatenate([values[1:], zero_row], 0)
    return jnp.stack([from_left, values, from_right], 1)


def tgrp_sum(value):
    if lax.axis_size("tgrp") == 2:
        return value + lax.ppermute(value, "tgrp", [(0, 1), (1, 0)])
    return lax.psum(value, "tgrp")


SEQ = ("z", "y")


def seq_shifted(block, distance):
    devices = range(lax.axis_size("z") * lax.axis_size("y"))
    route = [(i - distance, i) for i in devices if i - distance in devices]
    return lax.ppermute(block, SEQ, route)


def gather_pairs(mine):
    z_size = lax.axis_size("z")
    cut = mine.shape[1] // 2
    part_a, part_b = mine[:, :cut], mine[:, cut:]
    second = lax.axis_index("y") == 1
    row_a = lax.all_to_all(jnp.broadcast_to(part_a, (z_size,) + part_a.shape), "z", 0, 0, tiled=False)
    partner_b = lax.ppermute(part_b, "y", [(0, 1), (1, 0)])
    pair_b = jnp.stack([jnp.where(second, partner_b, part_b), jnp.where(second, part_b, partner_b)])
    other_a = lax.ppermute(row_a, "y", [(0, 1), (1, 0)])
    got_b = lax.all_to_all(jnp.broadcast_to(pair_b, (z_size,) + pair_b.shape), "z", 0, 0, tiled=False)
    got_a = jnp.stack([jnp.where(second, other_a, row_a), jnp.where(second, row_a, other_a)], 1)
    got = jnp.concatenate([got_a, got_b], -1)
    return got.reshape((z_size * 2,) + mine.shape)


def gather_halves(packed):
    half = packed.shape[1] // 2
    core = lax.axis_index("tgrp")
    mine = lax.dynamic_slice_in_dim(packed, core * half, half, 1)
    got = gather_pairs(mine)
    theirs = lax.ppermute(got, "tgrp", [(0, 1), (1, 0)])
    first = jnp.where(core == 0, got, theirs)
    second = jnp.where(core == 0, theirs, got)
    return jnp.concatenate([first, second], 2)


def body_local(
    student_hidden, teacher_hidden, student_proj, teacher_proj, student_chars, teacher_chars, band
):
    rows = student_hidden.shape[0]
    proj_width = student_proj.shape[1]
    blocks = lax.axis_size("z") * lax.axis_size("y")
    me = lax.axis_index("z") * lax.axis_size("y") + lax.axis_index("y")

    s_part = jnp.dot(student_hidden, student_proj, preferred_element_type=jnp.float32)
    t_part = jnp.dot(teacher_hidden, teacher_proj, preferred_element_type=jnp.float32)
    feats = tgrp_sum(jnp.concatenate([s_part, t_part], 1))
    units = jnp.concatenate(
        [unit_rows(feats[:, :proj_width]), unit_rows(feats[:, proj_width:])], 1
    )
    digits = jnp.stack([student_chars, teacher_chars])
    digits = jnp.stack([digits // 4096, digits // 64 % 64, digits % 64], 1)
    digit_rows = digits.reshape(-1, units.shape[1]).astype(jnp.bfloat16)
    flag_row = jnp.zeros((1, units.shape[1]), jnp.bfloat16).at[0, :2].set(band[0].astype(jnp.bfloat16))
    extra = jnp.concatenate([digit_rows, flag_row], 0)
    pad = -(rows + extra.shape[0]) % 16
    packed = jnp.concatenate([units, extra, jnp.zeros((pad, units.shape[1]), jnp.bfloat16)], 0)
    gathered = gather_halves(packed)

    left_rows = seq_shifted(teacher_hidden, 1)
    right_rows = seq_shifted(teacher_hidden, -1)

    s_unit = gathered[:, :rows, :proj_width]
    t_unit = gathered[:, :rows, proj_width:]
    got = gathered[:, rows : rows + digit_rows.shape[0]].astype(jnp.float32).reshape(blocks, 2, 3, rows)
    chars = got[:, :, 0] * 4096.0 + got[:, :, 1] * 64.0 + got[:, :, 2]
    s_pos = chars[:, 0]
    t_pos = beside(chars[:, 1])
    flags = gathered[:, rows + digit_rows.shape[0]].astype(jnp.float32)
    ones_col = jnp.ones((blocks,), jnp.float32)
    slot_mask = jnp.stack([flags[:, 0], ones_col, flags[:, 1]], 1)
    scores = jnp.einsum(
        "bkjp,bip->bkji", beside(t_unit), s_unit, preferred_element_type=jnp.float32
    ) / math.sqrt(proj_width)
    distance = jnp.abs(s_pos[:, None, None, :] - t_pos[:, :, :, None]) / (4.0 * rows)
    kernel = jnp.exp(scores - distance) * slot_mask[:, :, None, None]

    def iterate(iteration, scales):
        row_scale, col_scale = scales
        partial_cols = jnp.sum(row_scale[:, None, None, :] * kernel, axis=3)
        zero_row = jnp.zeros_like(partial_cols[:1, 0])
        column_total = (
            partial_cols[:, 1]
            + jnp.concatenate([zero_row, partial_cols[:-1, 2]], 0)
            + jnp.concatenate([partial_cols[1:, 0], zero_row], 0)
        )
        col_scale = beside(1.0 / column_total)
        row_scale = 1.0 / jnp.sum(kernel * col_scale[:, :, :, None], axis=(1, 2))
        return row_scale, col_scale

    row_scale, col_scale = lax.fori_loop(
        0,
        ITERS,
        iterate,
        (jnp.ones((blocks, rows), jnp.float32), jnp.zeros((blocks, 3, rows), jnp.float32)),
    )
    own_kernel = lax.dynamic_index_in_dim(kernel, me, 0, keepdims=False)
    own_row = lax.dynamic_index_in_dim(row_scale, me, 0, keepdims=False)
    own_col = lax.dynamic_index_in_dim(col_scale, me, 0, keepdims=False)
    plan = (own_row[None, None, :] * own_kernel * own_col[:, :, None]).astype(jnp.bfloat16)
    along_j = (((0,), (0,)), ((), ()))
    aligned = lax.dot_general(plan[1], teacher_hidden, along_j, preferred_element_type=jnp.float32)
    sides = jnp.concatenate([plan[0], plan[2]], 0)
    near_rows = jnp.concatenate([left_rows, right_rows], 0)
    aligned = aligned + lax.dot_general(sides, near_rows, along_j, preferred_element_type=jnp.float32)
    return aligned.astype(jnp.bfloat16)


def body_banded(
    student_hidden, teacher_hidden, student_proj, teacher_proj, student_chars, teacher_chars, band
):
    block_rows = student_hidden.shape[0]
    proj_width = student_proj.shape[1]
    s_part = jnp.dot(student_hidden, student_proj, preferred_element_type=jnp.float32)
    t_part = jnp.dot(teacher_hidden, teacher_proj, preferred_element_type=jnp.float32)
    s_feat, t_feat = lax.psum((s_part, t_part), "tgrp")
    s_unit = unit_rows(s_feat)
    t_unit = unit_rows(t_feat)
    left_rows, left_unit, left_chars = shifted((teacher_hidden, t_unit, teacher_chars), "seq", 1)
    right_rows, right_unit, right_chars = shifted(
        (teacher_hidden, t_unit, teacher_chars), "seq", -1
    )
    near_unit = jnp.stack([left_unit, t_unit, right_unit])
    near_pos = jnp.stack([left_chars, teacher_chars, right_chars]).astype(jnp.float32)
    s_pos = student_chars.astype(jnp.float32)
    flags = band[0]
    slot_mask = jnp.stack([flags[0], jnp.ones((), jnp.int32), flags[1]]).astype(jnp.float32)
    scores = jnp.einsum(
        "ip,kjp->kij", s_unit, near_unit, preferred_element_type=jnp.float32
    ) / math.sqrt(proj_width)
    distance = jnp.abs(s_pos[None, :, None] - near_pos[:, None, :]) / (4.0 * block_rows)
    kernel = jnp.exp(scores - distance) * slot_mask[:, None, None]
    row_scale = jnp.ones((block_rows,), jnp.float32)
    col_scale = jnp.zeros((3, block_rows), jnp.float32)
    for iteration in range(ITERS):
        partial_cols = jnp.sum(row_scale[None, :, None] * kernel, axis=1)
        left_one = shifted(partial_cols[1:], "seq", 1)
        left_two = shifted(partial_cols[2:], "seq", 2)
        right_one = shifted(partial_cols[:2], "seq", -1)
        right_two = shifted(partial_cols[:1], "seq", -2)
        column_total = jnp.stack(
            [
                left_two[0] + left_one[0] + partial_cols[0],
                left_one[1] + partial_cols[1] + right_one[0],
                partial_cols[2] + right_one[1] + right_two[0],
            ]
        )
        col_scale = slot_mask[:, None] / jnp.where(slot_mask[:, None] > 0.0, column_total, 1.0)
        row_scale = 1.0 / jnp.sum(kernel * col_scale[:, None, :], axis=(0, 2))
    plan = (row_scale[None, :, None] * kernel * col_scale[:, None, :]).astype(jnp.bfloat16)
    aligned = jnp.dot(plan[0], left_rows, preferred_element_type=jnp.float32)
    aligned = aligned + jnp.dot(plan[1], teacher_hidden, preferred_element_type=jnp.float32)
    aligned = aligned + jnp.dot(plan[2], right_rows, preferred_element_type=jnp.float32)
    return aligned.astype(jnp.bfloat16)


def specs(seq):
    return dict(
        in_specs=(
            P(("groups",) + seq, "tgrp"),
            P(("groups",) + seq, "tgrp"),
            P("tgrp", None),
            P("tgrp", None),
            P(("groups",) + seq),
            P(("groups",) + seq),
            P(("groups",) + seq, None),
        ),
        out_specs=P(("groups",) + seq, "tgrp"),
    )


def solution(mesh):
    blocks = mesh.shape["seq"]
    sizes = dict(mesh.shape)

    def fits(rows):
        return blocks * 3 * rows * rows * 4 <= LOCAL_KERNEL_BYTES

    local = blocks % 2 == 0 and sizes["tgrp"] == 2
    if local:
        view = jax.sharding.Mesh(
            mesh.devices.reshape(sizes["groups"], blocks // 2, 2, sizes["tgrp"]),
            ("groups", "z", "y", "tgrp"),
        )
        local_fn = jax.shard_map(body_local, mesh=view, check_vma=False, **specs(SEQ))
    banded_fn = jax.shard_map(body_banded, mesh=mesh, check_vma=False, **specs(("seq",)))

    def run(*args):
        rows = args[0].shape[0] // (sizes["groups"] * blocks)
        if local and fits(rows):
            return local_fn(*args)
        return banded_fn(*args)

    return run
```

```python
import math

import jax
import jax.numpy as jnp
from jax import lax
from jax.sharding import PartitionSpec as P

ITERS = 4

LOCAL_KERNEL_BYTES = 24 * 2**20

norm_eps = 1e-05


def shifted(block, axis, distance):
    devices = range(lax.axis_size(axis))
    route = [(i - distance, i) for i in devices if i - distance in devices]
    return lax.ppermute(block, axis, route)


def unit_rows(features):
    factor = lax.rsqrt(jnp.mean(features * features, axis=-1, keepdims=True) + norm_eps)
    return (features * factor).astype(jnp.bfloat16)


def beside(values):
    zero_row = jnp.zeros_like(values[:1])
    from_left = jnp.concatenate([zero_row, values[:-1]], 0)
    from_right = jnp.concatenate([values[1:], zero_row], 0)
    return jnp.stack([from_left, values, from_right], 1)


def tgrp_sum(value):
    if lax.axis_size("tgrp") == 2:
        return value + lax.ppermute(value, "tgrp", [(0, 1), (1, 0)])
    return lax.psum(value, "tgrp")


def gather_seq(block):
    n = lax.axis_size("seq")
    if n % 2:
        return lax.all_gather(block, "seq")
    me = lax.axis_index("seq")
    pairs = n // 2
    partner = lax.ppermute(block, "seq", [(i, i ^ 1) for i in range(n)])
    odd = me % 2 == 1
    pair = jnp.stack([jnp.where(odd, partner, block), jnp.where(odd, block, partner)])
    by_offset = [pair]
    for d in range(1, pairs):
        by_offset = [shifted(pair, "seq", 2 * d)] + by_offset + [shifted(pair, "seq", -2 * d)]
    window = lax.dynamic_slice_in_dim(jnp.stack(by_offset), pairs - 1 - me // 2, pairs, 0)
    return window.reshape((n,) + block.shape)


def gather_halves(packed):
    if lax.axis_size("tgrp") != 2:
        return lax.all_gather(packed, "seq")
    half = packed.shape[1] // 2
    core = lax.axis_index("tgrp")
    mine = lax.dynamic_slice_in_dim(packed, core * half, half, 1)
    n = lax.axis_size("seq")
    got = lax.all_to_all(jnp.broadcast_to(mine, (n,) + mine.shape), "seq", 0, 0, tiled=False)
    theirs = lax.ppermute(got, "tgrp", [(0, 1), (1, 0)])
    first = jnp.where(core == 0, got, theirs)
    second = jnp.where(core == 0, theirs, got)
    return jnp.concatenate([first, second], 2)


def body_local(
    student_hidden, teacher_hidden, student_proj, teacher_proj, student_chars, teacher_chars, band
):
    rows = student_hidden.shape[0]
    proj_width = student_proj.shape[1]
    blocks = lax.axis_size("seq")
    me = lax.axis_index("seq")

    s_part = jnp.dot(student_hidden, student_proj, preferred_element_type=jnp.float32)
    t_part = jnp.dot(teacher_hidden, teacher_proj, preferred_element_type=jnp.float32)
    feats = tgrp_sum(jnp.concatenate([s_part, t_part], 1))
    units = jnp.concatenate(
        [unit_rows(feats[:, :proj_width]), unit_rows(feats[:, proj_width:])], 1
    )
    digits = jnp.stack([student_chars, teacher_chars])
    digits = jnp.stack([digits // 4096, digits // 64 % 64, digits % 64], 1)
    digit_rows = digits.reshape(-1, units.shape[1]).astype(jnp.bfloat16)
    flag_row = jnp.concatenate(
        [band[0].astype(jnp.bfloat16), jnp.zeros((units.shape[1] - 2,), jnp.bfloat16)]
    )[None]
    extra = jnp.concatenate([digit_rows, flag_row], 0)
    pad = -(rows + extra.shape[0]) % 16
    packed = jnp.concatenate([units, extra, jnp.zeros((pad, units.shape[1]), jnp.bfloat16)], 0)
    gathered = gather_halves(packed)

    left_rows = shifted(teacher_hidden, "seq", 1)
    right_rows = shifted(teacher_hidden, "seq", -1)

    s_unit = gathered[:, :rows, :proj_width]
    t_unit = gathered[:, :rows, proj_width:]
    got = gathered[:, rows : rows + digit_rows.shape[0]].astype(jnp.float32).reshape(blocks, 2, 3, rows)
    chars = got[:, :, 0] * 4096.0 + got[:, :, 1] * 64.0 + got[:, :, 2]
    s_pos = chars[:, 0]
    t_pos = beside(chars[:, 1])
    flags = gathered[:, rows + digit_rows.shape[0]].astype(jnp.float32)
    ones_col = jnp.ones((blocks,), jnp.float32)
    slot_mask = jnp.stack([flags[:, 0], ones_col, flags[:, 1]], 1)
    scores = jnp.einsum(
        "bkjp,bip->bkji", beside(t_unit), s_unit, preferred_element_type=jnp.float32
    ) / math.sqrt(proj_width)
    distance = jnp.abs(s_pos[:, None, None, :] - t_pos[:, :, :, None]) / (4.0 * rows)
    kernel = jnp.exp(scores - distance) * slot_mask[:, :, None, None]

    def iterate(iteration, scales):
        row_scale, col_scale = scales
        partial_cols = jnp.sum(row_scale[:, None, None, :] * kernel, axis=3)
        zero_row = jnp.zeros_like(partial_cols[:1, 0])
        column_total = (
            partial_cols[:, 1]
            + jnp.concatenate([zero_row, partial_cols[:-1, 2]], 0)
            + jnp.concatenate([partial_cols[1:, 0], zero_row], 0)
        )
        col_scale = beside(1.0 / column_total)
        row_scale = 1.0 / jnp.sum(kernel * col_scale[:, :, :, None], axis=(1, 2))
        return row_scale, col_scale

    row_scale, col_scale = lax.fori_loop(
        0,
        ITERS,
        iterate,
        (jnp.ones((blocks, rows), jnp.float32), jnp.zeros((blocks, 3, rows), jnp.float32)),
    )
    own_kernel = lax.dynamic_index_in_dim(kernel, me, 0, keepdims=False)
    own_row = lax.dynamic_index_in_dim(row_scale, me, 0, keepdims=False)
    own_col = lax.dynamic_index_in_dim(col_scale, me, 0, keepdims=False)
    plan = (own_row[None, None, :] * own_kernel * own_col[:, :, None]).astype(jnp.bfloat16)
    along_j = (((0,), (0,)), ((), ()))
    aligned = lax.dot_general(plan[1], teacher_hidden, along_j, preferred_element_type=jnp.float32)
    sides = jnp.concatenate([plan[0], plan[2]], 0)
    near_rows = jnp.concatenate([left_rows, right_rows], 0)
    aligned = aligned + lax.dot_general(sides, near_rows, along_j, preferred_element_type=jnp.float32)
    return aligned.astype(jnp.bfloat16)


def body_banded(
    student_hidden, teacher_hidden, student_proj, teacher_proj, student_chars, teacher_chars, band
):
    block_rows = student_hidden.shape[0]
    proj_width = student_proj.shape[1]
    s_part = jnp.dot(student_hidden, student_proj, preferred_element_type=jnp.float32)
    t_part = jnp.dot(teacher_hidden, teacher_proj, preferred_element_type=jnp.float32)
    s_feat, t_feat = lax.psum((s_part, t_part), "tgrp")
    s_unit = unit_rows(s_feat)
    t_unit = unit_rows(t_feat)
    left_rows, left_unit, left_chars = shifted((teacher_hidden, t_unit, teacher_chars), "seq", 1)
    right_rows, right_unit, right_chars = shifted(
        (teacher_hidden, t_unit, teacher_chars), "seq", -1
    )
    near_unit = jnp.stack([left_unit, t_unit, right_unit])
    near_pos = jnp.stack([left_chars, teacher_chars, right_chars]).astype(jnp.float32)
    s_pos = student_chars.astype(jnp.float32)
    flags = band[0]
    slot_mask = jnp.stack([flags[0], jnp.ones((), jnp.int32), flags[1]]).astype(jnp.float32)
    scores = jnp.einsum(
        "ip,kjp->kij", s_unit, near_unit, preferred_element_type=jnp.float32
    ) / math.sqrt(proj_width)
    distance = jnp.abs(s_pos[None, :, None] - near_pos[:, None, :]) / (4.0 * block_rows)
    kernel = jnp.exp(scores - distance) * slot_mask[:, None, None]
    row_scale = jnp.ones((block_rows,), jnp.float32)
    col_scale = jnp.zeros((3, block_rows), jnp.float32)
    for iteration in range(ITERS):
        partial_cols = jnp.sum(row_scale[None, :, None] * kernel, axis=1)
        left_one = shifted(partial_cols[1:], "seq", 1)
        left_two = shifted(partial_cols[2:], "seq", 2)
        right_one = shifted(partial_cols[:2], "seq", -1)
        right_two = shifted(partial_cols[:1], "seq", -2)
        column_total = jnp.stack(
            [
                left_two[0] + left_one[0] + partial_cols[0],
                left_one[1] + partial_cols[1] + right_one[0],
                partial_cols[2] + right_one[1] + right_two[0],
            ]
        )
        col_scale = slot_mask[:, None] / jnp.where(slot_mask[:, None] > 0.0, column_total, 1.0)
        row_scale = 1.0 / jnp.sum(kernel * col_scale[:, None, :], axis=(0, 2))
    plan = (row_scale[None, :, None] * kernel * col_scale[:, None, :]).astype(jnp.bfloat16)
    aligned = jnp.dot(plan[0], left_rows, preferred_element_type=jnp.float32)
    aligned = aligned + jnp.dot(plan[1], teacher_hidden, preferred_element_type=jnp.float32)
    aligned = aligned + jnp.dot(plan[2], right_rows, preferred_element_type=jnp.float32)
    return aligned.astype(jnp.bfloat16)


def solution(mesh):
    blocks = mesh.shape["seq"]

    def body(*args):
        rows = args[0].shape[0]
        if blocks * 3 * rows * rows * 4 <= LOCAL_KERNEL_BYTES:
            return body_local(*args)
        return body_banded(*args)

    return jax.shard_map(
        body,
        mesh=mesh,
        in_specs=(
            P(("groups", "seq"), "tgrp"),
            P(("groups", "seq"), "tgrp"),
            P("tgrp", None),
            P("tgrp", None),
            P(("groups", "seq")),
            P(("groups", "seq")),
            P(("groups", "seq"), None),
        ),
        out_specs=P(("groups", "seq"), "tgrp"),
        check_vma=False,
    )
```

```python
import math

import jax
import jax.numpy as jnp
from jax import lax
from jax.sharding import PartitionSpec as P

ITERS = 4

LOCAL_KERNEL_BYTES = 24 * 2**20

norm_eps = 1e-05


def shifted(block, axis, distance):
    devices = range(lax.axis_size(axis))
    route = [(i - distance, i) for i in devices if i - distance in devices]
    return lax.ppermute(block, axis, route)


def unit_rows(features):
    factor = lax.rsqrt(jnp.mean(features * features, axis=-1, keepdims=True) + norm_eps)
    return (features * factor).astype(jnp.bfloat16)


def beside(values):
    zero_row = jnp.zeros_like(values[:1])
    from_left = jnp.concatenate([zero_row, values[:-1]], 0)
    from_right = jnp.concatenate([values[1:], zero_row], 0)
    return jnp.stack([from_left, values, from_right], 1)


def tgrp_sum(value):
    if lax.axis_size("tgrp") == 2:
        return value + lax.ppermute(value, "tgrp", [(0, 1), (1, 0)])
    return lax.psum(value, "tgrp")


def gather_seq(block):
    n = lax.axis_size("seq")
    if n % 2:
        return lax.all_gather(block, "seq")
    me = lax.axis_index("seq")
    pairs = n // 2
    partner = lax.ppermute(block, "seq", [(i, i ^ 1) for i in range(n)])
    odd = me % 2 == 1
    pair = jnp.stack([jnp.where(odd, partner, block), jnp.where(odd, block, partner)])
    by_offset = [pair]
    for d in range(1, pairs):
        by_offset = [shifted(pair, "seq", 2 * d)] + by_offset + [shifted(pair, "seq", -2 * d)]
    window = lax.dynamic_slice_in_dim(jnp.stack(by_offset), pairs - 1 - me // 2, pairs, 0)
    return window.reshape((n,) + block.shape)


def gather_halves(packed):
    if lax.axis_size("tgrp") != 2:
        return lax.all_gather(packed, "seq")
    half = packed.shape[1] // 2
    core = lax.axis_index("tgrp")
    mine = lax.dynamic_slice_in_dim(packed, core * half, half, 1)
    n = lax.axis_size("seq")
    got = lax.all_to_all(jnp.broadcast_to(mine, (n,) + mine.shape), "seq", 0, 0, tiled=False)
    theirs = lax.ppermute(got, "tgrp", [(0, 1), (1, 0)])
    first = jnp.where(core == 0, got, theirs)
    second = jnp.where(core == 0, theirs, got)
    return jnp.concatenate([first, second], 2)


def body_local(
    student_hidden, teacher_hidden, student_proj, teacher_proj, student_chars, teacher_chars, band
):
    rows = student_hidden.shape[0]
    proj_width = student_proj.shape[1]
    blocks = lax.axis_size("seq")
    me = lax.axis_index("seq")

    s_part = jnp.dot(student_hidden, student_proj, preferred_element_type=jnp.float32)
    t_part = jnp.dot(teacher_hidden, teacher_proj, preferred_element_type=jnp.float32)
    first_core = lax.axis_index("tgrp") == 0
    own_part = jnp.where(first_core, s_part, t_part)
    their_part = jnp.where(first_core, t_part, s_part)
    own_units = unit_rows(own_part + lax.ppermute(their_part, "tgrp", [(0, 1), (1, 0)]))
    units = jnp.concatenate([own_units, own_units], 1)
    digits = jnp.stack([student_chars, teacher_chars])
    digits = jnp.stack([digits // 4096, digits // 64 % 64, digits % 64], 1)
    digit_rows = digits.reshape(-1, units.shape[1]).astype(jnp.bfloat16)
    flag_row = jnp.concatenate(
        [band[0].astype(jnp.bfloat16), jnp.zeros((units.shape[1] - 2,), jnp.bfloat16)]
    )[None]
    extra = jnp.concatenate([digit_rows, flag_row], 0)
    pad = -(rows + extra.shape[0]) % 16
    packed = jnp.concatenate([units, extra, jnp.zeros((pad, units.shape[1]), jnp.bfloat16)], 0)
    gathered = gather_halves(packed)

    left_rows = shifted(teacher_hidden, "seq", 1)
    right_rows = shifted(teacher_hidden, "seq", -1)

    s_unit = gathered[:, :rows, :proj_width]
    t_unit = gathered[:, :rows, proj_width:]
    got = gathered[:, rows : rows + digit_rows.shape[0]].astype(jnp.float32).reshape(blocks, 2, 3, rows)
    chars = got[:, :, 0] * 4096.0 + got[:, :, 1] * 64.0 + got[:, :, 2]
    s_pos = chars[:, 0]
    t_pos = beside(chars[:, 1])
    flags = gathered[:, rows + digit_rows.shape[0]].astype(jnp.float32)
    ones_col = jnp.ones((blocks,), jnp.float32)
    slot_mask = jnp.stack([flags[:, 0], ones_col, flags[:, 1]], 1)
    scores = jnp.einsum(
        "bkjp,bip->bkji", beside(t_unit), s_unit, preferred_element_type=jnp.float32
    ) / math.sqrt(proj_width)
    distance = jnp.abs(s_pos[:, None, None, :] - t_pos[:, :, :, None]) / (4.0 * rows)
    kernel = jnp.exp(scores - distance) * slot_mask[:, :, None, None]

    def iterate(iteration, scales):
        row_scale, col_scale = scales
        partial_cols = jnp.sum(row_scale[:, None, None, :] * kernel, axis=3)
        zero_row = jnp.zeros_like(partial_cols[:1, 0])
        column_total = (
            partial_cols[:, 1]
            + jnp.concatenate([zero_row, partial_cols[:-1, 2]], 0)
            + jnp.concatenate([partial_cols[1:, 0], zero_row], 0)
        )
        col_scale = beside(1.0 / column_total)
        row_scale = 1.0 / jnp.sum(kernel * col_scale[:, :, :, None], axis=(1, 2))
        return row_scale, col_scale

    row_scale, col_scale = lax.fori_loop(
        0,
        ITERS,
        iterate,
        (jnp.ones((blocks, rows), jnp.float32), jnp.zeros((blocks, 3, rows), jnp.float32)),
    )
    own_kernel = lax.dynamic_index_in_dim(kernel, me, 0, keepdims=False)
    own_row = lax.dynamic_index_in_dim(row_scale, me, 0, keepdims=False)
    own_col = lax.dynamic_index_in_dim(col_scale, me, 0, keepdims=False)
    plan = (own_row[None, None, :] * own_kernel * own_col[:, :, None]).astype(jnp.bfloat16)
    along_j = (((0,), (0,)), ((), ()))
    aligned = lax.dot_general(plan[1], teacher_hidden, along_j, preferred_element_type=jnp.float32)
    sides = jnp.concatenate([plan[0], plan[2]], 0)
    near_rows = jnp.concatenate([left_rows, right_rows], 0)
    aligned = aligned + lax.dot_general(sides, near_rows, along_j, preferred_element_type=jnp.float32)
    return aligned.astype(jnp.bfloat16)


def body_banded(
    student_hidden, teacher_hidden, student_proj, teacher_proj, student_chars, teacher_chars, band
):
    block_rows = student_hidden.shape[0]
    proj_width = student_proj.shape[1]
    s_part = jnp.dot(student_hidden, student_proj, preferred_element_type=jnp.float32)
    t_part = jnp.dot(teacher_hidden, teacher_proj, preferred_element_type=jnp.float32)
    s_feat, t_feat = lax.psum((s_part, t_part), "tgrp")
    s_unit = unit_rows(s_feat)
    t_unit = unit_rows(t_feat)
    left_rows, left_unit, left_chars = shifted((teacher_hidden, t_unit, teacher_chars), "seq", 1)
    right_rows, right_unit, right_chars = shifted(
        (teacher_hidden, t_unit, teacher_chars), "seq", -1
    )
    near_unit = jnp.stack([left_unit, t_unit, right_unit])
    near_pos = jnp.stack([left_chars, teacher_chars, right_chars]).astype(jnp.float32)
    s_pos = student_chars.astype(jnp.float32)
    flags = band[0]
    slot_mask = jnp.stack([flags[0], jnp.ones((), jnp.int32), flags[1]]).astype(jnp.float32)
    scores = jnp.einsum(
        "ip,kjp->kij", s_unit, near_unit, preferred_element_type=jnp.float32
    ) / math.sqrt(proj_width)
    distance = jnp.abs(s_pos[None, :, None] - near_pos[:, None, :]) / (4.0 * block_rows)
    kernel = jnp.exp(scores - distance) * slot_mask[:, None, None]
    row_scale = jnp.ones((block_rows,), jnp.float32)
    col_scale = jnp.zeros((3, block_rows), jnp.float32)
    for iteration in range(ITERS):
        partial_cols = jnp.sum(row_scale[None, :, None] * kernel, axis=1)
        left_one = shifted(partial_cols[1:], "seq", 1)
        left_two = shifted(partial_cols[2:], "seq", 2)
        right_one = shifted(partial_cols[:2], "seq", -1)
        right_two = shifted(partial_cols[:1], "seq", -2)
        column_total = jnp.stack(
            [
                left_two[0] + left_one[0] + partial_cols[0],
                left_one[1] + partial_cols[1] + right_one[0],
                partial_cols[2] + right_one[1] + right_two[0],
            ]
        )
        col_scale = slot_mask[:, None] / jnp.where(slot_mask[:, None] > 0.0, column_total, 1.0)
        row_scale = 1.0 / jnp.sum(kernel * col_scale[:, None, :], axis=(0, 2))
    plan = (row_scale[None, :, None] * kernel * col_scale[:, None, :]).astype(jnp.bfloat16)
    aligned = jnp.dot(plan[0], left_rows, preferred_element_type=jnp.float32)
    aligned = aligned + jnp.dot(plan[1], teacher_hidden, preferred_element_type=jnp.float32)
    aligned = aligned + jnp.dot(plan[2], right_rows, preferred_element_type=jnp.float32)
    return aligned.astype(jnp.bfloat16)


def solution(mesh):
    blocks = mesh.shape["seq"]

    def body(*args):
        rows = args[0].shape[0]
        if blocks * 3 * rows * rows * 4 <= LOCAL_KERNEL_BYTES:
            return body_local(*args)
        return body_banded(*args)

    return jax.shard_map(
        body,
        mesh=mesh,
        in_specs=(
            P(("groups", "seq"), "tgrp"),
            P(("groups", "seq"), "tgrp"),
            P("tgrp", None),
            P("tgrp", None),
            P(("groups", "seq")),
            P(("groups", "seq")),
            P(("groups", "seq"), None),
        ),
        out_specs=P(("groups", "seq"), "tgrp"),
        check_vma=False,
    )
```

```python
import math

import jax
import jax.numpy as jnp
from jax import lax
from jax.sharding import PartitionSpec as P

ITERS = 4

LOCAL_KERNEL_BYTES = 24 * 2**20

norm_eps = 1e-05


def shifted(block, axis, distance):
    devices = range(lax.axis_size(axis))
    route = [(i - distance, i) for i in devices if i - distance in devices]
    return lax.ppermute(block, axis, route)


def unit_rows(features):
    factor = lax.rsqrt(jnp.mean(features * features, axis=-1, keepdims=True) + norm_eps)
    return (features * factor).astype(jnp.bfloat16)


def beside(values):
    zero_row = jnp.zeros_like(values[:1])
    from_left = jnp.concatenate([zero_row, values[:-1]], 0)
    from_right = jnp.concatenate([values[1:], zero_row], 0)
    return jnp.stack([from_left, values, from_right], 1)


def tgrp_sum(value):
    if lax.axis_size("tgrp") == 2:
        return value + lax.ppermute(value, "tgrp", [(0, 1), (1, 0)])
    return lax.psum(value, "tgrp")


def gather_seq(block):
    n = lax.axis_size("seq")
    if n % 2:
        return lax.all_gather(block, "seq")
    me = lax.axis_index("seq")
    pairs = n // 2
    partner = lax.ppermute(block, "seq", [(i, i ^ 1) for i in range(n)])
    odd = me % 2 == 1
    pair = jnp.stack([jnp.where(odd, partner, block), jnp.where(odd, block, partner)])
    by_offset = [pair]
    for d in range(1, pairs):
        by_offset = [shifted(pair, "seq", 2 * d)] + by_offset + [shifted(pair, "seq", -2 * d)]
    window = lax.dynamic_slice_in_dim(jnp.stack(by_offset), pairs - 1 - me // 2, pairs, 0)
    return window.reshape((n,) + block.shape)


def gather_halves(packed):
    if lax.axis_size("tgrp") != 2:
        return lax.all_gather(packed, "seq")
    half = packed.shape[1] // 2
    core = lax.axis_index("tgrp")
    mine = lax.dynamic_slice_in_dim(packed, core * half, half, 1)
    n = lax.axis_size("seq")
    got = lax.all_to_all(jnp.broadcast_to(mine, (n,) + mine.shape), "seq", 0, 0, tiled=False)
    theirs = lax.ppermute(got, "tgrp", [(0, 1), (1, 0)])
    first = jnp.where(core == 0, got, theirs)
    second = jnp.where(core == 0, theirs, got)
    return jnp.concatenate([first, second], 2)


def body_local(
    student_hidden, teacher_hidden, student_proj, teacher_proj, student_chars, teacher_chars, band
):
    rows = student_hidden.shape[0]
    proj_width = student_proj.shape[1]
    blocks = lax.axis_size("seq")
    me = lax.axis_index("seq")

    t_part = jnp.dot(teacher_hidden, teacher_proj, preferred_element_type=jnp.float32)
    student_rows, t_part = lax.optimization_barrier((student_hidden, t_part))
    s_part = jnp.dot(student_rows, student_proj, preferred_element_type=jnp.float32)
    first_core = lax.axis_index("tgrp") == 0
    own_part = jnp.where(first_core, s_part, t_part)
    their_part = jnp.where(first_core, t_part, s_part)
    own_units = unit_rows(own_part + lax.ppermute(their_part, "tgrp", [(0, 1), (1, 0)]))
    units = jnp.concatenate([own_units, own_units], 1)
    digits = jnp.stack([student_chars, teacher_chars])
    digits = jnp.stack([digits // 4096, digits // 64 % 64, digits % 64], 1)
    digit_rows = digits.reshape(-1, units.shape[1]).astype(jnp.bfloat16)
    flag_row = jnp.concatenate(
        [band[0].astype(jnp.bfloat16), jnp.zeros((units.shape[1] - 2,), jnp.bfloat16)]
    )[None]
    extra = jnp.concatenate([digit_rows, flag_row], 0)
    pad = -(rows + extra.shape[0]) % 16
    packed = jnp.concatenate([units, extra, jnp.zeros((pad, units.shape[1]), jnp.bfloat16)], 0)
    gathered = gather_halves(packed)

    left_rows = shifted(teacher_hidden, "seq", 1)
    right_rows = shifted(teacher_hidden, "seq", -1)

    s_unit = gathered[:, :rows, :proj_width]
    t_unit = gathered[:, :rows, proj_width:]
    got = gathered[:, rows : rows + digit_rows.shape[0]].astype(jnp.float32).reshape(blocks, 2, 3, rows)
    chars = got[:, :, 0] * 4096.0 + got[:, :, 1] * 64.0 + got[:, :, 2]
    s_pos = chars[:, 0]
    t_pos = beside(chars[:, 1])
    flags = gathered[:, rows + digit_rows.shape[0]].astype(jnp.float32)
    ones_col = jnp.ones((blocks,), jnp.float32)
    slot_mask = jnp.stack([flags[:, 0], ones_col, flags[:, 1]], 1)
    scores = jnp.einsum(
        "bkjp,bip->bkji", beside(t_unit), s_unit, preferred_element_type=jnp.float32
    ) / math.sqrt(proj_width)
    distance = jnp.abs(s_pos[:, None, None, :] - t_pos[:, :, :, None]) / (4.0 * rows)
    kernel = jnp.exp(scores - distance) * slot_mask[:, :, None, None]

    def iterate(iteration, scales):
        row_scale, col_scale = scales
        partial_cols = jnp.sum(row_scale[:, None, None, :] * kernel, axis=3)
        zero_row = jnp.zeros_like(partial_cols[:1, 0])
        column_total = (
            partial_cols[:, 1]
            + jnp.concatenate([zero_row, partial_cols[:-1, 2]], 0)
            + jnp.concatenate([partial_cols[1:, 0], zero_row], 0)
        )
        col_scale = beside(1.0 / column_total)
        row_scale = 1.0 / jnp.sum(kernel * col_scale[:, :, :, None], axis=(1, 2))
        return row_scale, col_scale

    row_scale, col_scale = lax.fori_loop(
        0,
        ITERS,
        iterate,
        (jnp.ones((blocks, rows), jnp.float32), jnp.zeros((blocks, 3, rows), jnp.float32)),
    )
    own_kernel = lax.dynamic_index_in_dim(kernel, me, 0, keepdims=False)
    own_row = lax.dynamic_index_in_dim(row_scale, me, 0, keepdims=False)
    own_col = lax.dynamic_index_in_dim(col_scale, me, 0, keepdims=False)
    plan = (own_row[None, None, :] * own_kernel * own_col[:, :, None]).astype(jnp.bfloat16)
    along_j = (((0,), (0,)), ((), ()))
    aligned = lax.dot_general(plan[1], teacher_hidden, along_j, preferred_element_type=jnp.float32)
    sides = jnp.concatenate([plan[0], plan[2]], 0)
    near_rows = jnp.concatenate([left_rows, right_rows], 0)
    aligned = aligned + lax.dot_general(sides, near_rows, along_j, preferred_element_type=jnp.float32)
    return aligned.astype(jnp.bfloat16)


def body_banded(
    student_hidden, teacher_hidden, student_proj, teacher_proj, student_chars, teacher_chars, band
):
    block_rows = student_hidden.shape[0]
    proj_width = student_proj.shape[1]
    s_part = jnp.dot(student_hidden, student_proj, preferred_element_type=jnp.float32)
    t_part = jnp.dot(teacher_hidden, teacher_proj, preferred_element_type=jnp.float32)
    s_feat, t_feat = lax.psum((s_part, t_part), "tgrp")
    s_unit = unit_rows(s_feat)
    t_unit = unit_rows(t_feat)
    left_rows, left_unit, left_chars = shifted((teacher_hidden, t_unit, teacher_chars), "seq", 1)
    right_rows, right_unit, right_chars = shifted(
        (teacher_hidden, t_unit, teacher_chars), "seq", -1
    )
    near_unit = jnp.stack([left_unit, t_unit, right_unit])
    near_pos = jnp.stack([left_chars, teacher_chars, right_chars]).astype(jnp.float32)
    s_pos = student_chars.astype(jnp.float32)
    flags = band[0]
    slot_mask = jnp.stack([flags[0], jnp.ones((), jnp.int32), flags[1]]).astype(jnp.float32)
    scores = jnp.einsum(
        "ip,kjp->kij", s_unit, near_unit, preferred_element_type=jnp.float32
    ) / math.sqrt(proj_width)
    distance = jnp.abs(s_pos[None, :, None] - near_pos[:, None, :]) / (4.0 * block_rows)
    kernel = jnp.exp(scores - distance) * slot_mask[:, None, None]
    row_scale = jnp.ones((block_rows,), jnp.float32)
    col_scale = jnp.zeros((3, block_rows), jnp.float32)
    for iteration in range(ITERS):
        partial_cols = jnp.sum(row_scale[None, :, None] * kernel, axis=1)
        left_one = shifted(partial_cols[1:], "seq", 1)
        left_two = shifted(partial_cols[2:], "seq", 2)
        right_one = shifted(partial_cols[:2], "seq", -1)
        right_two = shifted(partial_cols[:1], "seq", -2)
        column_total = jnp.stack(
            [
                left_two[0] + left_one[0] + partial_cols[0],
                left_one[1] + partial_cols[1] + right_one[0],
                partial_cols[2] + right_one[1] + right_two[0],
            ]
        )
        col_scale = slot_mask[:, None] / jnp.where(slot_mask[:, None] > 0.0, column_total, 1.0)
        row_scale = 1.0 / jnp.sum(kernel * col_scale[:, None, :], axis=(0, 2))
    plan = (row_scale[None, :, None] * kernel * col_scale[:, None, :]).astype(jnp.bfloat16)
    aligned = jnp.dot(plan[0], left_rows, preferred_element_type=jnp.float32)
    aligned = aligned + jnp.dot(plan[1], teacher_hidden, preferred_element_type=jnp.float32)
    aligned = aligned + jnp.dot(plan[2], right_rows, preferred_element_type=jnp.float32)
    return aligned.astype(jnp.bfloat16)


def solution(mesh):
    blocks = mesh.shape["seq"]

    def body(*args):
        rows = args[0].shape[0]
        if blocks * 3 * rows * rows * 4 <= LOCAL_KERNEL_BYTES:
            return body_local(*args)
        return body_banded(*args)

    return jax.shard_map(
        body,
        mesh=mesh,
        in_specs=(
            P(("groups", "seq"), "tgrp"),
            P(("groups", "seq"), "tgrp"),
            P("tgrp", None),
            P("tgrp", None),
            P(("groups", "seq")),
            P(("groups", "seq")),
            P(("groups", "seq"), None),
        ),
        out_specs=P(("groups", "seq"), "tgrp"),
        check_vma=False,
    )
```
